32 devices in a mesh: tm: 4 (over x, core), space: 8 (over z, y).
Axes of the slice: x: 2, y: 2, z: 4, core: 2. Of those that a mesh axis runs over, the one named last changes fastest.
Arguments:
- u_start: float32 [12, 64, 16, 128], P(None, 'space'), may hold values from -6 to 6
- guess: float32 [4, 3, 12, 64, 16, 128], P('tm', None, None, 'space'), may hold values from -6 to 6
- velocity: float32 [3, 12], replicated, may hold values from -1 to 1
- rates: float32 [21], replicated, may hold values from 0.5 to 5
- energies: float32 [21], replicated, may hold values from 0.5 to 4
- reactions: int32 [21, 3], replicated, may hold values from 0 to 11
Outputs:
- fine_end: float32 [4, 12, 64, 16, 128], P('tm', None, 'space')
- coarse_end: float32 [4, 12, 64, 8, 128], P('tm', None, 'space')
The draws below stay inside these ranges and needn't reach their ends.
All inputs are finite; a program needn't handle non-finite values.
Results may differ from the reference program's by a relative error of at most 0.0001.
Values sent between devices are 32-bit elements; how exact they have to be, the bound alone decides.
No kernel may reach another device: no remote copies, remote signals or barrier semaphores. Data moves between devices by JAX's collectives and lax.ppermute only.
A program may use at most 64 MiB of HBM per device.

```python
import math
import jax
import jax.numpy as jnp
import numpy as np
from jax import lax

FIELDS = 12
REACTIONS = 21
ITERS = 2
NX = 128
NY = 16
SECTIONS = 4
NZ = 64


def with_ends(result, own_key, smallest, largest):
    shape = result.shape
    place = [jax.random.randint(jax.random.fold_in(own_key, axis), (), 0, shape[axis]) for axis in range(len(shape))]
    result = result.at[tuple(place)].set(smallest)
    longest = shape.index(max(shape))
    place[longest] = (place[longest] + 1) % shape[longest]
    return result.at[tuple(place)].set(largest)


def level_of(rng, shape, cuts, low, top_value):
    gain, own = 1.0, jax.random.fold_in(rng, 6)
    for dim, shards_of in cuts:
        heights = jnp.exp(jax.random.uniform(jax.random.fold_in(own, dim), (shards_of,), jnp.float32, low / len(cuts), top_value / len(cuts)))
        gain = gain * jnp.repeat(heights, shape[dim] // shards_of).reshape([-1 if axis == dim else 1 for axis in range(len(shape))])
    return gain


def scatter_about(stream_key, dims, spread, bound, pieces=(), kind=jnp.bfloat16):
    result = spread * jax.random.normal(stream_key, dims, jnp.float32)
    if pieces:
        result = result * level_of(stream_key, dims, pieces, -0.22, 0.18)
    return jnp.clip(result, -bound, bound).astype(kind)


def setup_inputs(seed: int = 0) -> dict:
    splits = jax.random.split(jax.random.key(seed), 7)
    return {
        "u_start": scatter_about(splits[0], (FIELDS, NZ, NY, NX), 1.0, 6.0, ((1, 8),), jnp.float32),
        "guess": scatter_about(splits[1], (SECTIONS, 3, FIELDS, NZ, NY, NX), 1.0, 6.0, ((0, 4), (3, 8)), jnp.float32),
        "velocity": jnp.clip(jax.random.uniform(splits[2], (3, FIELDS), jnp.float32, -1.0, 1.0), -1.0, 1.0),
        "rates": jnp.clip(jnp.exp(jax.random.uniform(splits[3], (REACTIONS,), jnp.float32, math.log(0.5), math.log(5.0))), 0.5, 5.0),
        "energies": jnp.clip(jnp.exp(jax.random.uniform(splits[4], (REACTIONS,), jnp.float32, math.log(0.5), math.log(4.0))), 0.5, 4.0),
        "reactions": with_ends(jax.random.randint(splits[5], (REACTIONS, 3), 0, FIELDS), jax.random.fold_in(splits[5], 1), 0, FIELDS - 1).astype(jnp.int32),
    }


STEP = 0.01
FINE_NODES = np.array([-1.0, -0.8717401485096066, -0.5917001814331423, -0.2092992179024789, 0.2092992179024789, 0.5917001814331423, 0.8717401485096066, 1.0])
COARSE_NODES = np.array([-1.0, -0.4472135954999579, 0.4472135954999579, 1.0])


def lagrange_table(source, target):
    table = np.ones((len(target), len(source)))
    for j in range(len(source)):
        for m in range(len(source)):
            if m != j:
                table[:, j] *= (target - source[m]) / (source[j] - source[m])
    return table


def derivative_table(points):
    total = len(points)
    weights = np.array([1.0 / np.prod([points[j] - points[m] for m in range(total) if m != j]) for j in range(total)])
    table = np.zeros((total, total))
    for i in range(total):
        for j in range(total):
            if i != j:
                table[i, j] = weights[j] / weights[i] / (points[i] - points[j])
        table[i, i] = -np.sum(table[i])
    return table


def element_map(field, axis, table):
    moved = jnp.moveaxis(field, axis, -1)
    per_input = table.shape[1]
    shaped = moved.reshape(moved.shape[:-1] + (moved.shape[-1] // per_input, per_input))
    matrix = jnp.asarray(table).astype(field.dtype)
    mapped = jnp.einsum('fabej,ij->fabei', shaped, matrix, precision=lax.Precision.HIGHEST)
    return jnp.moveaxis(mapped.reshape(moved.shape[:-1] + (-1,)), -1, axis)


def direction_term(field, axis, speed, table, lift):
    per_element = table.shape[0]
    slope = jnp.moveaxis(element_map(field, axis, table), axis, -1)
    moved = jnp.moveaxis(field, axis, -1)
    length = moved.shape[-1]
    position = jnp.arange(length) % per_element
    speeds = speed.reshape(-1, 1, 1, 1)
    upwind = jnp.maximum(speeds, 0.0)
    downwind = jnp.maximum(-speeds, 0.0)
    inflow = jnp.where(position == 0, upwind * (jnp.roll(moved, 1, axis=-1) - moved), 0.0)
    outflow = jnp.where(position == per_element - 1, downwind * (jnp.roll(moved, -1, axis=-1) - moved), 0.0)
    term = -speeds * slope + lift * (inflow + outflow)
    return jnp.moveaxis(term, -1, axis)


def reaction_source(field, reactions, rates, energies):
    squash = jnp.tanh(field)
    temper = 1.5 + 0.5 * squash[-1]
    first_in = squash[reactions[:, 0]]
    second_in = squash[reactions[:, 1]]
    arrhenius = rates.reshape(-1, 1, 1, 1) * jnp.exp(-energies.reshape(-1, 1, 1, 1) / temper[None])
    progress = arrhenius * first_in * second_in
    labels = jnp.arange(field.shape[0]).astype(jnp.int32)
    stoich = ((reactions[:, 2][:, None] == labels[None, :]).astype(field.dtype)
              - (reactions[:, 0][:, None] == labels[None, :]).astype(field.dtype)
              - (reactions[:, 1][:, None] == labels[None, :]).astype(field.dtype))
    return jnp.einsum('rf,rzyx->fzyx', stoich, progress, precision=lax.Precision.HIGHEST)


def tendency(field, velocity, y_table, y_lift, reactions, rates, energies):
    fine_table = derivative_table(FINE_NODES)
    first_axis = direction_term(field, 3, velocity[0], fine_table, 28.0)
    second_axis = direction_term(field, 2, velocity[1], y_table, y_lift)
    third_axis = direction_term(field, 1, velocity[2], fine_table, 28.0)
    return first_axis + second_axis + third_axis + reaction_source(field, reactions, rates, energies)


def reference(u_start, guess, velocity, rates, energies, reactions):
    fine_table = derivative_table(FINE_NODES)
    coarse_table = derivative_table(COARSE_NODES)
    down_table = lagrange_table(FINE_NODES, COARSE_NODES)
    up_table = lagrange_table(COARSE_NODES, FINE_NODES)

    def fine_eval(field):
        return tendency(field, velocity, fine_table, 28.0, reactions, rates, energies)

    def coarse_eval(field):
        return tendency(field, velocity, coarse_table, 6.0, reactions, rates, energies)

    def restrict(field):
        return element_map(field, 2, down_table)

    def prolong(field):
        return element_map(field, 2, up_table)

    starts = [u_start] + [guess[n, 0] for n in range(1, SECTIONS)]
    middles = [guess[n, 1] for n in range(SECTIONS)]
    endings = [guess[n, 2] for n in range(SECTIONS)]
    coarse_ends = []
    for iteration in range(ITERS):
        records = []
        for n in range(SECTIONS):
            old_first = fine_eval(starts[n])
            old_middle = fine_eval(middles[n])
            old_last = fine_eval(endings[n])
            start_value = starts[n]
            middle = start_value + STEP * (5.0 * old_first + 8.0 * old_middle - old_last) / 24.0
            new_middle = fine_eval(middle)
            ending = middle + 0.5 * STEP * (new_middle - old_middle) + STEP * (-old_first + 8.0 * old_middle + 5.0 * old_last) / 24.0
            new_ending = fine_eval(ending)
            integral = STEP * (old_first + 4.0 * new_middle + new_ending) / 6.0
            coarse_first = restrict(start_value)
            records.append((start_value, middle, ending, coarse_first, restrict(ending), restrict(integral), coarse_eval(coarse_first)))
        begin = restrict(u_start)
        coarse_begins = []
        coarse_ends = []
        for n in range(SECTIONS):
            finish = begin + STEP * (coarse_eval(begin) - records[n][6]) + records[n][5]
            coarse_begins.append(begin)
            coarse_ends.append(finish)
            begin = finish
        new_starts = []
        new_middles = []
        new_endings = []
        for n in range(SECTIONS):
            start_value, middle, ending, coarse_first, coarse_last, unused_sum, unused_base = records[n]
            first_change = coarse_begins[n] - coarse_first
            last_change = coarse_ends[n] - coarse_last
            new_starts.append(start_value + prolong(first_change))
            new_middles.append(middle + prolong(0.5 * (first_change + last_change)))
            new_endings.append(ending + prolong(last_change))
        starts = [u_start] + [new_endings[n - 1] for n in range(1, SECTIONS)]
        middles = new_middles
        endings = new_endings
    return jnp.stack(endings), jnp.stack(coarse_ends)
```

```python
import jax
import jax.numpy as jnp
import numpy as np
from jax import lax
from jax.experimental import pallas as pl
from jax.experimental.pallas import tpu as pltpu
from jax.sharding import PartitionSpec as P

ITERS = 2


STEP = 0.01
HIGHEST = lax.Precision.HIGHEST
FINE_NODES = np.array(
    [
        -1.0,
        -0.8717401485096066,
        -0.5917001814331423,
        -0.2092992179024789,
        0.2092992179024789,
        0.5917001814331423,
        0.8717401485096066,
        1.0,
    ]
)
COARSE_NODES = np.array([-1.0, -0.4472135954999579, 0.4472135954999579, 1.0])


def lagrange_table(source, target):
    table = np.ones((len(target), len(source)))
    for j in range(len(source)):
        for m in range(len(source)):
            if m != j:
                table[:, j] *= (target - source[m]) / (source[j] - source[m])
    return table


def derivative_table(points):
    total = len(points)
    weights = np.array(
        [
            1.0 / np.prod([points[j] - points[m] for m in range(total) if m != j])
            for j in range(total)
        ]
    )
    table = np.zeros((total, total))
    for i in range(total):
        for j in range(total):
            if i != j:
                table[i, j] = weights[j] / weights[i] / (points[i] - points[j])
        table[i, i] = -np.sum(table[i])
    return table


def element_tables(length, table, lift):
    per_element = table.shape[0]
    block = np.kron(np.eye(length // per_element), table)
    position = np.arange(length) % per_element
    identity = np.eye(length)
    before = np.roll(identity, -1, axis=1)
    after = np.roll(identity, 1, axis=1)
    first_mask = np.where(position == 0, 1.0, 0.0)
    last_mask = np.where(position == per_element - 1, 1.0, 0.0)
    upwind = lift * first_mask[:, None] * (before - identity)
    downwind = lift * last_mask[:, None] * (after - identity)
    return (block, upwind, downwind)


def widen(matrix):
    length = matrix.shape[0]
    wider = np.zeros((length, matrix.shape[1] + 2))
    wider[:, 1:-1] = matrix
    return wider


def padded_tables(length, table, lift):
    block, upwind, downwind = element_tables(length, table, lift)
    block_wide = widen(block)
    upwind_wide = widen(upwind)
    downwind_wide = widen(downwind)
    upwind_wide[0, length] = 0.0
    upwind_wide[0, 0] = lift
    downwind_wide[length - 1, 1] = 0.0
    downwind_wide[length - 1, length + 1] = lift
    return (block_wide, upwind_wide, downwind_wide)


def field_operators(speed, tables):
    block = jnp.asarray(tables[0], jnp.float32)
    upwind = jnp.asarray(tables[1], jnp.float32)
    downwind = jnp.asarray(tables[2], jnp.float32)
    speeds = speed[:, None, None]
    return (
        -speeds * block + jnp.maximum(speeds, 0.0) * upwind + jnp.maximum(-speeds, 0.0) * downwind
    )


def plane_operator(y_mats, z_local):
    depth = z_local.shape[1]
    rows = y_mats.shape[1]
    eye_z = jnp.eye(depth, dtype=jnp.float32)
    eye_y = jnp.eye(rows, dtype=jnp.float32)
    op = (
        eye_z[None, :, None, :, None] * y_mats[:, None, :, None, :]
        + z_local[:, :, None, :, None] * eye_y[None, None, :, None, :]
    )
    fields = y_mats.shape[0]
    return op.reshape(fields, depth * rows, depth * rows)


def dot(a, b):
    return jnp.dot(a, b, precision=HIGHEST, preferred_element_type=jnp.float32)


def tendency_into(out_ref, b, v_ref, prev_ref, next_ref, lop_ref, xt_ref, zc_ref, rx_ref,
                  rate_ref, en_ref, s_ref):
    fields, span = v_ref.shape[1], v_ref.shape[2]
    rows = prev_ref.shape[2]

    def field_body(f, carry):
        v = v_ref[b, f]
        out_ref[b, f] = dot(lop_ref[f], v) + dot(v, xt_ref[f])
        out_ref[b, f, pl.ds(0, rows), :] = (
            out_ref[b, f, pl.ds(0, rows), :] + zc_ref[0, f] * prev_ref[b, f]
        )
        out_ref[b, f, pl.ds(span - rows, rows), :] = (
            out_ref[b, f, pl.ds(span - rows, rows), :] + zc_ref[1, f] * next_ref[b, f]
        )
        s_ref[f] = jnp.tanh(v)
        return carry

    lax.fori_loop(0, fields, field_body, 0)
    temper = 1.5 + 0.5 * s_ref[fields - 1]

    def reaction_body(r, carry):
        first = rx_ref[r, 0]
        second = rx_ref[r, 1]
        product = rx_ref[r, 2]
        progress = rate_ref[r] * jnp.exp(-en_ref[r] / temper) * s_ref[first] * s_ref[second]
        out_ref[b, product] = out_ref[b, product] + progress
        out_ref[b, first] = out_ref[b, first] - progress
        out_ref[b, second] = out_ref[b, second] - progress
        return carry

    lax.fori_loop(0, rx_ref.shape[0], reaction_body, 0)


def vmem():
    return pl.BlockSpec(memory_space=pltpu.VMEM)


def smem():
    return pl.BlockSpec(memory_space=pltpu.SMEM)


def tendency_cost(states, fields, span, columns, reactions):
    flops = states * fields * (2 * span * span * columns + 2 * span * columns * columns) * 6
    flops += states * span * columns * (8 * reactions + 4 * fields)
    trans = states * span * columns * (fields + 2 * reactions)
    return flops, trans


def call(kernel, ins, in_kinds, outs, scratch, flops, trans):
    nbytes = sum(int(np.prod(x.shape)) * 4 for x in ins) + sum(
        int(np.prod(o.shape)) * 4 for o in outs
    )
    return pl.pallas_call(
        kernel,
        out_shape=outs,
        in_specs=[smem() if k else vmem() for k in in_kinds],
        out_specs=tuple(vmem() for _ in outs),
        scratch_shapes=scratch,
        cost_estimate=pl.CostEstimate(
            flops=int(flops), transcendentals=int(trans), bytes_accessed=int(nbytes)
        ),
    )(*ins)


def per_device(u_start, guess, velocity, rates, energies, reactions):
    fields, depth, rows, columns = u_start.shape
    coarse_rows = rows // 2
    span = depth * rows
    coarse_span = depth * coarse_rows
    reaction_count = rates.shape[0]
    fine_table = derivative_table(FINE_NODES)
    coarse_table = derivative_table(COARSE_NODES)
    x_mats = field_operators(velocity[0], element_tables(columns, fine_table, 28.0))
    xt = jnp.swapaxes(x_mats, 1, 2)
    y_fine = field_operators(velocity[1], element_tables(rows, fine_table, 28.0))
    y_coarse = field_operators(velocity[1], element_tables(coarse_rows, coarse_table, 6.0))
    z_mats = field_operators(velocity[2], padded_tables(depth, fine_table, 28.0))
    z_local = z_mats[:, :, 1:-1]
    zc = jnp.stack([z_mats[:, 0, 0], z_mats[:, depth - 1, depth + 1]])
    lop_fine = plane_operator(y_fine, z_local)
    lop_coarse = plane_operator(y_coarse, z_local)
    restrict_rows = np.kron(np.eye(rows // 8), lagrange_table(FINE_NODES, COARSE_NODES))
    prolong_rows = np.kron(np.eye(rows // 8), lagrange_table(COARSE_NODES, FINE_NODES))
    rmat = jnp.asarray(np.kron(np.eye(depth), restrict_rows), jnp.float32)
    pmat = jnp.asarray(np.kron(np.eye(depth), prolong_rows), jnp.float32)
    restrict_plane = jnp.asarray(restrict_rows, jnp.float32)
    scalars = (zc, reactions.astype(jnp.int32), rates, energies)
    scalar_kinds = (True, True, True, True)

    space_n = lax.axis_size("space")
    sections = lax.axis_size("tm")
    section = lax.axis_index("tm")
    lead = (section == 0).astype(jnp.int32).reshape(1)

    def halo(x, plane_rows):
        head = x[..., :plane_rows, :]
        tail = x[..., x.shape[-2] - plane_rows:, :]
        prev = lax.ppermute(tail, "space", [(i, (i + 1) % space_n) for i in range(space_n)])
        nxt = lax.ppermute(head, "space", [((i + 1) % space_n, i) for i in range(space_n)])
        return prev, nxt

    f32 = jnp.float32
    fine_state = jax.ShapeDtypeStruct((1, fields, span, columns), f32)
    coarse_state = jax.ShapeDtypeStruct((fields, coarse_span, columns), f32)

    def nodes_kernel(u_ref, p_ref, n_ref, l_ref, x_ref, zc_ref, rx_ref, ra_ref, en_ref,
                     f_ref, a1_ref, s_ref):
        for b in range(u_ref.shape[0]):
            tendency_into(f_ref, b, u_ref, p_ref, n_ref, l_ref, x_ref, zc_ref, rx_ref, ra_ref,
                          en_ref, s_ref)

        def body(f, carry):
            a1_ref[0, f] = u_ref[0, f] + STEP * (
                5.0 * f_ref[0, f] + 8.0 * f_ref[1, f] - f_ref[2, f]
            ) / 24.0
            return carry

        lax.fori_loop(0, fields, body, 0)

    def middle_kernel(a1_ref, p_ref, n_ref, l_ref, x_ref, zc_ref, rx_ref, ra_ref, en_ref,
                      f_ref, g1_ref, a2_ref, s_ref):
        tendency_into(g1_ref, 0, a1_ref, p_ref, n_ref, l_ref, x_ref, zc_ref, rx_ref, ra_ref,
                      en_ref, s_ref)

        def body(f, carry):
            a2_ref[0, f] = (
                a1_ref[0, f]
                + 0.5 * STEP * (g1_ref[0, f] - f_ref[1, f])
                + STEP * (-f_ref[0, f] + 8.0 * f_ref[1, f] + 5.0 * f_ref[2, f]) / 24.0
            )
            return carry

        lax.fori_loop(0, fields, body, 0)

    def ending_kernel(a2_ref, p_ref, n_ref, l_ref, x_ref, zc_ref, rx_ref, ra_ref, en_ref,
                      f_ref, g1_ref, u_ref, r_ref, rint_ref, c1_ref, c0_ref, g2_ref, s_ref):
        tendency_into(g2_ref, 0, a2_ref, p_ref, n_ref, l_ref, x_ref, zc_ref, rx_ref, ra_ref,
                      en_ref, s_ref)

        def body(f, carry):
            integral = STEP * (f_ref[0, f] + 4.0 * g1_ref[0, f] + g2_ref[0, f]) / 6.0
            rint_ref[f] = dot(r_ref[...], integral)
            c1_ref[f] = dot(r_ref[...], a2_ref[0, f])
            c0_ref[f] = dot(r_ref[...], u_ref[0, f])
            return carry

        lax.fori_loop(0, fields, body, 0)

    def base_kernel(c_ref, p_ref, n_ref, l_ref, x_ref, zc_ref, rx_ref, ra_ref, en_ref,
                    out_ref, s_ref):
        tendency_into(out_ref, 0, c_ref, p_ref, n_ref, l_ref, x_ref, zc_ref, rx_ref, ra_ref,
                      en_ref, s_ref)

    def chain_kernel(w_ref, p_ref, n_ref, l_ref, x_ref, zc_ref, rx_ref, ra_ref, en_ref,
                     base_ref, rint_ref, out_ref, g_ref, s_ref):
        tendency_into(g_ref, 0, w_ref, p_ref, n_ref, l_ref, x_ref, zc_ref, rx_ref, ra_ref,
                      en_ref, s_ref)

        def body(f, carry):
            out_ref[f] = w_ref[0, f] + STEP * (g_ref[0, f] - base_ref[f]) + rint_ref[f]
            return carry

        lax.fori_loop(0, fields, body, 0)

    def correct_kernel(a1_ref, a2_ref, c0_ref, c1_ref, w0_ref, w1_ref, prev_ref, us_ref,
                       r_ref, pm_ref, lead_ref, out_ref):
        def body(f, carry):
            first_change = w0_ref[f] - c0_ref[f]
            last_change = w1_ref[f] - c1_ref[f]
            out_ref[1, f] = a1_ref[0, f] + dot(pm_ref[...], 0.5 * (first_change + last_change))
            out_ref[2, f] = a2_ref[0, f] + dot(pm_ref[...], last_change)
            handed = prev_ref[0, f]
            fixed = handed + dot(pm_ref[...], w0_ref[f] - dot(r_ref[...], handed))
            out_ref[0, f] = jnp.where(lead_ref[0] != 0, us_ref[f], fixed)
            return carry

        lax.fori_loop(0, fields, body, 0)

    def finish_kernel(a2_ref, c1_ref, w1_ref, pm_ref, out_ref):
        def body(f, carry):
            out_ref[0, f] = a2_ref[0, f] + dot(pm_ref[...], w1_ref[f] - c1_ref[f])
            return carry

        lax.fori_loop(0, fields, body, 0)

    fine_cost = tendency_cost(1, fields, span, columns, reaction_count)
    coarse_cost = tendency_cost(1, fields, coarse_span, columns, reaction_count)

    def fine_scratch():
        return pltpu.VMEM((fields, span, columns), f32)

    def coarse_scratch():
        return pltpu.VMEM((fields, coarse_span, columns), f32)

    u_flat = u_start.reshape(fields, span, columns)
    nodes = guess[0].reshape(3, fields, span, columns)
    nodes = jnp.concatenate([jnp.where(section == 0, u_flat, nodes[0])[None], nodes[1:]], axis=0)
    coarse_start = jnp.einsum("cy,fzyx->fzcx", restrict_plane,
                              u_start, precision=HIGHEST).reshape(fields, coarse_span, columns)
    start_halo = halo(coarse_start, coarse_rows)

    def coarse_step(w, w_halo, base, rint):
        return call(
            chain_kernel,
            (w[None], w_halo[0][None], w_halo[1][None], lop_coarse, xt) + scalars + (base, rint),
            (False,) * 5 + scalar_kinds + (False, False),
            (coarse_state,),
            [pltpu.VMEM((1, fields, coarse_span, columns), f32), coarse_scratch()],
            *coarse_cost,
        )[0]

    fine_end = None
    coarse_end = None
    for iteration in range(ITERS):
        node_prev, node_next = halo(nodes, rows)
        f_all, a1 = call(
            nodes_kernel,
            (nodes, node_prev, node_next, lop_fine, xt) + scalars,
            (False,) * 5 + scalar_kinds,
            (jax.ShapeDtypeStruct((3, fields, span, columns), f32), fine_state),
            [fine_scratch()],
            fine_cost[0] * 3, fine_cost[1] * 3,
        )
        c0_prev = jnp.einsum("cy,fyx->fcx", restrict_plane, node_prev[0], precision=HIGHEST)
        c0_next = jnp.einsum("cy,fyx->fcx", restrict_plane, node_next[0], precision=HIGHEST)
        a1_prev, a1_next = halo(a1, rows)
        g1, a2 = call(
            middle_kernel,
            (a1, a1_prev, a1_next, lop_fine, xt) + scalars + (f_all,),
            (False,) * 5 + scalar_kinds + (False,),
            (fine_state, fine_state),
            [fine_scratch()],
            *fine_cost,
        )
        a2_prev, a2_next = halo(a2, rows)
        rint, c1, c0 = call(
            ending_kernel,
            (a2, a2_prev, a2_next, lop_fine, xt) + scalars + (f_all, g1, nodes, rmat),
            (False,) * 5 + scalar_kinds + (False,) * 4,
            (coarse_state, coarse_state, coarse_state),
            [pltpu.VMEM((1, fields, span, columns), f32), fine_scratch()],
            *fine_cost,
        )
        (base,) = call(
            base_kernel,
            (c0[None], c0_prev[None], c0_next[None], lop_coarse, xt) + scalars,
            (False,) * 5 + scalar_kinds,
            (jax.ShapeDtypeStruct((1, fields, coarse_span, columns), f32),),
            [coarse_scratch()],
            *coarse_cost,
        )
        gathered = lax.all_gather(jnp.stack([base[0], rint]), "tm")
        last = iteration + 1 == ITERS
        if not last:
            a2_handed = lax.ppermute(a2, "tm", [(i, i + 1) for i in range(sections - 1)])
        w = coarse_start
        w_halo = start_halo
        chain = [w]
        for n in range(sections):
            w = coarse_step(w, w_halo, gathered[n, 0], gathered[n, 1])
            chain.append(w)
            if n + 1 < sections:
                w_halo = halo(w, coarse_rows)
        chain = jnp.stack(chain)
        w0 = lax.dynamic_index_in_dim(chain, section, 0, keepdims=False)
        w1 = lax.dynamic_index_in_dim(chain, section + 1, 0, keepdims=False)
        if last:
            (fine_end,) = call(
                finish_kernel,
                (a2, c1, w1, pmat),
                (False,) * 4,
                (fine_state,),
                [],
                2 * fields * span * coarse_span * columns * 6, 0,
            )
            coarse_end = w1
        else:
            (nodes,) = call(
                correct_kernel,
                (a1, a2, c0, c1, w0, w1, a2_handed, u_flat, rmat, pmat, lead),
                (False,) * 10 + (True,),
                (jax.ShapeDtypeStruct((3, fields, span, columns), f32),),
                [],
                8 * fields * span * coarse_span * columns * 6, 0,
            )
    fine_end = fine_end.reshape(1, fields, depth, rows, columns)
    coarse_end = coarse_end.reshape(1, fields, depth, coarse_rows, columns)
    return (fine_end, coarse_end)


def solution(mesh):
    return jax.shard_map(
        per_device,
        mesh=mesh,
        in_specs=(
            P(None, "space", None, None),
            P("tm", None, None, "space", None, None),
            P(),
            P(),
            P(),
            P(),
        ),
        out_specs=(P("tm", None, "space", None, None), P("tm", None, "space", None, None)),
        check_vma=False,
    )
```

```python
import jax
import jax.numpy as jnp
import numpy as np
from jax import lax
from jax.experimental import pallas as pl
from jax.experimental.pallas import tpu as pltpu
from jax.sharding import PartitionSpec as P

ITERS = 2


STEP = 0.01
HIGHEST = lax.Precision.HIGHEST
FINE_NODES = np.array(
    [
        -1.0,
        -0.8717401485096066,
        -0.5917001814331423,
        -0.2092992179024789,
        0.2092992179024789,
        0.5917001814331423,
        0.8717401485096066,
        1.0,
    ]
)
COARSE_NODES = np.array([-1.0, -0.4472135954999579, 0.4472135954999579, 1.0])


def lagrange_table(source, target):
    table = np.ones((len(target), len(source)))
    for j in range(len(source)):
        for m in range(len(source)):
            if m != j:
                table[:, j] *= (target - source[m]) / (source[j] - source[m])
    return table


def derivative_table(points):
    total = len(points)
    weights = np.array(
        [
            1.0 / np.prod([points[j] - points[m] for m in range(total) if m != j])
            for j in range(total)
        ]
    )
    table = np.zeros((total, total))
    for i in range(total):
        for j in range(total):
            if i != j:
                table[i, j] = weights[j] / weights[i] / (points[i] - points[j])
        table[i, i] = -np.sum(table[i])
    return table


def element_tables(length, table, lift):
    per_element = table.shape[0]
    block = np.kron(np.eye(length // per_element), table)
    position = np.arange(length) % per_element
    identity = np.eye(length)
    before = np.roll(identity, -1, axis=1)
    after = np.roll(identity, 1, axis=1)
    first_mask = np.where(position == 0, 1.0, 0.0)
    last_mask = np.where(position == per_element - 1, 1.0, 0.0)
    upwind = lift * first_mask[:, None] * (before - identity)
    downwind = lift * last_mask[:, None] * (after - identity)
    return (block, upwind, downwind)


def widen(matrix):
    length = matrix.shape[0]
    wider = np.zeros((length, matrix.shape[1] + 2))
    wider[:, 1:-1] = matrix
    return wider


def padded_tables(length, table, lift):
    block, upwind, downwind = element_tables(length, table, lift)
    block_wide = widen(block)
    upwind_wide = widen(upwind)
    downwind_wide = widen(downwind)
    upwind_wide[0, length] = 0.0
    upwind_wide[0, 0] = lift
    downwind_wide[length - 1, 1] = 0.0
    downwind_wide[length - 1, length + 1] = lift
    return (block_wide, upwind_wide, downwind_wide)


def field_operators(speed, tables):
    block = jnp.asarray(tables[0], jnp.float32)
    upwind = jnp.asarray(tables[1], jnp.float32)
    downwind = jnp.asarray(tables[2], jnp.float32)
    speeds = speed[:, None, None]
    return (
        -speeds * block + jnp.maximum(speeds, 0.0) * upwind + jnp.maximum(-speeds, 0.0) * downwind
    )


def speed_combination(speed, tables):
    block = jnp.asarray(tables[0], jnp.float32)[None]
    upwind = jnp.asarray(tables[1], jnp.float32)[None]
    downwind = jnp.asarray(tables[2], jnp.float32)[None]
    speeds = speed[:, None, None]
    return (
        -speeds * block + jnp.maximum(speeds, 0.0) * upwind + jnp.maximum(-speeds, 0.0) * downwind
    )


def dot(a, b):
    return jnp.dot(a, b, precision=HIGHEST, preferred_element_type=jnp.float32)


def tendency_into(out_ref, b, v_ref, prev_ref, next_ref, lop_ref, xt_ref, zc_ref, rx_ref,
                  rate_ref, en_ref, s_ref):
    fields, span = v_ref.shape[1], v_ref.shape[2]
    rows = prev_ref.shape[2]

    def field_body(f, carry):
        v = v_ref[b, f]
        out_ref[b, f] = dot(lop_ref[f], v) + dot(v, xt_ref[f])
        out_ref[b, f, pl.ds(0, rows), :] = (
            out_ref[b, f, pl.ds(0, rows), :] + zc_ref[0, f] * prev_ref[b, f]
        )
        out_ref[b, f, pl.ds(span - rows, rows), :] = (
            out_ref[b, f, pl.ds(span - rows, rows), :] + zc_ref[1, f] * next_ref[b, f]
        )
        s_ref[f] = jnp.tanh(v)
        return carry

    lax.fori_loop(0, fields, field_body, 0)
    cooling = 1.0 / (1.5 + 0.5 * s_ref[fields - 1])

    def reaction_body(r, carry):
        first = rx_ref[r, 0]
        second = rx_ref[r, 1]
        product = rx_ref[r, 2]
        progress = rate_ref[r] * jnp.exp(-en_ref[r] * cooling) * s_ref[first] * s_ref[second]
        out_ref[b, product] = out_ref[b, product] + progress
        out_ref[b, first] = out_ref[b, first] - progress
        out_ref[b, second] = out_ref[b, second] - progress
        return carry

    lax.fori_loop(0, rx_ref.shape[0], reaction_body, 0)


def vmem():
    return pl.BlockSpec(memory_space=pltpu.VMEM)


def smem():
    return pl.BlockSpec(memory_space=pltpu.SMEM)


def tendency_cost(states, fields, span, columns, reactions):
    flops = states * fields * (2 * span * span * columns + 2 * span * columns * columns) * 6
    flops += states * span * columns * (8 * reactions + 4 * fields)
    trans = states * span * columns * (fields + 2 * reactions)
    return flops, trans


def call(kernel, ins, in_kinds, outs, scratch, flops, trans):
    nbytes = sum(int(np.prod(x.shape)) * 4 for x in ins) + sum(
        int(np.prod(o.shape)) * 4 for o in outs
    )
    return pl.pallas_call(
        kernel,
        out_shape=outs,
        in_specs=[smem() if k else vmem() for k in in_kinds],
        out_specs=tuple(vmem() for _ in outs),
        scratch_shapes=scratch,
        cost_estimate=pl.CostEstimate(
            flops=int(flops), transcendentals=int(trans), bytes_accessed=int(nbytes)
        ),
    )(*ins)


def per_device(u_start, guess, velocity, rates, energies, reactions):
    fields, depth, rows, columns = u_start.shape
    coarse_rows = rows // 2
    span = depth * rows
    coarse_span = depth * coarse_rows
    reaction_count = rates.shape[0]
    fine_table = derivative_table(FINE_NODES)
    coarse_table = derivative_table(COARSE_NODES)
    x_tables = element_tables(columns, fine_table, 28.0)
    xt = speed_combination(velocity[0], [t.T for t in x_tables])
    y_fine_tables = element_tables(rows, fine_table, 28.0)
    y_coarse_tables = element_tables(coarse_rows, coarse_table, 6.0)
    z_tables = padded_tables(depth, fine_table, 28.0)
    z_local = [t[:, 1:-1] for t in z_tables]
    z_mats = field_operators(velocity[2], z_tables)
    zc = jnp.stack([z_mats[:, 0, 0], z_mats[:, depth - 1, depth + 1]])

    def plane_operator(y_tables, plane_rows):
        along_y = speed_combination(
            velocity[1], [np.kron(np.eye(depth), t) for t in y_tables]
        )
        along_z = speed_combination(
            velocity[2], [np.kron(t, np.eye(plane_rows)) for t in z_local]
        )
        return along_y + along_z

    lop_fine = plane_operator(y_fine_tables, rows)
    lop_coarse = plane_operator(y_coarse_tables, coarse_rows)
    restrict_rows = np.kron(np.eye(rows // 8), lagrange_table(FINE_NODES, COARSE_NODES))
    prolong_rows = np.kron(np.eye(rows // 8), lagrange_table(COARSE_NODES, FINE_NODES))
    rmat = jnp.asarray(np.kron(np.eye(depth), restrict_rows), jnp.float32)
    pmat = jnp.asarray(np.kron(np.eye(depth), prolong_rows), jnp.float32)
    restrict_plane = jnp.asarray(restrict_rows, jnp.float32)
    scalars = (zc, reactions.astype(jnp.int32), rates, energies)
    scalar_kinds = (True, True, True, True)

    space_n = lax.axis_size("space")
    sections = lax.axis_size("tm")
    section = lax.axis_index("tm")
    lead = (section == 0).astype(jnp.int32).reshape(1)

    def halo(x, plane_rows):
        head = x[..., :plane_rows, :]
        tail = x[..., x.shape[-2] - plane_rows:, :]
        prev = lax.ppermute(tail, "space", [(i, (i + 1) % space_n) for i in range(space_n)])
        nxt = lax.ppermute(head, "space", [((i + 1) % space_n, i) for i in range(space_n)])
        return prev, nxt

    f32 = jnp.float32
    fine_state = jax.ShapeDtypeStruct((1, fields, span, columns), f32)
    coarse_state = jax.ShapeDtypeStruct((fields, coarse_span, columns), f32)

    def nodes_kernel(u_ref, p_ref, n_ref, l_ref, x_ref, zc_ref, rx_ref, ra_ref, en_ref,
                     f_ref, a1_ref, s_ref):
        for b in range(u_ref.shape[0]):
            tendency_into(f_ref, b, u_ref, p_ref, n_ref, l_ref, x_ref, zc_ref, rx_ref, ra_ref,
                          en_ref, s_ref)

        def body(f, carry):
            a1_ref[0, f] = u_ref[0, f] + STEP * (
                5.0 * f_ref[0, f] + 8.0 * f_ref[1, f] - f_ref[2, f]
            ) / 24.0
            return carry

        lax.fori_loop(0, fields, body, 0)

    def middle_kernel(a1_ref, p_ref, n_ref, l_ref, x_ref, zc_ref, rx_ref, ra_ref, en_ref,
                      f_ref, g1_ref, a2_ref, s_ref):
        tendency_into(g1_ref, 0, a1_ref, p_ref, n_ref, l_ref, x_ref, zc_ref, rx_ref, ra_ref,
                      en_ref, s_ref)

        def body(f, carry):
            a2_ref[0, f] = (
                a1_ref[0, f]
                + 0.5 * STEP * (g1_ref[0, f] - f_ref[1, f])
                + STEP * (-f_ref[0, f] + 8.0 * f_ref[1, f] + 5.0 * f_ref[2, f]) / 24.0
            )
            return carry

        lax.fori_loop(0, fields, body, 0)

    def ending_kernel(a2_ref, p_ref, n_ref, l_ref, x_ref, zc_ref, rx_ref, ra_ref, en_ref,
                      f_ref, g1_ref, u_ref, r_ref, rint_ref, c1_ref, c0_ref, g2_ref, s_ref):
        tendency_into(g2_ref, 0, a2_ref, p_ref, n_ref, l_ref, x_ref, zc_ref, rx_ref, ra_ref,
                      en_ref, s_ref)

        def body(f, carry):
            integral = STEP * (f_ref[0, f] + 4.0 * g1_ref[0, f] + g2_ref[0, f]) / 6.0
            rint_ref[f] = dot(r_ref[...], integral)
            c1_ref[f] = dot(r_ref[...], a2_ref[0, f])
            c0_ref[f] = dot(r_ref[...], u_ref[0, f])
            return carry

        lax.fori_loop(0, fields, body, 0)

    def base_kernel(c_ref, p_ref, n_ref, l_ref, x_ref, zc_ref, rx_ref, ra_ref, en_ref,
                    out_ref, s_ref):
        tendency_into(out_ref, 0, c_ref, p_ref, n_ref, l_ref, x_ref, zc_ref, rx_ref, ra_ref,
                      en_ref, s_ref)

    def chain_kernel(lead_ref, w_ref, p_ref, n_ref, ws_ref, ps_ref, ns_ref, l_ref, x_ref,
                     zc_ref, rx_ref, ra_ref, en_ref, base_ref, rint_ref, out_ref, begin_ref,
                     bp_ref, bn_ref, g_ref, s_ref):
        @pl.when(lead_ref[0] != 0)
        def _():
            begin_ref[...] = ws_ref[...]
            bp_ref[...] = ps_ref[...]
            bn_ref[...] = ns_ref[...]

        @pl.when(lead_ref[0] == 0)
        def _():
            begin_ref[...] = w_ref[...]
            bp_ref[...] = p_ref[...]
            bn_ref[...] = n_ref[...]

        tendency_into(g_ref, 0, begin_ref, bp_ref, bn_ref, l_ref, x_ref, zc_ref, rx_ref, ra_ref,
                      en_ref, s_ref)

        def body(f, carry):
            out_ref[0, f] = begin_ref[0, f] + STEP * (g_ref[0, f] - base_ref[0, f]) + rint_ref[0, f]
            return carry

        lax.fori_loop(0, fields, body, 0)

    def correct_kernel(a1_ref, a2_ref, c0_ref, c1_ref, w0_ref, w1_ref, prev_ref, us_ref,
                       r_ref, pm_ref, lead_ref, out_ref):
        def body(f, carry):
            first_change = w0_ref[f] - c0_ref[f]
            last_change = w1_ref[f] - c1_ref[f]
            out_ref[1, f] = a1_ref[0, f] + dot(pm_ref[...], 0.5 * (first_change + last_change))
            out_ref[2, f] = a2_ref[0, f] + dot(pm_ref[...], last_change)
            handed = prev_ref[0, f]
            fixed = handed + dot(pm_ref[...], w0_ref[f] - dot(r_ref[...], handed))
            out_ref[0, f] = jnp.where(lead_ref[0] != 0, us_ref[f], fixed)
            return carry

        lax.fori_loop(0, fields, body, 0)

    def finish_kernel(a2_ref, c1_ref, w1_ref, pm_ref, out_ref):
        def body(f, carry):
            out_ref[0, f] = a2_ref[0, f] + dot(pm_ref[...], w1_ref[f] - c1_ref[f])
            return carry

        lax.fori_loop(0, fields, body, 0)

    fine_cost = tendency_cost(1, fields, span, columns, reaction_count)
    coarse_cost = tendency_cost(1, fields, coarse_span, columns, reaction_count)

    def fine_scratch():
        return pltpu.VMEM((fields, span, columns), f32)

    def coarse_scratch():
        return pltpu.VMEM((fields, coarse_span, columns), f32)

    u_flat = u_start.reshape(fields, span, columns)
    nodes = guess[0].reshape(3, fields, span, columns)
    nodes = jnp.concatenate([jnp.where(section == 0, u_flat, nodes[0])[None], nodes[1:]], axis=0)
    coarse_start = jnp.einsum("cy,fzyx->fzcx", restrict_plane,
                              u_start, precision=HIGHEST).reshape(fields, coarse_span, columns)
    start_halo = halo(coarse_start, coarse_rows)

    coarse_one = jax.ShapeDtypeStruct((1, fields, coarse_span, columns), f32)
    plane_one = jax.ShapeDtypeStruct((1, fields, coarse_rows, columns), f32)

    def coarse_step(flag, w, w_halo, base, rint):
        return call(
            chain_kernel,
            (flag, w, w_halo[0], w_halo[1], coarse_start[None], start_halo[0][None],
             start_halo[1][None], lop_coarse, xt) + scalars + (base, rint),
            (True,) + (False,) * 8 + scalar_kinds + (False, False),
            (coarse_one, coarse_one, plane_one, plane_one),
            [pltpu.VMEM((1, fields, coarse_span, columns), f32), coarse_scratch()],
            *coarse_cost,
        )

    tm_n = sections
    both = ("tm", "space")
    hop_pairs = [(d, d + 1) for d in range(tm_n - 1)]
    prev_pairs = [
        (d * space_n + s, (d + 1) * space_n + (s + 1) % space_n)
        for d in range(tm_n - 1) for s in range(space_n)
    ]
    next_pairs = [
        (d * space_n + s, (d + 1) * space_n + (s - 1) % space_n)
        for d in range(tm_n - 1) for s in range(space_n)
    ]
    always = jnp.ones((1,), jnp.int32)

    fine_end = None
    coarse_end = None
    for iteration in range(ITERS):
        node_prev, node_next = halo(nodes, rows)
        f_all, a1 = call(
            nodes_kernel,
            (nodes, node_prev, node_next, lop_fine, xt) + scalars,
            (False,) * 5 + scalar_kinds,
            (jax.ShapeDtypeStruct((3, fields, span, columns), f32), fine_state),
            [fine_scratch()],
            fine_cost[0] * 3, fine_cost[1] * 3,
        )
        c0_prev = jnp.einsum("cy,fyx->fcx", restrict_plane, node_prev[0], precision=HIGHEST)
        c0_next = jnp.einsum("cy,fyx->fcx", restrict_plane, node_next[0], precision=HIGHEST)
        a1_prev, a1_next = halo(a1, rows)
        g1, a2 = call(
            middle_kernel,
            (a1, a1_prev, a1_next, lop_fine, xt) + scalars + (f_all,),
            (False,) * 5 + scalar_kinds + (False,),
            (fine_state, fine_state),
            [fine_scratch()],
            *fine_cost,
        )
        a2_prev, a2_next = halo(a2, rows)
        rint, c1, c0 = call(
            ending_kernel,
            (a2, a2_prev, a2_next, lop_fine, xt) + scalars + (f_all, g1, nodes, rmat),
            (False,) * 5 + scalar_kinds + (False,) * 4,
            (coarse_state, coarse_state, coarse_state),
            [pltpu.VMEM((1, fields, span, columns), f32), fine_scratch()],
            *fine_cost,
        )
        (base,) = call(
            base_kernel,
            (c0[None], c0_prev[None], c0_next[None], lop_coarse, xt) + scalars,
            (False,) * 5 + scalar_kinds,
            (jax.ShapeDtypeStruct((1, fields, coarse_span, columns), f32),),
            [coarse_scratch()],
            *coarse_cost,
        )
        last = iteration + 1 == ITERS
        if not last:
            a2_handed = lax.ppermute(a2, "tm", hop_pairs)
        begin = coarse_start[None]
        begin_halo = (start_halo[0][None], start_halo[1][None])
        flag = always
        for n in range(sections):
            finish, w0, _, _ = coarse_step(flag, begin, begin_halo, base, rint[None])
            if n + 1 < sections:
                begin = lax.ppermute(finish, "tm", hop_pairs)
                tail = finish[:, :, coarse_span - coarse_rows:, :]
                head = finish[:, :, :coarse_rows, :]
                begin_halo = (lax.ppermute(tail, both, prev_pairs),
                              lax.ppermute(head, both, next_pairs))
                flag = lead
        w0 = w0[0]
        w1 = finish[0]
        if last:
            (fine_end,) = call(
                finish_kernel,
                (a2, c1, w1, pmat),
                (False,) * 4,
                (fine_state,),
                [],
                2 * fields * span * coarse_span * columns * 6, 0,
            )
            coarse_end = w1
        else:
            (nodes,) = call(
                correct_kernel,
                (a1, a2, c0, c1, w0, w1, a2_handed, u_flat, rmat, pmat, lead),
                (False,) * 10 + (True,),
                (jax.ShapeDtypeStruct((3, fields, span, columns), f32),),
                [],
                8 * fields * span * coarse_span * columns * 6, 0,
            )
    fine_end = fine_end.reshape(1, fields, depth, rows, columns)
    coarse_end = coarse_end.reshape(1, fields, depth, coarse_rows, columns)
    return (fine_end, coarse_end)


def solution(mesh):
    return jax.shard_map(
        per_device,
        mesh=mesh,
        in_specs=(
            P(None, "space", None, None),
            P("tm", None, None, "space", None, None),
            P(),
            P(),
            P(),
            P(),
        ),
        out_specs=(P("tm", None, "space", None, None), P("tm", None, "space", None, None)),
        check_vma=False,
    )
```

```python
import jax
import jax.numpy as jnp
import numpy as np
from jax import lax
from jax.experimental import pallas as pl
from jax.experimental.pallas import tpu as pltpu
from jax.sharding import PartitionSpec as P

ITERS = 2


STEP = 0.01
HIGHEST = lax.Precision.HIGHEST
FINE_NODES = np.array(
    [
        -1.0,
        -0.8717401485096066,
        -0.5917001814331423,
        -0.2092992179024789,
        0.2092992179024789,
        0.5917001814331423,
        0.8717401485096066,
        1.0,
    ]
)
COARSE_NODES = np.array([-1.0, -0.4472135954999579, 0.4472135954999579, 1.0])


def lagrange_table(source, target):
    table = np.ones((len(target), len(source)))
    for j in range(len(source)):
        for m in range(len(source)):
            if m != j:
                table[:, j] *= (target - source[m]) / (source[j] - source[m])
    return table


def derivative_table(points):
    total = len(points)
    weights = np.array(
        [
            1.0 / np.prod([points[j] - points[m] for m in range(total) if m != j])
            for j in range(total)
        ]
    )
    table = np.zeros((total, total))
    for i in range(total):
        for j in range(total):
            if i != j:
                table[i, j] = weights[j] / weights[i] / (points[i] - points[j])
        table[i, i] = -np.sum(table[i])
    return table


def element_tables(length, table, lift):
    per_element = table.shape[0]
    block = np.kron(np.eye(length // per_element), table)
    position = np.arange(length) % per_element
    identity = np.eye(length)
    before = np.roll(identity, -1, axis=1)
    after = np.roll(identity, 1, axis=1)
    first_mask = np.where(position == 0, 1.0, 0.0)
    last_mask = np.where(position == per_element - 1, 1.0, 0.0)
    upwind = lift * first_mask[:, None] * (before - identity)
    downwind = lift * last_mask[:, None] * (after - identity)
    return (block, upwind, downwind)


def widen(matrix):
    length = matrix.shape[0]
    wider = np.zeros((length, matrix.shape[1] + 2))
    wider[:, 1:-1] = matrix
    return wider


def padded_tables(length, table, lift):
    block, upwind, downwind = element_tables(length, table, lift)
    block_wide = widen(block)
    upwind_wide = widen(upwind)
    downwind_wide = widen(downwind)
    upwind_wide[0, length] = 0.0
    upwind_wide[0, 0] = lift
    downwind_wide[length - 1, 1] = 0.0
    downwind_wide[length - 1, length + 1] = lift
    return (block_wide, upwind_wide, downwind_wide)


def field_operators(speed, tables):
    block = jnp.asarray(tables[0], jnp.float32)
    upwind = jnp.asarray(tables[1], jnp.float32)
    downwind = jnp.asarray(tables[2], jnp.float32)
    speeds = speed[:, None, None]
    return (
        -speeds * block + jnp.maximum(speeds, 0.0) * upwind + jnp.maximum(-speeds, 0.0) * downwind
    )


def speed_combination(speed, tables):
    block = jnp.asarray(tables[0], jnp.float32)[None]
    upwind = jnp.asarray(tables[1], jnp.float32)[None]
    downwind = jnp.asarray(tables[2], jnp.float32)[None]
    speeds = speed[:, None, None]
    return (
        -speeds * block + jnp.maximum(speeds, 0.0) * upwind + jnp.maximum(-speeds, 0.0) * downwind
    )


def dot(a, b):
    return jnp.dot(a, b, precision=HIGHEST, preferred_element_type=jnp.float32)


def tdot(a, b):
    return jnp.dot(a, b, precision=lax.Precision.HIGH, preferred_element_type=jnp.float32)


def lanes(parts):
    return jnp.concatenate(parts, axis=1)


def unlanes(wide, width):
    return [wide[:, i * width:(i + 1) * width] for i in range(wide.shape[1] // width)]


def tendency_into(out_ref, b, v_ref, prev_ref, next_ref, lop_ref, xt_ref, zc_ref, rx_ref,
                  rate_ref, en_ref, s_ref):
    fields, span = v_ref.shape[1], v_ref.shape[2]
    rows = prev_ref.shape[2]

    def field_body(f, carry):
        v = v_ref[b, f]
        out_ref[b, f] = tdot(lop_ref[f], v) + tdot(v, xt_ref[f])
        out_ref[b, f, pl.ds(0, rows), :] = (
            out_ref[b, f, pl.ds(0, rows), :] + zc_ref[0, f] * prev_ref[b, f]
        )
        out_ref[b, f, pl.ds(span - rows, rows), :] = (
            out_ref[b, f, pl.ds(span - rows, rows), :] + zc_ref[1, f] * next_ref[b, f]
        )
        s_ref[f] = jnp.tanh(v)
        return carry

    lax.fori_loop(0, fields, field_body, 0)
    cooling = 1.0 / (1.5 + 0.5 * s_ref[fields - 1])

    def reaction_body(r, carry):
        first = rx_ref[r, 0]
        second = rx_ref[r, 1]
        product = rx_ref[r, 2]
        progress = rate_ref[r] * jnp.exp(-en_ref[r] * cooling) * s_ref[first] * s_ref[second]
        out_ref[b, product] = out_ref[b, product] + progress
        out_ref[b, first] = out_ref[b, first] - progress
        out_ref[b, second] = out_ref[b, second] - progress
        return carry

    lax.fori_loop(0, rx_ref.shape[0], reaction_body, 0)


def vmem():
    return pl.BlockSpec(memory_space=pltpu.VMEM)


def smem():
    return pl.BlockSpec(memory_space=pltpu.SMEM)


def tendency_cost(states, fields, span, columns, reactions):
    flops = states * fields * (2 * span * span * columns + 2 * span * columns * columns) * 6
    flops += states * span * columns * (8 * reactions + 4 * fields)
    trans = states * span * columns * (fields + 2 * reactions)
    return flops, trans


def call(kernel, ins, in_kinds, outs, scratch, flops, trans):
    nbytes = sum(int(np.prod(x.shape)) * 4 for x in ins) + sum(
        int(np.prod(o.shape)) * 4 for o in outs
    )
    return pl.pallas_call(
        kernel,
        out_shape=outs,
        in_specs=[smem() if k else vmem() for k in in_kinds],
        out_specs=tuple(vmem() for _ in outs),
        scratch_shapes=scratch,
        cost_estimate=pl.CostEstimate(
            flops=int(flops), transcendentals=int(trans), bytes_accessed=int(nbytes)
        ),
    )(*ins)


def per_device(u_start, guess, velocity, rates, energies, reactions):
    fields, depth, rows, columns = u_start.shape
    coarse_rows = rows // 2
    span = depth * rows
    coarse_span = depth * coarse_rows
    reaction_count = rates.shape[0]
    fine_table = derivative_table(FINE_NODES)
    coarse_table = derivative_table(COARSE_NODES)
    x_tables = element_tables(columns, fine_table, 28.0)
    xt = speed_combination(velocity[0], [t.T for t in x_tables])
    y_fine_tables = element_tables(rows, fine_table, 28.0)
    y_coarse_tables = element_tables(coarse_rows, coarse_table, 6.0)
    z_tables = padded_tables(depth, fine_table, 28.0)
    z_local = [t[:, 1:-1] for t in z_tables]
    z_mats = field_operators(velocity[2], z_tables)
    zc = jnp.stack([z_mats[:, 0, 0], z_mats[:, depth - 1, depth + 1]])

    def plane_operator(y_tables, plane_rows):
        along_y = speed_combination(
            velocity[1], [np.kron(np.eye(depth), t) for t in y_tables]
        )
        along_z = speed_combination(
            velocity[2], [np.kron(t, np.eye(plane_rows)) for t in z_local]
        )
        return along_y + along_z

    lop_fine = plane_operator(y_fine_tables, rows)
    lop_coarse = plane_operator(y_coarse_tables, coarse_rows)
    restrict_rows = np.kron(np.eye(rows // 8), lagrange_table(FINE_NODES, COARSE_NODES))
    prolong_rows = np.kron(np.eye(rows // 8), lagrange_table(COARSE_NODES, FINE_NODES))
    rmat = jnp.asarray(np.kron(np.eye(depth), restrict_rows), jnp.float32)
    pmat = jnp.asarray(np.kron(np.eye(depth), prolong_rows), jnp.float32)
    restrict_plane = jnp.asarray(restrict_rows, jnp.float32)
    scalars = (zc, reactions.astype(jnp.int32), rates, energies)
    scalar_kinds = (True, True, True, True)

    space_n = lax.axis_size("space")
    sections = lax.axis_size("tm")
    section = lax.axis_index("tm")
    lead = (section == 0).astype(jnp.int32).reshape(1)

    def halo(x, plane_rows):
        head = x[..., :plane_rows, :]
        tail = x[..., x.shape[-2] - plane_rows:, :]
        prev = lax.ppermute(tail, "space", [(i, (i + 1) % space_n) for i in range(space_n)])
        nxt = lax.ppermute(head, "space", [((i + 1) % space_n, i) for i in range(space_n)])
        return prev, nxt

    f32 = jnp.float32
    fine_state = jax.ShapeDtypeStruct((1, fields, span, columns), f32)
    coarse_state = jax.ShapeDtypeStruct((fields, coarse_span, columns), f32)

    def nodes_kernel(u_ref, p_ref, n_ref, l_ref, x_ref, zc_ref, rx_ref, ra_ref, en_ref,
                     f_ref, a1_ref, s_ref):
        for b in range(u_ref.shape[0]):
            tendency_into(f_ref, b, u_ref, p_ref, n_ref, l_ref, x_ref, zc_ref, rx_ref, ra_ref,
                          en_ref, s_ref)

        def body(f, carry):
            a1_ref[0, f] = u_ref[0, f] + STEP * (
                5.0 * f_ref[0, f] + 8.0 * f_ref[1, f] - f_ref[2, f]
            ) / 24.0
            return carry

        lax.fori_loop(0, fields, body, 0)

    def middle_kernel(a1_ref, p_ref, n_ref, l_ref, x_ref, zc_ref, rx_ref, ra_ref, en_ref,
                      f_ref, g1_ref, a2_ref, s_ref):
        tendency_into(g1_ref, 0, a1_ref, p_ref, n_ref, l_ref, x_ref, zc_ref, rx_ref, ra_ref,
                      en_ref, s_ref)

        def body(f, carry):
            a2_ref[0, f] = (
                a1_ref[0, f]
                + 0.5 * STEP * (g1_ref[0, f] - f_ref[1, f])
                + STEP * (-f_ref[0, f] + 8.0 * f_ref[1, f] + 5.0 * f_ref[2, f]) / 24.0
            )
            return carry

        lax.fori_loop(0, fields, body, 0)

    def ending_kernel(a2_ref, p_ref, n_ref, l_ref, x_ref, zc_ref, rx_ref, ra_ref, en_ref,
                      f_ref, g1_ref, u_ref, r_ref, rint_ref, c1_ref, c0_ref, g2_ref, s_ref):
        tendency_into(g2_ref, 0, a2_ref, p_ref, n_ref, l_ref, x_ref, zc_ref, rx_ref, ra_ref,
                      en_ref, s_ref)

        def body(f, carry):
            g2_ref[0, f] = STEP * (f_ref[0, f] + 4.0 * g1_ref[0, f] + g2_ref[0, f]) / 6.0
            return carry

        lax.fori_loop(0, fields, body, 0)
        rm = r_ref[...]
        for dst, src_ref, lead_index in ((rint_ref, g2_ref, 0), (c1_ref, a2_ref, 0), (c0_ref, u_ref, 0)):
            wide = dot(rm, lanes([src_ref[lead_index, f] for f in range(fields)]))
            for f, part in enumerate(unlanes(wide, columns)):
                dst[f] = part

    def base_kernel(c_ref, p_ref, n_ref, l_ref, x_ref, zc_ref, rx_ref, ra_ref, en_ref,
                    out_ref, s_ref):
        tendency_into(out_ref, 0, c_ref, p_ref, n_ref, l_ref, x_ref, zc_ref, rx_ref, ra_ref,
                      en_ref, s_ref)

    def chain_kernel(lead_ref, w_ref, p_ref, n_ref, ws_ref, ps_ref, ns_ref, l_ref, x_ref,
                     zc_ref, rx_ref, ra_ref, en_ref, base_ref, rint_ref, out_ref, begin_ref,
                     bp_ref, bn_ref, g_ref, s_ref):
        @pl.when(lead_ref[0] != 0)
        def _():
            begin_ref[...] = ws_ref[...]
            bp_ref[...] = ps_ref[...]
            bn_ref[...] = ns_ref[...]

        @pl.when(lead_ref[0] == 0)
        def _():
            begin_ref[...] = w_ref[...]
            bp_ref[...] = p_ref[...]
            bn_ref[...] = n_ref[...]

        tendency_into(g_ref, 0, begin_ref, bp_ref, bn_ref, l_ref, x_ref, zc_ref, rx_ref, ra_ref,
                      en_ref, s_ref)

        def body(f, carry):
            out_ref[0, f] = begin_ref[0, f] + STEP * (g_ref[0, f] - base_ref[0, f]) + rint_ref[0, f]
            return carry

        lax.fori_loop(0, fields, body, 0)

    def correct_kernel(a1_ref, a2_ref, c0_ref, c1_ref, w0_ref, w1_ref, prev_ref, us_ref,
                       r_ref, pm_ref, lead_ref, out_ref):
        pm = pm_ref[...]
        first_change = [w0_ref[f] - c0_ref[f] for f in range(fields)]
        last_change = [w1_ref[f] - c1_ref[f] for f in range(fields)]
        middle_fix = unlanes(
            dot(pm, lanes([0.5 * (first_change[f] + last_change[f]) for f in range(fields)])),
            columns,
        )
        last_fix = unlanes(dot(pm, lanes(last_change)), columns)
        handed = lanes([prev_ref[0, f] for f in range(fields)])
        handed_fix = unlanes(
            dot(pm, lanes([w0_ref[f] for f in range(fields)]) - dot(r_ref[...], handed)),
            columns,
        )
        for f in range(fields):
            out_ref[1, f] = a1_ref[0, f] + middle_fix[f]
            out_ref[2, f] = a2_ref[0, f] + last_fix[f]
            out_ref[0, f] = jnp.where(
                lead_ref[0] != 0, us_ref[f], prev_ref[0, f] + handed_fix[f]
            )

    def finish_kernel(a2_ref, c1_ref, w1_ref, pm_ref, out_ref):
        fix = unlanes(
            dot(pm_ref[...], lanes([w1_ref[f] - c1_ref[f] for f in range(fields)])), columns
        )
        for f in range(fields):
            out_ref[0, f] = a2_ref[0, f] + fix[f]

    fine_cost = tendency_cost(1, fields, span, columns, reaction_count)
    coarse_cost = tendency_cost(1, fields, coarse_span, columns, reaction_count)

    def fine_scratch():
        return pltpu.VMEM((fields, span, columns), f32)

    def coarse_scratch():
        return pltpu.VMEM((fields, coarse_span, columns), f32)

    u_flat = u_start.reshape(fields, span, columns)
    nodes = guess[0].reshape(3, fields, span, columns)
    nodes = jnp.concatenate([jnp.where(section == 0, u_flat, nodes[0])[None], nodes[1:]], axis=0)
    coarse_start = jnp.einsum("cy,fzyx->fzcx", restrict_plane,
                              u_start, precision=HIGHEST).reshape(fields, coarse_span, columns)
    start_halo = halo(coarse_start, coarse_rows)

    coarse_one = jax.ShapeDtypeStruct((1, fields, coarse_span, columns), f32)
    plane_one = jax.ShapeDtypeStruct((1, fields, coarse_rows, columns), f32)

    def coarse_step(flag, w, w_halo, base, rint):
        return call(
            chain_kernel,
            (flag, w, w_halo[0], w_halo[1], coarse_start[None], start_halo[0][None],
             start_halo[1][None], lop_coarse, xt) + scalars + (base, rint),
            (True,) + (False,) * 8 + scalar_kinds + (False, False),
            (coarse_one, coarse_one, plane_one, plane_one),
            [pltpu.VMEM((1, fields, coarse_span, columns), f32), coarse_scratch()],
            *coarse_cost,
        )

    tm_n = sections
    both = ("tm", "space")
    hop_pairs = [(d, d + 1) for d in range(tm_n - 1)]
    prev_pairs = [
        (d * space_n + s, (d + 1) * space_n + (s + 1) % space_n)
        for d in range(tm_n - 1) for s in range(space_n)
    ]
    next_pairs = [
        (d * space_n + s, (d + 1) * space_n + (s - 1) % space_n)
        for d in range(tm_n - 1) for s in range(space_n)
    ]
    always = jnp.ones((1,), jnp.int32)

    fine_end = None
    coarse_end = None
    for iteration in range(ITERS):
        node_prev, node_next = halo(nodes, rows)
        f_all, a1 = call(
            nodes_kernel,
            (nodes, node_prev, node_next, lop_fine, xt) + scalars,
            (False,) * 5 + scalar_kinds,
            (jax.ShapeDtypeStruct((3, fields, span, columns), f32), fine_state),
            [fine_scratch()],
            fine_cost[0] * 3, fine_cost[1] * 3,
        )
        c0_prev = jnp.einsum("cy,fyx->fcx", restrict_plane, node_prev[0], precision=HIGHEST)
        c0_next = jnp.einsum("cy,fyx->fcx", restrict_plane, node_next[0], precision=HIGHEST)
        a1_prev, a1_next = halo(a1, rows)
        g1, a2 = call(
            middle_kernel,
            (a1, a1_prev, a1_next, lop_fine, xt) + scalars + (f_all,),
            (False,) * 5 + scalar_kinds + (False,),
            (fine_state, fine_state),
            [fine_scratch()],
            *fine_cost,
        )
        a2_prev, a2_next = halo(a2, rows)
        rint, c1, c0 = call(
            ending_kernel,
            (a2, a2_prev, a2_next, lop_fine, xt) + scalars + (f_all, g1, nodes, rmat),
            (False,) * 5 + scalar_kinds + (False,) * 4,
            (coarse_state, coarse_state, coarse_state),
            [pltpu.VMEM((1, fields, span, columns), f32), fine_scratch()],
            *fine_cost,
        )
        (base,) = call(
            base_kernel,
            (c0[None], c0_prev[None], c0_next[None], lop_coarse, xt) + scalars,
            (False,) * 5 + scalar_kinds,
            (jax.ShapeDtypeStruct((1, fields, coarse_span, columns), f32),),
            [coarse_scratch()],
            *coarse_cost,
        )
        last = iteration + 1 == ITERS
        if not last:
            a2_handed = lax.ppermute(a2, "tm", hop_pairs)
        begin = coarse_start[None]
        begin_halo = (start_halo[0][None], start_halo[1][None])
        flag = always
        for n in range(sections):
            finish, w0, _, _ = coarse_step(flag, begin, begin_halo, base, rint[None])
            if n + 1 < sections:
                begin = lax.ppermute(finish, "tm", hop_pairs)
                tail = finish[:, :, coarse_span - coarse_rows:, :]
                head = finish[:, :, :coarse_rows, :]
                begin_halo = (lax.ppermute(tail, both, prev_pairs),
                              lax.ppermute(head, both, next_pairs))
                flag = lead
        w0 = w0[0]
        w1 = finish[0]
        if last:
            (fine_end,) = call(
                finish_kernel,
                (a2, c1, w1, pmat),
                (False,) * 4,
                (fine_state,),
                [],
                2 * fields * span * coarse_span * columns * 6, 0,
            )
            coarse_end = w1
        else:
            (nodes,) = call(
                correct_kernel,
                (a1, a2, c0, c1, w0, w1, a2_handed, u_flat, rmat, pmat, lead),
                (False,) * 10 + (True,),
                (jax.ShapeDtypeStruct((3, fields, span, columns), f32),),
                [],
                8 * fields * span * coarse_span * columns * 6, 0,
            )
    fine_end = fine_end.reshape(1, fields, depth, rows, columns)
    coarse_end = coarse_end.reshape(1, fields, depth, coarse_rows, columns)
    return (fine_end, coarse_end)


def solution(mesh):
    return jax.shard_map(
        per_device,
        mesh=mesh,
        in_specs=(
            P(None, "space", None, None),
            P("tm", None, None, "space", None, None),
            P(),
            P(),
            P(),
            P(),
        ),
        out_specs=(P("tm", None, "space", None, None), P("tm", None, "space", None, None)),
        check_vma=False,
    )
```

```python
import jax
import jax.numpy as jnp
import numpy as np
from jax import lax
from jax.experimental import pallas as pl
from jax.experimental.pallas import tpu as pltpu
from jax.sharding import PartitionSpec as P

ITERS = 2


STEP = 0.01
HIGHEST = lax.Precision.HIGHEST
FINE_NODES = np.array(
    [
        -1.0,
        -0.8717401485096066,
        -0.5917001814331423,
        -0.2092992179024789,
        0.2092992179024789,
        0.5917001814331423,
        0.8717401485096066,
        1.0,
    ]
)
COARSE_NODES = np.array([-1.0, -0.4472135954999579, 0.4472135954999579, 1.0])


def lagrange_table(source, target):
    table = np.ones((len(target), len(source)))
    for j in range(len(source)):
        for m in range(len(source)):
            if m != j:
                table[:, j] *= (target - source[m]) / (source[j] - source[m])
    return table


def derivative_table(points):
    total = len(points)
    weights = np.array(
        [
            1.0 / np.prod([points[j] - points[m] for m in range(total) if m != j])
            for j in range(total)
        ]
    )
    table = np.zeros((total, total))
    for i in range(total):
        for j in range(total):
            if i != j:
                table[i, j] = weights[j] / weights[i] / (points[i] - points[j])
        table[i, i] = -np.sum(table[i])
    return table


def element_tables(length, table, lift):
    per_element = table.shape[0]
    block = np.kron(np.eye(length // per_element), table)
    position = np.arange(length) % per_element
    identity = np.eye(length)
    before = np.roll(identity, -1, axis=1)
    after = np.roll(identity, 1, axis=1)
    first_mask = np.where(position == 0, 1.0, 0.0)
    last_mask = np.where(position == per_element - 1, 1.0, 0.0)
    upwind = lift * first_mask[:, None] * (before - identity)
    downwind = lift * last_mask[:, None] * (after - identity)
    return (block, upwind, downwind)


def widen(matrix):
    length = matrix.shape[0]
    wider = np.zeros((length, matrix.shape[1] + 2))
    wider[:, 1:-1] = matrix
    return wider


def padded_tables(length, table, lift):
    block, upwind, downwind = element_tables(length, table, lift)
    block_wide = widen(block)
    upwind_wide = widen(upwind)
    downwind_wide = widen(downwind)
    upwind_wide[0, length] = 0.0
    upwind_wide[0, 0] = lift
    downwind_wide[length - 1, 1] = 0.0
    downwind_wide[length - 1, length + 1] = lift
    return (block_wide, upwind_wide, downwind_wide)


def field_operators(speed, tables):
    block = jnp.asarray(tables[0], jnp.float32)
    upwind = jnp.asarray(tables[1], jnp.float32)
    downwind = jnp.asarray(tables[2], jnp.float32)
    speeds = speed[:, None, None]
    return (
        -speeds * block + jnp.maximum(speeds, 0.0) * upwind + jnp.maximum(-speeds, 0.0) * downwind
    )


def speed_combination(speed, tables):
    block = jnp.asarray(tables[0], jnp.float32)[None]
    upwind = jnp.asarray(tables[1], jnp.float32)[None]
    downwind = jnp.asarray(tables[2], jnp.float32)[None]
    speeds = speed[:, None, None]
    return (
        -speeds * block + jnp.maximum(speeds, 0.0) * upwind + jnp.maximum(-speeds, 0.0) * downwind
    )


def dot(a, b):
    return jnp.dot(a, b, precision=HIGHEST, preferred_element_type=jnp.float32)


def tdot(a, b):
    return jnp.dot(a, b, precision=lax.Precision.HIGH, preferred_element_type=jnp.float32)


def lanes(parts):
    return jnp.concatenate(parts, axis=1)


def unlanes(wide, width):
    return [wide[:, i * width:(i + 1) * width] for i in range(wide.shape[1] // width)]


def tendency_into(out_ref, v_ref, prev_ref, next_ref, lop_ref, xt_ref, zc_ref, rx_ref,
                  rate_ref, en_ref, s_ref):
    states, fields, span, columns = v_ref.shape
    rows = prev_ref.shape[2]

    def field_body(f, carry):
        parts = [v_ref[b, f] for b in range(states)]
        left = unlanes(tdot(lop_ref[f], lanes(parts)), columns)
        right = tdot(jnp.concatenate(parts, axis=0), xt_ref[f])
        for b in range(states):
            out_ref[b, f] = left[b] + right[b * span:(b + 1) * span]
            out_ref[b, f, pl.ds(0, rows), :] = (
                out_ref[b, f, pl.ds(0, rows), :] + zc_ref[0, f] * prev_ref[b, f]
            )
            out_ref[b, f, pl.ds(span - rows, rows), :] = (
                out_ref[b, f, pl.ds(span - rows, rows), :] + zc_ref[1, f] * next_ref[b, f]
            )
            s_ref[b, f] = jnp.tanh(parts[b])
        return carry

    lax.fori_loop(0, fields, field_body, 0)
    for b in range(states):
        cooling = 1.0 / (1.5 + 0.5 * s_ref[b, fields - 1])

        def reaction_body(r, carry):
            first = rx_ref[r, 0]
            second = rx_ref[r, 1]
            product = rx_ref[r, 2]
            progress = (
                rate_ref[r] * jnp.exp(-en_ref[r] * cooling) * s_ref[b, first] * s_ref[b, second]
            )
            out_ref[b, product] = out_ref[b, product] + progress
            out_ref[b, first] = out_ref[b, first] - progress
            out_ref[b, second] = out_ref[b, second] - progress
            return carry

        lax.fori_loop(0, rx_ref.shape[0], reaction_body, 0)


def vmem():
    return pl.BlockSpec(memory_space=pltpu.VMEM)


def smem():
    return pl.BlockSpec(memory_space=pltpu.SMEM)


def tendency_cost(states, fields, span, columns, reactions):
    flops = states * fields * (2 * span * span * columns + 2 * span * columns * columns) * 6
    flops += states * span * columns * (8 * reactions + 4 * fields)
    trans = states * span * columns * (fields + 2 * reactions)
    return flops, trans


def call(kernel, ins, in_kinds, outs, scratch, flops, trans):
    nbytes = sum(int(np.prod(x.shape)) * 4 for x in ins) + sum(
        int(np.prod(o.shape)) * 4 for o in outs
    )
    return pl.pallas_call(
        kernel,
        out_shape=outs,
        in_specs=[smem() if k else vmem() for k in in_kinds],
        out_specs=tuple(vmem() for _ in outs),
        scratch_shapes=scratch,
        cost_estimate=pl.CostEstimate(
            flops=int(flops), transcendentals=int(trans), bytes_accessed=int(nbytes)
        ),
    )(*ins)


def per_device(u_start, guess, velocity, rates, energies, reactions):
    fields, depth, rows, columns = u_start.shape
    coarse_rows = rows // 2
    span = depth * rows
    coarse_span = depth * coarse_rows
    reaction_count = rates.shape[0]
    fine_table = derivative_table(FINE_NODES)
    coarse_table = derivative_table(COARSE_NODES)
    x_tables = element_tables(columns, fine_table, 28.0)
    xt = speed_combination(velocity[0], [t.T for t in x_tables])
    y_fine_tables = element_tables(rows, fine_table, 28.0)
    y_coarse_tables = element_tables(coarse_rows, coarse_table, 6.0)
    z_tables = padded_tables(depth, fine_table, 28.0)
    z_local = [t[:, 1:-1] for t in z_tables]
    z_mats = field_operators(velocity[2], z_tables)
    zc = jnp.stack([z_mats[:, 0, 0], z_mats[:, depth - 1, depth + 1]])

    def plane_operator(y_tables, plane_rows):
        along_y = speed_combination(
            velocity[1], [np.kron(np.eye(depth), t) for t in y_tables]
        )
        along_z = speed_combination(
            velocity[2], [np.kron(t, np.eye(plane_rows)) for t in z_local]
        )
        return along_y + along_z

    lop_fine = plane_operator(y_fine_tables, rows)
    lop_coarse = plane_operator(y_coarse_tables, coarse_rows)
    restrict_rows = np.kron(np.eye(rows // 8), lagrange_table(FINE_NODES, COARSE_NODES))
    prolong_rows = np.kron(np.eye(rows // 8), lagrange_table(COARSE_NODES, FINE_NODES))
    rmat = jnp.asarray(np.kron(np.eye(depth), restrict_rows), jnp.float32)
    pmat = jnp.asarray(np.kron(np.eye(depth), prolong_rows), jnp.float32)
    restrict_plane = jnp.asarray(restrict_rows, jnp.float32)
    scalars = (zc, reactions.astype(jnp.int32), rates, energies)
    scalar_kinds = (True, True, True, True)

    space_n = lax.axis_size("space")
    sections = lax.axis_size("tm")
    section = lax.axis_index("tm")
    lead = (section == 0).astype(jnp.int32).reshape(1)

    def halo(x, plane_rows):
        head = x[..., :plane_rows, :]
        tail = x[..., x.shape[-2] - plane_rows:, :]
        prev = lax.ppermute(tail, "space", [(i, (i + 1) % space_n) for i in range(space_n)])
        nxt = lax.ppermute(head, "space", [((i + 1) % space_n, i) for i in range(space_n)])
        return prev, nxt

    f32 = jnp.float32
    fine_state = jax.ShapeDtypeStruct((1, fields, span, columns), f32)
    coarse_state = jax.ShapeDtypeStruct((fields, coarse_span, columns), f32)

    def nodes_kernel(u_ref, p_ref, n_ref, l_ref, x_ref, zc_ref, rx_ref, ra_ref, en_ref,
                     f_ref, a1_ref, s_ref):
        tendency_into(f_ref, u_ref, p_ref, n_ref, l_ref, x_ref, zc_ref, rx_ref, ra_ref, en_ref,
                      s_ref)

        def body(f, carry):
            a1_ref[0, f] = u_ref[0, f] + STEP * (
                5.0 * f_ref[0, f] + 8.0 * f_ref[1, f] - f_ref[2, f]
            ) / 24.0
            return carry

        lax.fori_loop(0, fields, body, 0)

    def middle_kernel(a1_ref, p_ref, n_ref, l_ref, x_ref, zc_ref, rx_ref, ra_ref, en_ref,
                      f_ref, g1_ref, a2_ref, s_ref):
        tendency_into(g1_ref, a1_ref, p_ref, n_ref, l_ref, x_ref, zc_ref, rx_ref, ra_ref,
                      en_ref, s_ref)

        def body(f, carry):
            a2_ref[0, f] = (
                a1_ref[0, f]
                + 0.5 * STEP * (g1_ref[0, f] - f_ref[1, f])
                + STEP * (-f_ref[0, f] + 8.0 * f_ref[1, f] + 5.0 * f_ref[2, f]) / 24.0
            )
            return carry

        lax.fori_loop(0, fields, body, 0)

    def ending_kernel(a2_ref, p_ref, n_ref, l_ref, x_ref, zc_ref, rx_ref, ra_ref, en_ref,
                      f_ref, g1_ref, u_ref, r_ref, rint_ref, c1_ref, c0_ref, g2_ref, s_ref):
        tendency_into(g2_ref, a2_ref, p_ref, n_ref, l_ref, x_ref, zc_ref, rx_ref, ra_ref,
                      en_ref, s_ref)

        def body(f, carry):
            g2_ref[0, f] = STEP * (f_ref[0, f] + 4.0 * g1_ref[0, f] + g2_ref[0, f]) / 6.0
            return carry

        lax.fori_loop(0, fields, body, 0)
        rm = r_ref[...]
        for dst, src_ref, lead_index in ((rint_ref, g2_ref, 0), (c1_ref, a2_ref, 0), (c0_ref, u_ref, 0)):
            wide = dot(rm, lanes([src_ref[lead_index, f] for f in range(fields)]))
            for f, part in enumerate(unlanes(wide, columns)):
                dst[f] = part

    def base_kernel(c_ref, p_ref, n_ref, r_ref, l_ref, x_ref, zc_ref, rx_ref, ra_ref, en_ref,
                    out_ref, bp_ref, bn_ref, s_ref):
        rm = r_ref[...]
        for dst, src_ref in ((bp_ref, p_ref), (bn_ref, n_ref)):
            wide = dot(rm, lanes([src_ref[0, f] for f in range(fields)]))
            for f, part in enumerate(unlanes(wide, columns)):
                dst[0, f] = part
        tendency_into(out_ref, c_ref, bp_ref, bn_ref, l_ref, x_ref, zc_ref, rx_ref, ra_ref,
                      en_ref, s_ref)

    def chain_kernel(lead_ref, w_ref, p_ref, n_ref, ws_ref, ps_ref, ns_ref, l_ref, x_ref,
                     zc_ref, rx_ref, ra_ref, en_ref, base_ref, rint_ref, out_ref, begin_ref,
                     bp_ref, bn_ref, g_ref, s_ref):
        @pl.when(lead_ref[0] != 0)
        def _():
            begin_ref[...] = ws_ref[...]
            bp_ref[...] = ps_ref[...]
            bn_ref[...] = ns_ref[...]

        @pl.when(lead_ref[0] == 0)
        def _():
            begin_ref[...] = w_ref[...]
            bp_ref[...] = p_ref[...]
            bn_ref[...] = n_ref[...]

        tendency_into(g_ref, begin_ref, bp_ref, bn_ref, l_ref, x_ref, zc_ref, rx_ref, ra_ref,
                      en_ref, s_ref)

        def body(f, carry):
            out_ref[0, f] = begin_ref[0, f] + STEP * (g_ref[0, f] - base_ref[0, f]) + rint_ref[0, f]
            return carry

        lax.fori_loop(0, fields, body, 0)

    def correct_kernel(a1_ref, a2_ref, c0_ref, c1_ref, w0_ref, w1_ref, prev_ref, us_ref,
                       r_ref, pm_ref, lead_ref, out_ref):
        pm = pm_ref[...]
        first_change = [w0_ref[f] - c0_ref[f] for f in range(fields)]
        last_change = [w1_ref[f] - c1_ref[f] for f in range(fields)]
        middle_fix = unlanes(
            dot(pm, lanes([0.5 * (first_change[f] + last_change[f]) for f in range(fields)])),
            columns,
        )
        last_fix = unlanes(dot(pm, lanes(last_change)), columns)
        handed = lanes([prev_ref[0, f] for f in range(fields)])
        handed_fix = unlanes(
            dot(pm, lanes([w0_ref[f] for f in range(fields)]) - dot(r_ref[...], handed)),
            columns,
        )
        for f in range(fields):
            out_ref[1, f] = a1_ref[0, f] + middle_fix[f]
            out_ref[2, f] = a2_ref[0, f] + last_fix[f]
            out_ref[0, f] = jnp.where(
                lead_ref[0] != 0, us_ref[f], prev_ref[0, f] + handed_fix[f]
            )

    def finish_kernel(a2_ref, c1_ref, w1_ref, pm_ref, out_ref):
        fix = unlanes(
            dot(pm_ref[...], lanes([w1_ref[f] - c1_ref[f] for f in range(fields)])), columns
        )
        for f in range(fields):
            out_ref[0, f] = a2_ref[0, f] + fix[f]

    fine_cost = tendency_cost(1, fields, span, columns, reaction_count)
    coarse_cost = tendency_cost(1, fields, coarse_span, columns, reaction_count)

    def fine_scratch(states):
        return pltpu.VMEM((states, fields, span, columns), f32)

    def coarse_scratch(states):
        return pltpu.VMEM((states, fields, coarse_span, columns), f32)

    u_flat = u_start.reshape(fields, span, columns)
    nodes = guess[0].reshape(3, fields, span, columns)
    nodes = jnp.concatenate([jnp.where(section == 0, u_flat, nodes[0])[None], nodes[1:]], axis=0)
    coarse_start = jnp.einsum("cy,fzyx->fzcx", restrict_plane,
                              u_start, precision=HIGHEST).reshape(fields, coarse_span, columns)
    start_halo = halo(coarse_start, coarse_rows)

    coarse_one = jax.ShapeDtypeStruct((1, fields, coarse_span, columns), f32)
    plane_one = jax.ShapeDtypeStruct((1, fields, coarse_rows, columns), f32)

    def coarse_step(flag, w, w_halo, base, rint):
        return call(
            chain_kernel,
            (flag, w, w_halo[0], w_halo[1], coarse_start[None], start_halo[0][None],
             start_halo[1][None], lop_coarse, xt) + scalars + (base, rint),
            (True,) + (False,) * 8 + scalar_kinds + (False, False),
            (coarse_one, coarse_one, plane_one, plane_one),
            [pltpu.VMEM((1, fields, coarse_span, columns), f32), coarse_scratch(1)],
            *coarse_cost,
        )

    tm_n = sections
    both = ("tm", "space")
    hop_pairs = [(d, d + 1) for d in range(tm_n - 1)]
    prev_pairs = [
        (d * space_n + s, (d + 1) * space_n + (s + 1) % space_n)
        for d in range(tm_n - 1) for s in range(space_n)
    ]
    next_pairs = [
        (d * space_n + s, (d + 1) * space_n + (s - 1) % space_n)
        for d in range(tm_n - 1) for s in range(space_n)
    ]
    always = jnp.ones((1,), jnp.int32)

    fine_end = None
    coarse_end = None
    for iteration in range(ITERS):
        node_prev, node_next = halo(nodes, rows)
        f_all, a1 = call(
            nodes_kernel,
            (nodes, node_prev, node_next, lop_fine, xt) + scalars,
            (False,) * 5 + scalar_kinds,
            (jax.ShapeDtypeStruct((3, fields, span, columns), f32), fine_state),
            [fine_scratch(3)],
            fine_cost[0] * 3, fine_cost[1] * 3,
        )
        a1_prev, a1_next = halo(a1, rows)
        g1, a2 = call(
            middle_kernel,
            (a1, a1_prev, a1_next, lop_fine, xt) + scalars + (f_all,),
            (False,) * 5 + scalar_kinds + (False,),
            (fine_state, fine_state),
            [fine_scratch(1)],
            *fine_cost,
        )
        a2_prev, a2_next = halo(a2, rows)
        rint, c1, c0 = call(
            ending_kernel,
            (a2, a2_prev, a2_next, lop_fine, xt) + scalars + (f_all, g1, nodes, rmat),
            (False,) * 5 + scalar_kinds + (False,) * 4,
            (coarse_state, coarse_state, coarse_state),
            [pltpu.VMEM((1, fields, span, columns), f32), fine_scratch(1)],
            *fine_cost,
        )
        (base,) = call(
            base_kernel,
            (c0[None], node_prev, node_next, restrict_plane, lop_coarse, xt) + scalars,
            (False,) * 6 + scalar_kinds,
            (jax.ShapeDtypeStruct((1, fields, coarse_span, columns), f32),),
            [pltpu.VMEM((1, fields, coarse_rows, columns), f32),
             pltpu.VMEM((1, fields, coarse_rows, columns), f32), coarse_scratch(1)],
            *coarse_cost,
        )
        last = iteration + 1 == ITERS
        if not last:
            a2_handed = lax.ppermute(a2, "tm", hop_pairs)
        begin = coarse_start[None]
        begin_halo = (start_halo[0][None], start_halo[1][None])
        flag = always
        for n in range(sections):
            finish, w0, _, _ = coarse_step(flag, begin, begin_halo, base, rint[None])
            if n + 1 < sections:
                begin = lax.ppermute(finish, "tm", hop_pairs)
                tail = finish[:, :, coarse_span - coarse_rows:, :]
                head = finish[:, :, :coarse_rows, :]
                begin_halo = (lax.ppermute(tail, both, prev_pairs),
                              lax.ppermute(head, both, next_pairs))
                flag = lead
        w0 = w0[0]
        w1 = finish[0]
        if last:
            (fine_end,) = call(
                finish_kernel,
                (a2, c1, w1, pmat),
                (False,) * 4,
                (fine_state,),
                [],
                2 * fields * span * coarse_span * columns * 6, 0,
            )
            coarse_end = w1
        else:
            (nodes,) = call(
                correct_kernel,
                (a1, a2, c0, c1, w0, w1, a2_handed, u_flat, rmat, pmat, lead),
                (False,) * 10 + (True,),
                (jax.ShapeDtypeStruct((3, fields, span, columns), f32),),
                [],
                8 * fields * span * coarse_span * columns * 6, 0,
            )
    fine_end = fine_end.reshape(1, fields, depth, rows, columns)
    coarse_end = coarse_end.reshape(1, fields, depth, coarse_rows, columns)
    return (fine_end, coarse_end)


def solution(mesh):
    return jax.shard_map(
        per_device,
        mesh=mesh,
        in_specs=(
            P(None, "space", None, None),
            P("tm", None, None, "space", None, None),
            P(),
            P(),
            P(),
            P(),
        ),
        out_specs=(P("tm", None, "space", None, None), P("tm", None, "space", None, None)),
        check_vma=False,
    )
```

```python
import jax
import jax.numpy as jnp
import numpy as np
from jax import lax
from jax.experimental import pallas as pl
from jax.experimental.pallas import tpu as pltpu
from jax.sharding import PartitionSpec as P

ITERS = 2


STEP = 0.01
HIGHEST = lax.Precision.HIGHEST
FINE_NODES = np.array(
    [
        -1.0,
        -0.8717401485096066,
        -0.5917001814331423,
        -0.2092992179024789,
        0.2092992179024789,
        0.5917001814331423,
        0.8717401485096066,
        1.0,
    ]
)
COARSE_NODES = np.array([-1.0, -0.4472135954999579, 0.4472135954999579, 1.0])


def lagrange_table(source, target):
    table = np.ones((len(target), len(source)))
    for j in range(len(source)):
        for m in range(len(source)):
            if m != j:
                table[:, j] *= (target - source[m]) / (source[j] - source[m])
    return table


def derivative_table(points):
    total = len(points)
    weights = np.array(
        [
            1.0 / np.prod([points[j] - points[m] for m in range(total) if m != j])
            for j in range(total)
        ]
    )
    table = np.zeros((total, total))
    for i in range(total):
        for j in range(total):
            if i != j:
                table[i, j] = weights[j] / weights[i] / (points[i] - points[j])
        table[i, i] = -np.sum(table[i])
    return table


def element_tables(length, table, lift):
    per_element = table.shape[0]
    block = np.kron(np.eye(length // per_element), table)
    position = np.arange(length) % per_element
    identity = np.eye(length)
    before = np.roll(identity, -1, axis=1)
    after = np.roll(identity, 1, axis=1)
    first_mask = np.where(position == 0, 1.0, 0.0)
    last_mask = np.where(position == per_element - 1, 1.0, 0.0)
    upwind = lift * first_mask[:, None] * (before - identity)
    downwind = lift * last_mask[:, None] * (after - identity)
    return (block, upwind, downwind)


def widen(matrix):
    length = matrix.shape[0]
    wider = np.zeros((length, matrix.shape[1] + 2))
    wider[:, 1:-1] = matrix
    return wider


def padded_tables(length, table, lift):
    block, upwind, downwind = element_tables(length, table, lift)
    block_wide = widen(block)
    upwind_wide = widen(upwind)
    downwind_wide = widen(downwind)
    upwind_wide[0, length] = 0.0
    upwind_wide[0, 0] = lift
    downwind_wide[length - 1, 1] = 0.0
    downwind_wide[length - 1, length + 1] = lift
    return (block_wide, upwind_wide, downwind_wide)


def field_operators(speed, tables):
    block = jnp.asarray(tables[0], jnp.float32)
    upwind = jnp.asarray(tables[1], jnp.float32)
    downwind = jnp.asarray(tables[2], jnp.float32)
    speeds = speed[:, None, None]
    return (
        -speeds * block + jnp.maximum(speeds, 0.0) * upwind + jnp.maximum(-speeds, 0.0) * downwind
    )


def speed_combination(speed, tables):
    block = jnp.asarray(tables[0], jnp.float32)[None]
    upwind = jnp.asarray(tables[1], jnp.float32)[None]
    downwind = jnp.asarray(tables[2], jnp.float32)[None]
    speeds = speed[:, None, None]
    return (
        -speeds * block + jnp.maximum(speeds, 0.0) * upwind + jnp.maximum(-speeds, 0.0) * downwind
    )


def dot(a, b):
    return jnp.dot(a, b, precision=HIGHEST, preferred_element_type=jnp.float32)


def tdot(a, b):
    return jnp.dot(a, b, precision=lax.Precision.HIGH, preferred_element_type=jnp.float32)


def lanes(parts):
    return jnp.concatenate(parts, axis=1)


def unlanes(wide, width):
    return [wide[:, i * width:(i + 1) * width] for i in range(wide.shape[1] // width)]


def tendency_into(out_ref, v_ref, prev_ref, next_ref, lop_ref, xt_ref, zc_ref, rx_ref,
                  rate_ref, en_ref, s_ref):
    states, fields, span, columns = v_ref.shape
    rows = prev_ref.shape[2]

    def field_body(f, carry):
        parts = [v_ref[b, f] for b in range(states)]
        left = unlanes(tdot(lop_ref[f], lanes(parts)), columns)
        right = tdot(jnp.concatenate(parts, axis=0), xt_ref[f])
        for b in range(states):
            out_ref[b, f] = left[b] + right[b * span:(b + 1) * span]
            out_ref[b, f, pl.ds(0, rows), :] = (
                out_ref[b, f, pl.ds(0, rows), :] + zc_ref[0, f] * prev_ref[b, f]
            )
            out_ref[b, f, pl.ds(span - rows, rows), :] = (
                out_ref[b, f, pl.ds(span - rows, rows), :] + zc_ref[1, f] * next_ref[b, f]
            )
            s_ref[b, f] = jnp.tanh(parts[b])
        return carry

    lax.fori_loop(0, fields, field_body, 0)
    for b in range(states):
        cooling = 1.0 / (1.5 + 0.5 * s_ref[b, fields - 1])

        def reaction_body(r, carry):
            first = rx_ref[r, 0]
            second = rx_ref[r, 1]
            product = rx_ref[r, 2]
            progress = (
                rate_ref[r] * jnp.exp(-en_ref[r] * cooling) * s_ref[b, first] * s_ref[b, second]
            )
            out_ref[b, product] = out_ref[b, product] + progress
            out_ref[b, first] = out_ref[b, first] - progress
            out_ref[b, second] = out_ref[b, second] - progress
            return carry

        lax.fori_loop(0, rx_ref.shape[0], reaction_body, 0)


def vmem():
    return pl.BlockSpec(memory_space=pltpu.VMEM)


def smem():
    return pl.BlockSpec(memory_space=pltpu.SMEM)


def tendency_cost(states, fields, span, columns, reactions):
    flops = states * fields * (2 * span * span * columns + 2 * span * columns * columns) * 6
    flops += states * span * columns * (8 * reactions + 4 * fields)
    trans = states * span * columns * (fields + 2 * reactions)
    return flops, trans


def call(kernel, ins, in_kinds, outs, scratch, flops, trans):
    nbytes = sum(int(np.prod(x.shape)) * 4 for x in ins) + sum(
        int(np.prod(o.shape)) * 4 for o in outs
    )
    return pl.pallas_call(
        kernel,
        out_shape=outs,
        in_specs=[smem() if k else vmem() for k in in_kinds],
        out_specs=tuple(vmem() for _ in outs),
        scratch_shapes=scratch,
        cost_estimate=pl.CostEstimate(
            flops=int(flops), transcendentals=int(trans), bytes_accessed=int(nbytes)
        ),
    )(*ins)


def per_device(u_start, guess, velocity, rates, energies, reactions):
    fields, depth, rows, columns = u_start.shape
    coarse_rows = rows // 2
    span = depth * rows
    coarse_span = depth * coarse_rows
    reaction_count = rates.shape[0]
    fine_table = derivative_table(FINE_NODES)
    coarse_table = derivative_table(COARSE_NODES)
    x_tables = element_tables(columns, fine_table, 28.0)
    xt = speed_combination(velocity[0], [t.T for t in x_tables])
    y_fine_tables = element_tables(rows, fine_table, 28.0)
    y_coarse_tables = element_tables(coarse_rows, coarse_table, 6.0)
    z_tables = padded_tables(depth, fine_table, 28.0)
    z_local = [t[:, 1:-1] for t in z_tables]
    z_mats = field_operators(velocity[2], z_tables)
    zc = jnp.stack([z_mats[:, 0, 0], z_mats[:, depth - 1, depth + 1]])

    def plane_operator(y_tables, plane_rows):
        along_y = speed_combination(
            velocity[1], [np.kron(np.eye(depth), t) for t in y_tables]
        )
        along_z = speed_combination(
            velocity[2], [np.kron(t, np.eye(plane_rows)) for t in z_local]
        )
        return along_y + along_z

    lop_fine = plane_operator(y_fine_tables, rows)
    lop_coarse = plane_operator(y_coarse_tables, coarse_rows)
    restrict_rows = np.kron(np.eye(rows // 8), lagrange_table(FINE_NODES, COARSE_NODES))
    prolong_rows = np.kron(np.eye(rows // 8), lagrange_table(COARSE_NODES, FINE_NODES))
    rmat = jnp.asarray(np.kron(np.eye(depth), restrict_rows), jnp.float32)
    pmat = jnp.asarray(np.kron(np.eye(depth), prolong_rows), jnp.float32)
    restrict_plane = jnp.asarray(restrict_rows, jnp.float32)
    scalars = (zc, reactions.astype(jnp.int32), rates, energies)
    scalar_kinds = (True, True, True, True)

    space_n = lax.axis_size("space")
    sections = lax.axis_size("tm")
    section = lax.axis_index("tm")
    lead = (section == 0).astype(jnp.int32).reshape(1)

    def halo(x, plane_rows):
        head = x[..., :plane_rows, :]
        tail = x[..., x.shape[-2] - plane_rows:, :]
        return swap(head, tail)

    def swap(head, tail):
        prev = lax.ppermute(tail, "space", [(i, (i + 1) % space_n) for i in range(space_n)])
        nxt = lax.ppermute(head, "space", [((i + 1) % space_n, i) for i in range(space_n)])
        return prev, nxt

    f32 = jnp.float32
    fine_state = jax.ShapeDtypeStruct((1, fields, span, columns), f32)
    coarse_state = jax.ShapeDtypeStruct((fields, coarse_span, columns), f32)

    def nodes_kernel(u_ref, p_ref, n_ref, l_ref, x_ref, zc_ref, rx_ref, ra_ref, en_ref,
                     f_ref, a1_ref, h_ref, t_ref, s_ref):
        tendency_into(f_ref, u_ref, p_ref, n_ref, l_ref, x_ref, zc_ref, rx_ref, ra_ref, en_ref,
                      s_ref)

        def body(f, carry):
            value = u_ref[0, f] + STEP * (
                5.0 * f_ref[0, f] + 8.0 * f_ref[1, f] - f_ref[2, f]
            ) / 24.0
            a1_ref[0, f] = value
            h_ref[0, f] = value[:rows]
            t_ref[0, f] = value[span - rows:]
            return carry

        lax.fori_loop(0, fields, body, 0)

    def middle_kernel(a1_ref, p_ref, n_ref, l_ref, x_ref, zc_ref, rx_ref, ra_ref, en_ref,
                      f_ref, g1_ref, a2_ref, h_ref, t_ref, s_ref):
        tendency_into(g1_ref, a1_ref, p_ref, n_ref, l_ref, x_ref, zc_ref, rx_ref, ra_ref,
                      en_ref, s_ref)

        def body(f, carry):
            value = (
                a1_ref[0, f]
                + 0.5 * STEP * (g1_ref[0, f] - f_ref[1, f])
                + STEP * (-f_ref[0, f] + 8.0 * f_ref[1, f] + 5.0 * f_ref[2, f]) / 24.0
            )
            a2_ref[0, f] = value
            h_ref[0, f] = value[:rows]
            t_ref[0, f] = value[span - rows:]
            return carry

        lax.fori_loop(0, fields, body, 0)

    def ending_kernel(a2_ref, p_ref, n_ref, l_ref, x_ref, zc_ref, rx_ref, ra_ref, en_ref,
                      f_ref, g1_ref, u_ref, r_ref, rint_ref, c1_ref, c0_ref, g2_ref, s_ref):
        tendency_into(g2_ref, a2_ref, p_ref, n_ref, l_ref, x_ref, zc_ref, rx_ref, ra_ref,
                      en_ref, s_ref)

        def body(f, carry):
            g2_ref[0, f] = STEP * (f_ref[0, f] + 4.0 * g1_ref[0, f] + g2_ref[0, f]) / 6.0
            return carry

        lax.fori_loop(0, fields, body, 0)
        rm = r_ref[...]
        for dst, src_ref, lead_index in ((rint_ref, g2_ref, 0), (c1_ref, a2_ref, 0), (c0_ref, u_ref, 0)):
            wide = dot(rm, lanes([src_ref[lead_index, f] for f in range(fields)]))
            for f, part in enumerate(unlanes(wide, columns)):
                dst[f] = part

    def base_kernel(c_ref, p_ref, n_ref, r_ref, l_ref, x_ref, zc_ref, rx_ref, ra_ref, en_ref,
                    out_ref, bp_ref, bn_ref, s_ref):
        rm = r_ref[...]
        for dst, src_ref in ((bp_ref, p_ref), (bn_ref, n_ref)):
            wide = dot(rm, lanes([src_ref[0, f] for f in range(fields)]))
            for f, part in enumerate(unlanes(wide, columns)):
                dst[0, f] = part
        tendency_into(out_ref, c_ref, bp_ref, bn_ref, l_ref, x_ref, zc_ref, rx_ref, ra_ref,
                      en_ref, s_ref)

    def chain_kernel(lead_ref, w_ref, p_ref, n_ref, ws_ref, ps_ref, ns_ref, l_ref, x_ref,
                     zc_ref, rx_ref, ra_ref, en_ref, base_ref, rint_ref, out_ref, begin_ref,
                     bp_ref, bn_ref, h_ref, t_ref, g_ref, s_ref):
        @pl.when(lead_ref[0] != 0)
        def _():
            begin_ref[...] = ws_ref[...]
            bp_ref[...] = ps_ref[...]
            bn_ref[...] = ns_ref[...]

        @pl.when(lead_ref[0] == 0)
        def _():
            begin_ref[...] = w_ref[...]
            bp_ref[...] = p_ref[...]
            bn_ref[...] = n_ref[...]

        tendency_into(g_ref, begin_ref, bp_ref, bn_ref, l_ref, x_ref, zc_ref, rx_ref, ra_ref,
                      en_ref, s_ref)

        def body(f, carry):
            value = begin_ref[0, f] + STEP * (g_ref[0, f] - base_ref[0, f]) + rint_ref[0, f]
            out_ref[0, f] = value
            h_ref[0, f] = value[:coarse_rows]
            t_ref[0, f] = value[coarse_span - coarse_rows:]
            return carry

        lax.fori_loop(0, fields, body, 0)

    def correct_kernel(a1_ref, a2_ref, c0_ref, c1_ref, w0_ref, w1_ref, prev_ref, us_ref,
                       r_ref, pm_ref, lead_ref, out_ref, h_ref, t_ref):
        pm = pm_ref[...]
        first_change = [w0_ref[f] - c0_ref[f] for f in range(fields)]
        last_change = [w1_ref[f] - c1_ref[f] for f in range(fields)]
        middle_fix = unlanes(
            dot(pm, lanes([0.5 * (first_change[f] + last_change[f]) for f in range(fields)])),
            columns,
        )
        last_fix = unlanes(dot(pm, lanes(last_change)), columns)
        handed = lanes([prev_ref[0, f] for f in range(fields)])
        handed_fix = unlanes(
            dot(pm, lanes([w0_ref[f] for f in range(fields)]) - dot(r_ref[...], handed)),
            columns,
        )
        for f in range(fields):
            values = (
                jnp.where(lead_ref[0] != 0, us_ref[f], prev_ref[0, f] + handed_fix[f]),
                a1_ref[0, f] + middle_fix[f],
                a2_ref[0, f] + last_fix[f],
            )
            for b, value in enumerate(values):
                out_ref[b, f] = value
                h_ref[b, f] = value[:rows]
                t_ref[b, f] = value[span - rows:]

    def finish_kernel(a2_ref, c1_ref, w1_ref, pm_ref, out_ref):
        fix = unlanes(
            dot(pm_ref[...], lanes([w1_ref[f] - c1_ref[f] for f in range(fields)])), columns
        )
        for f in range(fields):
            out_ref[0, f] = a2_ref[0, f] + fix[f]

    fine_cost = tendency_cost(1, fields, span, columns, reaction_count)
    coarse_cost = tendency_cost(1, fields, coarse_span, columns, reaction_count)

    def fine_scratch(states):
        return pltpu.VMEM((states, fields, span, columns), f32)

    def coarse_scratch(states):
        return pltpu.VMEM((states, fields, coarse_span, columns), f32)

    u_flat = u_start.reshape(fields, span, columns)
    nodes = guess[0].reshape(3, fields, span, columns)
    nodes = jnp.concatenate([jnp.where(section == 0, u_flat, nodes[0])[None], nodes[1:]], axis=0)
    coarse_start = jnp.einsum("cy,fzyx->fzcx", restrict_plane,
                              u_start, precision=HIGHEST).reshape(fields, coarse_span, columns)
    start_halo = halo(coarse_start, coarse_rows)

    coarse_one = jax.ShapeDtypeStruct((1, fields, coarse_span, columns), f32)
    plane_one = jax.ShapeDtypeStruct((1, fields, coarse_rows, columns), f32)
    fine_plane = jax.ShapeDtypeStruct((1, fields, rows, columns), f32)
    node_planes = jax.ShapeDtypeStruct((3, fields, rows, columns), f32)

    def coarse_step(flag, w, w_halo, base, rint):
        return call(
            chain_kernel,
            (flag, w, w_halo[0], w_halo[1], coarse_start[None], start_halo[0][None],
             start_halo[1][None], lop_coarse, xt) + scalars + (base, rint),
            (True,) + (False,) * 8 + scalar_kinds + (False, False),
            (coarse_one, coarse_one, plane_one, plane_one, plane_one, plane_one),
            [pltpu.VMEM((1, fields, coarse_span, columns), f32), coarse_scratch(1)],
            *coarse_cost,
        )

    tm_n = sections
    both = ("tm", "space")
    hop_pairs = [(d, d + 1) for d in range(tm_n - 1)]
    prev_pairs = [
        (d * space_n + s, (d + 1) * space_n + (s + 1) % space_n)
        for d in range(tm_n - 1) for s in range(space_n)
    ]
    next_pairs = [
        (d * space_n + s, (d + 1) * space_n + (s - 1) % space_n)
        for d in range(tm_n - 1) for s in range(space_n)
    ]
    always = jnp.ones((1,), jnp.int32)

    fine_end = None
    coarse_end = None
    for iteration in range(ITERS):
        if iteration == 0:
            node_prev, node_next = halo(nodes, rows)
        else:
            node_prev, node_next = swap(node_head, node_tail)
        f_all, a1, a1_head, a1_tail = call(
            nodes_kernel,
            (nodes, node_prev, node_next, lop_fine, xt) + scalars,
            (False,) * 5 + scalar_kinds,
            (jax.ShapeDtypeStruct((3, fields, span, columns), f32), fine_state, fine_plane,
             fine_plane),
            [fine_scratch(3)],
            fine_cost[0] * 3, fine_cost[1] * 3,
        )
        a1_prev, a1_next = swap(a1_head, a1_tail)
        g1, a2, a2_head, a2_tail = call(
            middle_kernel,
            (a1, a1_prev, a1_next, lop_fine, xt) + scalars + (f_all,),
            (False,) * 5 + scalar_kinds + (False,),
            (fine_state, fine_state, fine_plane, fine_plane),
            [fine_scratch(1)],
            *fine_cost,
        )
        a2_prev, a2_next = swap(a2_head, a2_tail)
        rint, c1, c0 = call(
            ending_kernel,
            (a2, a2_prev, a2_next, lop_fine, xt) + scalars + (f_all, g1, nodes, rmat),
            (False,) * 5 + scalar_kinds + (False,) * 4,
            (coarse_state, coarse_state, coarse_state),
            [pltpu.VMEM((1, fields, span, columns), f32), fine_scratch(1)],
            *fine_cost,
        )
        (base,) = call(
            base_kernel,
            (c0[None], node_prev, node_next, restrict_plane, lop_coarse, xt) + scalars,
            (False,) * 6 + scalar_kinds,
            (jax.ShapeDtypeStruct((1, fields, coarse_span, columns), f32),),
            [pltpu.VMEM((1, fields, coarse_rows, columns), f32),
             pltpu.VMEM((1, fields, coarse_rows, columns), f32), coarse_scratch(1)],
            *coarse_cost,
        )
        last = iteration + 1 == ITERS
        if not last:
            a2_handed = lax.ppermute(a2, "tm", hop_pairs)
        begin = coarse_start[None]
        begin_halo = (start_halo[0][None], start_halo[1][None])
        flag = always
        for n in range(sections):
            finish, w0, _, _, head, tail = coarse_step(flag, begin, begin_halo, base, rint[None])
            if n + 1 < sections:
                begin = lax.ppermute(finish, "tm", hop_pairs)
                begin_halo = (lax.ppermute(tail, both, prev_pairs),
                              lax.ppermute(head, both, next_pairs))
                flag = lead
        w0 = w0[0]
        w1 = finish[0]
        if last:
            (fine_end,) = call(
                finish_kernel,
                (a2, c1, w1, pmat),
                (False,) * 4,
                (fine_state,),
                [],
                2 * fields * span * coarse_span * columns * 6, 0,
            )
            coarse_end = w1
        else:
            nodes, node_head, node_tail = call(
                correct_kernel,
                (a1, a2, c0, c1, w0, w1, a2_handed, u_flat, rmat, pmat, lead),
                (False,) * 10 + (True,),
                (jax.ShapeDtypeStruct((3, fields, span, columns), f32), node_planes,
                 node_planes),
                [],
                8 * fields * span * coarse_span * columns * 6, 0,
            )
    fine_end = fine_end.reshape(1, fields, depth, rows, columns)
    coarse_end = coarse_end.reshape(1, fields, depth, coarse_rows, columns)
    return (fine_end, coarse_end)


def solution(mesh):
    return jax.shard_map(
        per_device,
        mesh=mesh,
        in_specs=(
            P(None, "space", None, None),
            P("tm", None, None, "space", None, None),
            P(),
            P(),
            P(),
            P(),
        ),
        out_specs=(P("tm", None, "space", None, None), P("tm", None, "space", None, None)),
        check_vma=False,
    )
```

```python
import jax
import jax.numpy as jnp
import numpy as np
from jax import lax
from jax.experimental import pallas as pl
from jax.experimental.pallas import tpu as pltpu
from jax.sharding import PartitionSpec as P

ITERS = 2


STEP = 0.01
HIGHEST = lax.Precision.HIGHEST
FINE_NODES = np.array(
    [
        -1.0,
        -0.8717401485096066,
        -0.5917001814331423,
        -0.2092992179024789,
        0.2092992179024789,
        0.5917001814331423,
        0.8717401485096066,
        1.0,
    ]
)
COARSE_NODES = np.array([-1.0, -0.4472135954999579, 0.4472135954999579, 1.0])


def lagrange_table(source, target):
    table = np.ones((len(target), len(source)))
    for j in range(len(source)):
        for m in range(len(source)):
            if m != j:
                table[:, j] *= (target - source[m]) / (source[j] - source[m])
    return table


def derivative_table(points):
    total = len(points)
    weights = np.array(
        [
            1.0 / np.prod([points[j] - points[m] for m in range(total) if m != j])
            for j in range(total)
        ]
    )
    table = np.zeros((total, total))
    for i in range(total):
        for j in range(total):
            if i != j:
                table[i, j] = weights[j] / weights[i] / (points[i] - points[j])
        table[i, i] = -np.sum(table[i])
    return table


def element_tables(length, table, lift):
    per_element = table.shape[0]
    block = np.kron(np.eye(length // per_element), table)
    position = np.arange(length) % per_element
    identity = np.eye(length)
    before = np.roll(identity, -1, axis=1)
    after = np.roll(identity, 1, axis=1)
    first_mask = np.where(position == 0, 1.0, 0.0)
    last_mask = np.where(position == per_element - 1, 1.0, 0.0)
    upwind = lift * first_mask[:, None] * (before - identity)
    downwind = lift * last_mask[:, None] * (after - identity)
    return (block, upwind, downwind)


def widen(matrix):
    length = matrix.shape[0]
    wider = np.zeros((length, matrix.shape[1] + 2))
    wider[:, 1:-1] = matrix
    return wider


def padded_tables(length, table, lift):
    block, upwind, downwind = element_tables(length, table, lift)
    block_wide = widen(block)
    upwind_wide = widen(upwind)
    downwind_wide = widen(downwind)
    upwind_wide[0, length] = 0.0
    upwind_wide[0, 0] = lift
    downwind_wide[length - 1, 1] = 0.0
    downwind_wide[length - 1, length + 1] = lift
    return (block_wide, upwind_wide, downwind_wide)


def field_operators(speed, tables):
    block = jnp.asarray(tables[0], jnp.float32)
    upwind = jnp.asarray(tables[1], jnp.float32)
    downwind = jnp.asarray(tables[2], jnp.float32)
    speeds = speed[:, None, None]
    return (
        -speeds * block + jnp.maximum(speeds, 0.0) * upwind + jnp.maximum(-speeds, 0.0) * downwind
    )


def speed_combination(speed, tables):
    block = jnp.asarray(tables[0], jnp.float32)[None]
    upwind = jnp.asarray(tables[1], jnp.float32)[None]
    downwind = jnp.asarray(tables[2], jnp.float32)[None]
    speeds = speed[:, None, None]
    return (
        -speeds * block + jnp.maximum(speeds, 0.0) * upwind + jnp.maximum(-speeds, 0.0) * downwind
    )


def dot(a, b):
    return jnp.dot(a, b, precision=HIGHEST, preferred_element_type=jnp.float32)


def tdot(a, b):
    return jnp.dot(a, b, precision=lax.Precision.HIGH, preferred_element_type=jnp.float32)


def lanes(parts):
    return jnp.concatenate(parts, axis=1)


def unlanes(wide, width):
    return [wide[:, i * width:(i + 1) * width] for i in range(wide.shape[1] // width)]


def tendency_into(out_ref, v_ref, prev_ref, next_ref, k_ref, d_ref, cf_ref, rx_ref,
                  rate_ref, en_ref, s_ref, y_elem):
    states, fields, span, columns = v_ref.shape
    rows = prev_ref.shape[2]
    planes = span // rows
    f32 = jnp.float32
    row = lax.broadcasted_iota(jnp.int32, (span, columns), 0)
    lane = lax.broadcasted_iota(jnp.int32, (span, columns), 1)
    yy = row % rows
    zz = row // rows
    x_first = lane % 8 == 0
    x_last = lane % 8 == 7
    y_first = yy % y_elem == 0
    y_last = yy % y_elem == y_elem - 1
    z_first = zz % 8 == 0
    z_last = zz % 8 == 7

    def scoped(xd_ref, yz_ref):
        for b in range(states):
            xd_ref[b] = tdot(v_ref[b].reshape(fields * span, columns), d_ref[...]).reshape(
                fields, span, columns)
            yz_ref[b] = tdot(k_ref[...], lanes([v_ref[b, f] for f in range(fields)]))
        for b in range(states):
            for f in range(fields):
                v = v_ref[b, f]
                cols = slice(f * columns, (f + 1) * columns)
                t = (cf_ref[0, f] * xd_ref[b, f] + cf_ref[1, f] * yz_ref[b, :span, cols]
                     + cf_ref[2, f] * yz_ref[b, span:, cols])
                before_x = pltpu.roll(v, 1, 1)
                after_x = pltpu.roll(v, columns - 1, 1)
                t = t + jnp.where(x_first, cf_ref[3, f] * (before_x - v), 0.0)
                t = t + jnp.where(x_last, cf_ref[4, f] * (after_x - v), 0.0)
                before_y = jnp.where(yy == 0, pltpu.roll(v, span - rows + 1, 0),
                                     pltpu.roll(v, 1, 0))
                after_y = jnp.where(yy == rows - 1, pltpu.roll(v, rows - 1, 0),
                                    pltpu.roll(v, span - 1, 0))
                t = t + jnp.where(y_first, cf_ref[5, f] * (before_y - v), 0.0)
                t = t + jnp.where(y_last, cf_ref[6, f] * (after_y - v), 0.0)
                if planes > 8:
                    before_z = pltpu.roll(v, rows, 0)
                    after_z = pltpu.roll(v, span - rows, 0)
                    t = t + jnp.where(z_first & (zz > 0), cf_ref[7, f] * before_z, 0.0)
                    t = t + jnp.where(z_last & (zz < planes - 1), cf_ref[8, f] * after_z, 0.0)
                t = t - jnp.where(z_first, cf_ref[7, f] * v, 0.0)
                t = t - jnp.where(z_last, cf_ref[8, f] * v, 0.0)
                out_ref[b, f] = t
                out_ref[b, f, pl.ds(0, rows), :] = (
                    out_ref[b, f, pl.ds(0, rows), :] + cf_ref[7, f] * prev_ref[b, f]
                )
                out_ref[b, f, pl.ds(span - rows, rows), :] = (
                    out_ref[b, f, pl.ds(span - rows, rows), :] + cf_ref[8, f] * next_ref[b, f]
                )
                s_ref[b, f] = jnp.tanh(v)

    pl.run_scoped(scoped, pltpu.VMEM((states, fields, span, columns), f32),
                  pltpu.VMEM((states, 2 * span, fields * columns), f32))
    for b in range(states):
        cooling = 1.0 / (1.5 + 0.5 * s_ref[b, fields - 1])

        def reaction_body(r, carry):
            first = rx_ref[r, 0]
            second = rx_ref[r, 1]
            product = rx_ref[r, 2]
            progress = (
                rate_ref[r] * jnp.exp(-en_ref[r] * cooling) * s_ref[b, first] * s_ref[b, second]
            )
            out_ref[b, product] = out_ref[b, product] + progress
            out_ref[b, first] = out_ref[b, first] - progress
            out_ref[b, second] = out_ref[b, second] - progress
            return carry

        lax.fori_loop(0, rx_ref.shape[0], reaction_body, 0)


def vmem():
    return pl.BlockSpec(memory_space=pltpu.VMEM)


def smem():
    return pl.BlockSpec(memory_space=pltpu.SMEM)


def tendency_cost(states, fields, span, columns, reactions):
    flops = states * fields * (2 * span * span * columns + 2 * span * columns * columns) * 6
    flops += states * span * columns * (8 * reactions + 4 * fields)
    trans = states * span * columns * (fields + 2 * reactions)
    return flops, trans


def call(kernel, ins, in_kinds, outs, scratch, flops, trans):
    nbytes = sum(int(np.prod(x.shape)) * 4 for x in ins) + sum(
        int(np.prod(o.shape)) * 4 for o in outs
    )
    return pl.pallas_call(
        kernel,
        out_shape=outs,
        in_specs=[smem() if k else vmem() for k in in_kinds],
        out_specs=tuple(vmem() for _ in outs),
        scratch_shapes=scratch,
        cost_estimate=pl.CostEstimate(
            flops=int(flops), transcendentals=int(trans), bytes_accessed=int(nbytes)
        ),
    )(*ins)


def per_device(u_start, guess, velocity, rates, energies, reactions):
    fields, depth, rows, columns = u_start.shape
    coarse_rows = rows // 2
    span = depth * rows
    coarse_span = depth * coarse_rows
    reaction_count = rates.shape[0]
    fine_table = derivative_table(FINE_NODES)
    coarse_table = derivative_table(COARSE_NODES)
    fine_elem = len(FINE_NODES)
    coarse_elem = len(COARSE_NODES)
    xt = jnp.asarray(np.kron(np.eye(columns // fine_elem), fine_table).T, jnp.float32)
    z_block = np.kron(np.eye(depth // fine_elem), fine_table)

    def plane_operator(y_table, plane_rows):
        y_block = np.kron(np.eye(plane_rows // y_table.shape[0]), y_table)
        return jnp.asarray(
            np.concatenate([np.kron(np.eye(depth), y_block), np.kron(z_block, np.eye(plane_rows))]),
            jnp.float32,
        )

    lop_fine = plane_operator(fine_table, rows)
    lop_coarse = plane_operator(coarse_table, coarse_rows)

    def coefficients(y_lift):
        up = jnp.maximum(velocity, 0.0)
        down = jnp.maximum(-velocity, 0.0)
        return jnp.concatenate([
            -velocity,
            28.0 * up[0:1], 28.0 * down[0:1],
            y_lift * up[1:2], y_lift * down[1:2],
            28.0 * up[2:3], 28.0 * down[2:3],
        ])

    cf_fine = coefficients(28.0)
    cf_coarse = coefficients(6.0)
    restrict_rows = np.kron(np.eye(rows // 8), lagrange_table(FINE_NODES, COARSE_NODES))
    prolong_rows = np.kron(np.eye(rows // 8), lagrange_table(COARSE_NODES, FINE_NODES))
    rmat = jnp.asarray(np.kron(np.eye(depth), restrict_rows), jnp.float32)
    pmat = jnp.asarray(np.kron(np.eye(depth), prolong_rows), jnp.float32)
    restrict_plane = jnp.asarray(restrict_rows, jnp.float32)
    scalars = (cf_fine, reactions.astype(jnp.int32), rates, energies)
    coarse_scalars = (cf_coarse, reactions.astype(jnp.int32), rates, energies)
    scalar_kinds = (True, True, True, True)

    space_n = lax.axis_size("space")
    sections = lax.axis_size("tm")
    section = lax.axis_index("tm")
    lead = (section == 0).astype(jnp.int32).reshape(1)

    def halo(x, plane_rows):
        head = x[..., :plane_rows, :]
        tail = x[..., x.shape[-2] - plane_rows:, :]
        return swap(head, tail)

    def swap(head, tail):
        prev = lax.ppermute(tail, "space", [(i, (i + 1) % space_n) for i in range(space_n)])
        nxt = lax.ppermute(head, "space", [((i + 1) % space_n, i) for i in range(space_n)])
        return prev, nxt

    f32 = jnp.float32
    fine_state = jax.ShapeDtypeStruct((1, fields, span, columns), f32)
    coarse_state = jax.ShapeDtypeStruct((fields, coarse_span, columns), f32)

    def nodes_kernel(u_ref, p_ref, n_ref, l_ref, x_ref, zc_ref, rx_ref, ra_ref, en_ref,
                     f_ref, a1_ref, h_ref, t_ref, s_ref):
        tendency_into(f_ref, u_ref, p_ref, n_ref, l_ref, x_ref, zc_ref, rx_ref, ra_ref, en_ref,
                      s_ref, fine_elem)

        def body(f, carry):
            value = u_ref[0, f] + STEP * (
                5.0 * f_ref[0, f] + 8.0 * f_ref[1, f] - f_ref[2, f]
            ) / 24.0
            a1_ref[0, f] = value
            h_ref[0, f] = value[:rows]
            t_ref[0, f] = value[span - rows:]
            return carry

        lax.fori_loop(0, fields, body, 0)

    def middle_kernel(a1_ref, p_ref, n_ref, l_ref, x_ref, zc_ref, rx_ref, ra_ref, en_ref,
                      f_ref, g1_ref, a2_ref, h_ref, t_ref, s_ref):
        tendency_into(g1_ref, a1_ref, p_ref, n_ref, l_ref, x_ref, zc_ref, rx_ref, ra_ref,
                      en_ref, s_ref, fine_elem)

        def body(f, carry):
            value = (
                a1_ref[0, f]
                + 0.5 * STEP * (g1_ref[0, f] - f_ref[1, f])
                + STEP * (-f_ref[0, f] + 8.0 * f_ref[1, f] + 5.0 * f_ref[2, f]) / 24.0
            )
            a2_ref[0, f] = value
            h_ref[0, f] = value[:rows]
            t_ref[0, f] = value[span - rows:]
            return carry

        lax.fori_loop(0, fields, body, 0)

    def ending_kernel(a2_ref, p_ref, n_ref, l_ref, x_ref, zc_ref, rx_ref, ra_ref, en_ref,
                      f_ref, g1_ref, u_ref, r_ref, rint_ref, c1_ref, c0_ref, g2_ref, s_ref):
        tendency_into(g2_ref, a2_ref, p_ref, n_ref, l_ref, x_ref, zc_ref, rx_ref, ra_ref,
                      en_ref, s_ref, fine_elem)

        def body(f, carry):
            g2_ref[0, f] = STEP * (f_ref[0, f] + 4.0 * g1_ref[0, f] + g2_ref[0, f]) / 6.0
            return carry

        lax.fori_loop(0, fields, body, 0)
        rm = r_ref[...]
        for dst, src_ref, lead_index in ((rint_ref, g2_ref, 0), (c1_ref, a2_ref, 0), (c0_ref, u_ref, 0)):
            wide = dot(rm, lanes([src_ref[lead_index, f] for f in range(fields)]))
            for f, part in enumerate(unlanes(wide, columns)):
                dst[f] = part

    def base_kernel(c_ref, p_ref, n_ref, r_ref, l_ref, x_ref, zc_ref, rx_ref, ra_ref, en_ref,
                    out_ref, bp_ref, bn_ref, s_ref):
        rm = r_ref[...]
        for dst, src_ref in ((bp_ref, p_ref), (bn_ref, n_ref)):
            wide = dot(rm, lanes([src_ref[0, f] for f in range(fields)]))
            for f, part in enumerate(unlanes(wide, columns)):
                dst[0, f] = part
        tendency_into(out_ref, c_ref, bp_ref, bn_ref, l_ref, x_ref, zc_ref, rx_ref, ra_ref,
                      en_ref, s_ref, coarse_elem)

    def chain_kernel(lead_ref, w_ref, p_ref, n_ref, ws_ref, ps_ref, ns_ref, l_ref, x_ref,
                     zc_ref, rx_ref, ra_ref, en_ref, base_ref, rint_ref, out_ref, begin_ref,
                     bp_ref, bn_ref, h_ref, t_ref, g_ref, s_ref):
        @pl.when(lead_ref[0] != 0)
        def _():
            begin_ref[...] = ws_ref[...]
            bp_ref[...] = ps_ref[...]
            bn_ref[...] = ns_ref[...]

        @pl.when(lead_ref[0] == 0)
        def _():
            begin_ref[...] = w_ref[...]
            bp_ref[...] = p_ref[...]
            bn_ref[...] = n_ref[...]

        tendency_into(g_ref, begin_ref, bp_ref, bn_ref, l_ref, x_ref, zc_ref, rx_ref, ra_ref,
                      en_ref, s_ref, coarse_elem)

        def body(f, carry):
            value = begin_ref[0, f] + STEP * (g_ref[0, f] - base_ref[0, f]) + rint_ref[0, f]
            out_ref[0, f] = value
            h_ref[0, f] = value[:coarse_rows]
            t_ref[0, f] = value[coarse_span - coarse_rows:]
            return carry

        lax.fori_loop(0, fields, body, 0)

    def correct_kernel(a1_ref, a2_ref, c0_ref, c1_ref, w0_ref, w1_ref, prev_ref, us_ref,
                       r_ref, pm_ref, lead_ref, out_ref, h_ref, t_ref):
        pm = pm_ref[...]
        first_change = [w0_ref[f] - c0_ref[f] for f in range(fields)]
        last_change = [w1_ref[f] - c1_ref[f] for f in range(fields)]
        middle_fix = unlanes(
            dot(pm, lanes([0.5 * (first_change[f] + last_change[f]) for f in range(fields)])),
            columns,
        )
        last_fix = unlanes(dot(pm, lanes(last_change)), columns)
        handed = lanes([prev_ref[0, f] for f in range(fields)])
        handed_fix = unlanes(
            dot(pm, lanes([w0_ref[f] for f in range(fields)]) - dot(r_ref[...], handed)),
            columns,
        )
        for f in range(fields):
            values = (
                jnp.where(lead_ref[0] != 0, us_ref[f], prev_ref[0, f] + handed_fix[f]),
                a1_ref[0, f] + middle_fix[f],
                a2_ref[0, f] + last_fix[f],
            )
            for b, value in enumerate(values):
                out_ref[b, f] = value
                h_ref[b, f] = value[:rows]
                t_ref[b, f] = value[span - rows:]

    def finish_kernel(a2_ref, c1_ref, w1_ref, pm_ref, out_ref):
        fix = unlanes(
            dot(pm_ref[...], lanes([w1_ref[f] - c1_ref[f] for f in range(fields)])), columns
        )
        for f in range(fields):
            out_ref[0, f] = a2_ref[0, f] + fix[f]

    fine_cost = tendency_cost(1, fields, span, columns, reaction_count)
    coarse_cost = tendency_cost(1, fields, coarse_span, columns, reaction_count)

    def fine_scratch(states):
        return pltpu.VMEM((states, fields, span, columns), f32)

    def coarse_scratch(states):
        return pltpu.VMEM((states, fields, coarse_span, columns), f32)

    u_flat = u_start.reshape(fields, span, columns)
    nodes = guess[0].reshape(3, fields, span, columns)
    nodes = jnp.concatenate([jnp.where(section == 0, u_flat, nodes[0])[None], nodes[1:]], axis=0)
    coarse_start = jnp.einsum("cy,fzyx->fzcx", restrict_plane,
                              u_start, precision=HIGHEST).reshape(fields, coarse_span, columns)
    start_halo = halo(coarse_start, coarse_rows)

    coarse_one = jax.ShapeDtypeStruct((1, fields, coarse_span, columns), f32)
    plane_one = jax.ShapeDtypeStruct((1, fields, coarse_rows, columns), f32)
    fine_plane = jax.ShapeDtypeStruct((1, fields, rows, columns), f32)
    node_planes = jax.ShapeDtypeStruct((3, fields, rows, columns), f32)

    def coarse_step(flag, w, w_halo, base, rint):
        return call(
            chain_kernel,
            (flag, w, w_halo[0], w_halo[1], coarse_start[None], start_halo[0][None],
             start_halo[1][None], lop_coarse, xt) + coarse_scalars + (base, rint),
            (True,) + (False,) * 8 + scalar_kinds + (False, False),
            (coarse_one, coarse_one, plane_one, plane_one, plane_one, plane_one),
            [pltpu.VMEM((1, fields, coarse_span, columns), f32), coarse_scratch(1)],
            *coarse_cost,
        )

    tm_n = sections
    both = ("tm", "space")
    hop_pairs = [(d, d + 1) for d in range(tm_n - 1)]
    prev_pairs = [
        (d * space_n + s, (d + 1) * space_n + (s + 1) % space_n)
        for d in range(tm_n - 1) for s in range(space_n)
    ]
    next_pairs = [
        (d * space_n + s, (d + 1) * space_n + (s - 1) % space_n)
        for d in range(tm_n - 1) for s in range(space_n)
    ]
    always = jnp.ones((1,), jnp.int32)

    fine_end = None
    coarse_end = None
    for iteration in range(ITERS):
        if iteration == 0:
            node_prev, node_next = halo(nodes, rows)
        else:
            node_prev, node_next = swap(node_head, node_tail)
        f_all, a1, a1_head, a1_tail = call(
            nodes_kernel,
            (nodes, node_prev, node_next, lop_fine, xt) + scalars,
            (False,) * 5 + scalar_kinds,
            (jax.ShapeDtypeStruct((3, fields, span, columns), f32), fine_state, fine_plane,
             fine_plane),
            [fine_scratch(3)],
            fine_cost[0] * 3, fine_cost[1] * 3,
        )
        a1_prev, a1_next = swap(a1_head, a1_tail)
        g1, a2, a2_head, a2_tail = call(
            middle_kernel,
            (a1, a1_prev, a1_next, lop_fine, xt) + scalars + (f_all,),
            (False,) * 5 + scalar_kinds + (False,),
            (fine_state, fine_state, fine_plane, fine_plane),
            [fine_scratch(1)],
            *fine_cost,
        )
        a2_prev, a2_next = swap(a2_head, a2_tail)
        rint, c1, c0 = call(
            ending_kernel,
            (a2, a2_prev, a2_next, lop_fine, xt) + scalars + (f_all, g1, nodes, rmat),
            (False,) * 5 + scalar_kinds + (False,) * 4,
            (coarse_state, coarse_state, coarse_state),
            [pltpu.VMEM((1, fields, span, columns), f32), fine_scratch(1)],
            *fine_cost,
        )
        (base,) = call(
            base_kernel,
            (c0[None], node_prev, node_next, restrict_plane, lop_coarse, xt) + coarse_scalars,
            (False,) * 6 + scalar_kinds,
            (jax.ShapeDtypeStruct((1, fields, coarse_span, columns), f32),),
            [pltpu.VMEM((1, fields, coarse_rows, columns), f32),
             pltpu.VMEM((1, fields, coarse_rows, columns), f32), coarse_scratch(1)],
            *coarse_cost,
        )
        last = iteration + 1 == ITERS
        if not last:
            a2_handed = lax.ppermute(a2, "tm", hop_pairs)
        begin = coarse_start[None]
        begin_halo = (start_halo[0][None], start_halo[1][None])
        flag = always
        for n in range(sections):
            finish, w0, _, _, head, tail = coarse_step(flag, begin, begin_halo, base, rint[None])
            if n + 1 < sections:
                begin = lax.ppermute(finish, "tm", hop_pairs)
                begin_halo = (lax.ppermute(tail, both, prev_pairs),
                              lax.ppermute(head, both, next_pairs))
                flag = lead
        w0 = w0[0]
        w1 = finish[0]
        if last:
            (fine_end,) = call(
                finish_kernel,
                (a2, c1, w1, pmat),
                (False,) * 4,
                (fine_state,),
                [],
                2 * fields * span * coarse_span * columns * 6, 0,
            )
            coarse_end = w1
        else:
            nodes, node_head, node_tail = call(
                correct_kernel,
                (a1, a2, c0, c1, w0, w1, a2_handed, u_flat, rmat, pmat, lead),
                (False,) * 10 + (True,),
                (jax.ShapeDtypeStruct((3, fields, span, columns), f32), node_planes,
                 node_planes),
                [],
                8 * fields * span * coarse_span * columns * 6, 0,
            )
    fine_end = fine_end.reshape(1, fields, depth, rows, columns)
    coarse_end = coarse_end.reshape(1, fields, depth, coarse_rows, columns)
    return (fine_end, coarse_end)


def solution(mesh):
    return jax.shard_map(
        per_device,
        mesh=mesh,
        in_specs=(
            P(None, "space", None, None),
            P("tm", None, None, "space", None, None),
            P(),
            P(),
            P(),
            P(),
        ),
        out_specs=(P("tm", None, "space", None, None), P("tm", None, "space", None, None)),
        check_vma=False,
    )
```

```python
import jax
import jax.numpy as jnp
import numpy as np
from jax import lax
from jax.experimental import pallas as pl
from jax.experimental.pallas import tpu as pltpu
from jax.sharding import PartitionSpec as P

ITERS = 2


STEP = 0.01
HIGHEST = lax.Precision.HIGHEST
FINE_NODES = np.array(
    [
        -1.0,
        -0.8717401485096066,
        -0.5917001814331423,
        -0.2092992179024789,
        0.2092992179024789,
        0.5917001814331423,
        0.8717401485096066,
        1.0,
    ]
)
COARSE_NODES = np.array([-1.0, -0.4472135954999579, 0.4472135954999579, 1.0])


def lagrange_table(source, target):
    table = np.ones((len(target), len(source)))
    for j in range(len(source)):
        for m in range(len(source)):
            if m != j:
                table[:, j] *= (target - source[m]) / (source[j] - source[m])
    return table


def derivative_table(points):
    total = len(points)
    weights = np.array(
        [
            1.0 / np.prod([points[j] - points[m] for m in range(total) if m != j])
            for j in range(total)
        ]
    )
    table = np.zeros((total, total))
    for i in range(total):
        for j in range(total):
            if i != j:
                table[i, j] = weights[j] / weights[i] / (points[i] - points[j])
        table[i, i] = -np.sum(table[i])
    return table


def element_tables(length, table, lift):
    per_element = table.shape[0]
    block = np.kron(np.eye(length // per_element), table)
    position = np.arange(length) % per_element
    identity = np.eye(length)
    before = np.roll(identity, -1, axis=1)
    after = np.roll(identity, 1, axis=1)
    first_mask = np.where(position == 0, 1.0, 0.0)
    last_mask = np.where(position == per_element - 1, 1.0, 0.0)
    upwind = lift * first_mask[:, None] * (before - identity)
    downwind = lift * last_mask[:, None] * (after - identity)
    return (block, upwind, downwind)


def widen(matrix):
    length = matrix.shape[0]
    wider = np.zeros((length, matrix.shape[1] + 2))
    wider[:, 1:-1] = matrix
    return wider


def padded_tables(length, table, lift):
    block, upwind, downwind = element_tables(length, table, lift)
    block_wide = widen(block)
    upwind_wide = widen(upwind)
    downwind_wide = widen(downwind)
    upwind_wide[0, length] = 0.0
    upwind_wide[0, 0] = lift
    downwind_wide[length - 1, 1] = 0.0
    downwind_wide[length - 1, length + 1] = lift
    return (block_wide, upwind_wide, downwind_wide)


def field_operators(speed, tables):
    block = jnp.asarray(tables[0], jnp.float32)
    upwind = jnp.asarray(tables[1], jnp.float32)
    downwind = jnp.asarray(tables[2], jnp.float32)
    speeds = speed[:, None, None]
    return (
        -speeds * block + jnp.maximum(speeds, 0.0) * upwind + jnp.maximum(-speeds, 0.0) * downwind
    )


def speed_combination(speed, tables):
    block = jnp.asarray(tables[0], jnp.float32)[None]
    upwind = jnp.asarray(tables[1], jnp.float32)[None]
    downwind = jnp.asarray(tables[2], jnp.float32)[None]
    speeds = speed[:, None, None]
    return (
        -speeds * block + jnp.maximum(speeds, 0.0) * upwind + jnp.maximum(-speeds, 0.0) * downwind
    )


def dot(a, b):
    return jnp.dot(a, b, precision=HIGHEST, preferred_element_type=jnp.float32)


def tdot(a, b):
    return jnp.dot(a, b, precision=lax.Precision.HIGH, preferred_element_type=jnp.float32)


def lanes(parts):
    return jnp.concatenate(parts, axis=1)


def unlanes(wide, width):
    return [wide[:, i * width:(i + 1) * width] for i in range(wide.shape[1] // width)]


def tendency_into(out_ref, v_ref, prev_ref, next_ref, k_ref, d_ref, cf_ref, rx_ref,
                  rate_ref, en_ref, s_ref, y_elem):
    states, fields, span, columns = v_ref.shape
    rows = prev_ref.shape[2]
    planes = span // rows
    f32 = jnp.float32
    row = lax.broadcasted_iota(jnp.int32, (span, columns), 0)
    lane = lax.broadcasted_iota(jnp.int32, (span, columns), 1)
    yy = row % rows
    zz = row // rows
    x_first = lane % 8 == 0
    x_last = lane % 8 == 7
    y_first = yy % y_elem == 0
    y_last = yy % y_elem == y_elem - 1
    z_first = zz % 8 == 0
    z_last = zz % 8 == 7

    def scoped(xd_ref, yz_ref):
        for b in range(states):
            xd_ref[b] = tdot(v_ref[b].reshape(fields * span, columns), d_ref[...]).reshape(
                fields, span, columns)
            yz_ref[b] = tdot(k_ref[...], lanes([v_ref[b, f] for f in range(fields)]))
        for b in range(states):
            def field_body(f, carry):
                v = v_ref[b, f]
                cols = pl.ds(pl.multiple_of(f * columns, columns), columns)
                t = (cf_ref[0, f] * xd_ref[b, f] + cf_ref[1, f] * yz_ref[b, pl.ds(0, span), cols]
                     + cf_ref[2, f] * yz_ref[b, pl.ds(span, span), cols])
                before_x = pltpu.roll(v, 1, 1)
                after_x = pltpu.roll(v, columns - 1, 1)
                t = t + jnp.where(x_first, cf_ref[3, f] * (before_x - v), 0.0)
                t = t + jnp.where(x_last, cf_ref[4, f] * (after_x - v), 0.0)
                before_y = jnp.where(yy == 0, pltpu.roll(v, span - rows + 1, 0),
                                     pltpu.roll(v, 1, 0))
                after_y = jnp.where(yy == rows - 1, pltpu.roll(v, rows - 1, 0),
                                    pltpu.roll(v, span - 1, 0))
                t = t + jnp.where(y_first, cf_ref[5, f] * (before_y - v), 0.0)
                t = t + jnp.where(y_last, cf_ref[6, f] * (after_y - v), 0.0)
                if planes > 8:
                    before_z = pltpu.roll(v, rows, 0)
                    after_z = pltpu.roll(v, span - rows, 0)
                    t = t + jnp.where(z_first & (zz > 0), cf_ref[7, f] * before_z, 0.0)
                    t = t + jnp.where(z_last & (zz < planes - 1), cf_ref[8, f] * after_z, 0.0)
                t = t - jnp.where(z_first, cf_ref[7, f] * v, 0.0)
                t = t - jnp.where(z_last, cf_ref[8, f] * v, 0.0)
                out_ref[b, f] = t
                out_ref[b, f, pl.ds(0, rows), :] = (
                    out_ref[b, f, pl.ds(0, rows), :] + cf_ref[7, f] * prev_ref[b, f]
                )
                out_ref[b, f, pl.ds(span - rows, rows), :] = (
                    out_ref[b, f, pl.ds(span - rows, rows), :] + cf_ref[8, f] * next_ref[b, f]
                )
                s_ref[b, f] = jnp.tanh(v)
                return carry

            lax.fori_loop(0, fields, field_body, 0)

    pl.run_scoped(scoped, pltpu.VMEM((states, fields, span, columns), f32),
                  pltpu.VMEM((states, 2 * span, fields * columns), f32))
    for b in range(states):
        cooling = 1.0 / (1.5 + 0.5 * s_ref[b, fields - 1])

        def reaction_body(r, carry):
            first = rx_ref[r, 0]
            second = rx_ref[r, 1]
            product = rx_ref[r, 2]
            progress = (
                rate_ref[r] * jnp.exp(-en_ref[r] * cooling) * s_ref[b, first] * s_ref[b, second]
            )
            out_ref[b, product] = out_ref[b, product] + progress
            out_ref[b, first] = out_ref[b, first] - progress
            out_ref[b, second] = out_ref[b, second] - progress
            return carry

        lax.fori_loop(0, rx_ref.shape[0], reaction_body, 0)


def vmem():
    return pl.BlockSpec(memory_space=pltpu.VMEM)


def smem():
    return pl.BlockSpec(memory_space=pltpu.SMEM)


def tendency_cost(states, fields, span, columns, reactions):
    flops = states * fields * (2 * span * span * columns + 2 * span * columns * columns) * 6
    flops += states * span * columns * (8 * reactions + 4 * fields)
    trans = states * span * columns * (fields + 2 * reactions)
    return flops, trans


def call(kernel, ins, in_kinds, outs, scratch, flops, trans):
    nbytes = sum(int(np.prod(x.shape)) * 4 for x in ins) + sum(
        int(np.prod(o.shape)) * 4 for o in outs
    )
    return pl.pallas_call(
        kernel,
        out_shape=outs,
        in_specs=[smem() if k else vmem() for k in in_kinds],
        out_specs=tuple(vmem() for _ in outs),
        scratch_shapes=scratch,
        cost_estimate=pl.CostEstimate(
            flops=int(flops), transcendentals=int(trans), bytes_accessed=int(nbytes)
        ),
    )(*ins)


def per_device(u_start, guess, velocity, rates, energies, reactions):
    fields, depth, rows, columns = u_start.shape
    coarse_rows = rows // 2
    span = depth * rows
    coarse_span = depth * coarse_rows
    reaction_count = rates.shape[0]
    fine_table = derivative_table(FINE_NODES)
    coarse_table = derivative_table(COARSE_NODES)
    fine_elem = len(FINE_NODES)
    coarse_elem = len(COARSE_NODES)
    xt = jnp.asarray(np.kron(np.eye(columns // fine_elem), fine_table).T, jnp.float32)
    z_block = np.kron(np.eye(depth // fine_elem), fine_table)

    def plane_operator(y_table, plane_rows):
        y_block = np.kron(np.eye(plane_rows // y_table.shape[0]), y_table)
        return jnp.asarray(
            np.concatenate([np.kron(np.eye(depth), y_block), np.kron(z_block, np.eye(plane_rows))]),
            jnp.float32,
        )

    lop_fine = plane_operator(fine_table, rows)
    lop_coarse = plane_operator(coarse_table, coarse_rows)

    def coefficients(y_lift):
        up = jnp.maximum(velocity, 0.0)
        down = jnp.maximum(-velocity, 0.0)
        return jnp.concatenate([
            -velocity,
            28.0 * up[0:1], 28.0 * down[0:1],
            y_lift * up[1:2], y_lift * down[1:2],
            28.0 * up[2:3], 28.0 * down[2:3],
        ])

    cf_fine = coefficients(28.0)
    cf_coarse = coefficients(6.0)
    restrict_rows = np.kron(np.eye(rows // 8), lagrange_table(FINE_NODES, COARSE_NODES))
    prolong_rows = np.kron(np.eye(rows // 8), lagrange_table(COARSE_NODES, FINE_NODES))
    rmat = jnp.asarray(np.kron(np.eye(depth), restrict_rows), jnp.float32)
    pmat = jnp.asarray(np.kron(np.eye(depth), prolong_rows), jnp.float32)
    restrict_plane = jnp.asarray(restrict_rows, jnp.float32)
    scalars = (cf_fine, reactions.astype(jnp.int32), rates, energies)
    coarse_scalars = (cf_coarse, reactions.astype(jnp.int32), rates, energies)
    scalar_kinds = (True, True, True, True)

    space_n = lax.axis_size("space")
    sections = lax.axis_size("tm")
    section = lax.axis_index("tm")
    lead = (section == 0).astype(jnp.int32).reshape(1)

    def halo(x, plane_rows):
        head = x[..., :plane_rows, :]
        tail = x[..., x.shape[-2] - plane_rows:, :]
        return swap(head, tail)

    def swap(head, tail):
        prev = lax.ppermute(tail, "space", [(i, (i + 1) % space_n) for i in range(space_n)])
        nxt = lax.ppermute(head, "space", [((i + 1) % space_n, i) for i in range(space_n)])
        return prev, nxt

    f32 = jnp.float32
    fine_state = jax.ShapeDtypeStruct((1, fields, span, columns), f32)
    coarse_state = jax.ShapeDtypeStruct((fields, coarse_span, columns), f32)

    def nodes_kernel(u_ref, p_ref, n_ref, l_ref, x_ref, zc_ref, rx_ref, ra_ref, en_ref,
                     f_ref, a1_ref, h_ref, t_ref, s_ref):
        tendency_into(f_ref, u_ref, p_ref, n_ref, l_ref, x_ref, zc_ref, rx_ref, ra_ref, en_ref,
                      s_ref, fine_elem)

        def body(f, carry):
            value = u_ref[0, f] + STEP * (
                5.0 * f_ref[0, f] + 8.0 * f_ref[1, f] - f_ref[2, f]
            ) / 24.0
            a1_ref[0, f] = value
            h_ref[0, f] = value[:rows]
            t_ref[0, f] = value[span - rows:]
            return carry

        lax.fori_loop(0, fields, body, 0)

    def middle_kernel(a1_ref, p_ref, n_ref, l_ref, x_ref, zc_ref, rx_ref, ra_ref, en_ref,
                      f_ref, g1_ref, a2_ref, h_ref, t_ref, s_ref):
        tendency_into(g1_ref, a1_ref, p_ref, n_ref, l_ref, x_ref, zc_ref, rx_ref, ra_ref,
                      en_ref, s_ref, fine_elem)

        def body(f, carry):
            value = (
                a1_ref[0, f]
                + 0.5 * STEP * (g1_ref[0, f] - f_ref[1, f])
                + STEP * (-f_ref[0, f] + 8.0 * f_ref[1, f] + 5.0 * f_ref[2, f]) / 24.0
            )
            a2_ref[0, f] = value
            h_ref[0, f] = value[:rows]
            t_ref[0, f] = value[span - rows:]
            return carry

        lax.fori_loop(0, fields, body, 0)

    def ending_kernel(a2_ref, p_ref, n_ref, l_ref, x_ref, zc_ref, rx_ref, ra_ref, en_ref,
                      f_ref, g1_ref, u_ref, r_ref, rint_ref, c1_ref, c0_ref, g2_ref, s_ref):
        tendency_into(g2_ref, a2_ref, p_ref, n_ref, l_ref, x_ref, zc_ref, rx_ref, ra_ref,
                      en_ref, s_ref, fine_elem)

        def body(f, carry):
            g2_ref[0, f] = STEP * (f_ref[0, f] + 4.0 * g1_ref[0, f] + g2_ref[0, f]) / 6.0
            return carry

        lax.fori_loop(0, fields, body, 0)
        rm = r_ref[...]
        for dst, src_ref, lead_index in ((rint_ref, g2_ref, 0), (c1_ref, a2_ref, 0), (c0_ref, u_ref, 0)):
            wide = dot(rm, lanes([src_ref[lead_index, f] for f in range(fields)]))
            for f, part in enumerate(unlanes(wide, columns)):
                dst[f] = part

    def base_kernel(c_ref, p_ref, n_ref, r_ref, l_ref, x_ref, zc_ref, rx_ref, ra_ref, en_ref,
                    out_ref, bp_ref, bn_ref, s_ref):
        rm = r_ref[...]
        for dst, src_ref in ((bp_ref, p_ref), (bn_ref, n_ref)):
            wide = dot(rm, lanes([src_ref[0, f] for f in range(fields)]))
            for f, part in enumerate(unlanes(wide, columns)):
                dst[0, f] = part
        tendency_into(out_ref, c_ref, bp_ref, bn_ref, l_ref, x_ref, zc_ref, rx_ref, ra_ref,
                      en_ref, s_ref, coarse_elem)

    def chain_kernel(lead_ref, w_ref, p_ref, n_ref, ws_ref, ps_ref, ns_ref, l_ref, x_ref,
                     zc_ref, rx_ref, ra_ref, en_ref, base_ref, rint_ref, out_ref, begin_ref,
                     bp_ref, bn_ref, h_ref, t_ref, g_ref, s_ref):
        @pl.when(lead_ref[0] != 0)
        def _():
            begin_ref[...] = ws_ref[...]
            bp_ref[...] = ps_ref[...]
            bn_ref[...] = ns_ref[...]

        @pl.when(lead_ref[0] == 0)
        def _():
            begin_ref[...] = w_ref[...]
            bp_ref[...] = p_ref[...]
            bn_ref[...] = n_ref[...]

        tendency_into(g_ref, begin_ref, bp_ref, bn_ref, l_ref, x_ref, zc_ref, rx_ref, ra_ref,
                      en_ref, s_ref, coarse_elem)

        def body(f, carry):
            value = begin_ref[0, f] + STEP * (g_ref[0, f] - base_ref[0, f]) + rint_ref[0, f]
            out_ref[0, f] = value
            h_ref[0, f] = value[:coarse_rows]
            t_ref[0, f] = value[coarse_span - coarse_rows:]
            return carry

        lax.fori_loop(0, fields, body, 0)

    def correct_kernel(a1_ref, a2_ref, c0_ref, c1_ref, w0_ref, w1_ref, prev_ref, us_ref,
                       r_ref, pm_ref, lead_ref, out_ref, h_ref, t_ref):
        pm = pm_ref[...]
        first_change = [w0_ref[f] - c0_ref[f] for f in range(fields)]
        last_change = [w1_ref[f] - c1_ref[f] for f in range(fields)]
        middle_fix = unlanes(
            dot(pm, lanes([0.5 * (first_change[f] + last_change[f]) for f in range(fields)])),
            columns,
        )
        last_fix = unlanes(dot(pm, lanes(last_change)), columns)
        handed = lanes([prev_ref[0, f] for f in range(fields)])
        handed_fix = unlanes(
            dot(pm, lanes([w0_ref[f] for f in range(fields)]) - dot(r_ref[...], handed)),
            columns,
        )
        for f in range(fields):
            values = (
                jnp.where(lead_ref[0] != 0, us_ref[f], prev_ref[0, f] + handed_fix[f]),
                a1_ref[0, f] + middle_fix[f],
                a2_ref[0, f] + last_fix[f],
            )
            for b, value in enumerate(values):
                out_ref[b, f] = value
                h_ref[b, f] = value[:rows]
                t_ref[b, f] = value[span - rows:]

    def finish_kernel(a2_ref, c1_ref, w1_ref, pm_ref, out_ref):
        fix = unlanes(
            dot(pm_ref[...], lanes([w1_ref[f] - c1_ref[f] for f in range(fields)])), columns
        )
        for f in range(fields):
            out_ref[0, f] = a2_ref[0, f] + fix[f]

    fine_cost = tendency_cost(1, fields, span, columns, reaction_count)
    coarse_cost = tendency_cost(1, fields, coarse_span, columns, reaction_count)

    def fine_scratch(states):
        return pltpu.VMEM((states, fields, span, columns), f32)

    def coarse_scratch(states):
        return pltpu.VMEM((states, fields, coarse_span, columns), f32)

    u_flat = u_start.reshape(fields, span, columns)
    nodes = guess[0].reshape(3, fields, span, columns)
    nodes = jnp.concatenate([jnp.where(section == 0, u_flat, nodes[0])[None], nodes[1:]], axis=0)
    coarse_start = jnp.einsum("cy,fzyx->fzcx", restrict_plane,
                              u_start, precision=HIGHEST).reshape(fields, coarse_span, columns)
    start_halo = halo(coarse_start, coarse_rows)

    coarse_one = jax.ShapeDtypeStruct((1, fields, coarse_span, columns), f32)
    plane_one = jax.ShapeDtypeStruct((1, fields, coarse_rows, columns), f32)
    fine_plane = jax.ShapeDtypeStruct((1, fields, rows, columns), f32)
    node_planes = jax.ShapeDtypeStruct((3, fields, rows, columns), f32)

    def coarse_step(flag, w, w_halo, base, rint):
        return call(
            chain_kernel,
            (flag, w, w_halo[0], w_halo[1], coarse_start[None], start_halo[0][None],
             start_halo[1][None], lop_coarse, xt) + coarse_scalars + (base, rint),
            (True,) + (False,) * 8 + scalar_kinds + (False, False),
            (coarse_one, coarse_one, plane_one, plane_one, plane_one, plane_one),
            [pltpu.VMEM((1, fields, coarse_span, columns), f32), coarse_scratch(1)],
            *coarse_cost,
        )

    tm_n = sections
    both = ("tm", "space")
    hop_pairs = [(d, d + 1) for d in range(tm_n - 1)]
    prev_pairs = [
        (d * space_n + s, (d + 1) * space_n + (s + 1) % space_n)
        for d in range(tm_n - 1) for s in range(space_n)
    ]
    next_pairs = [
        (d * space_n + s, (d + 1) * space_n + (s - 1) % space_n)
        for d in range(tm_n - 1) for s in range(space_n)
    ]
    always = jnp.ones((1,), jnp.int32)

    fine_end = None
    coarse_end = None
    for iteration in range(ITERS):
        if iteration == 0:
            node_prev, node_next = halo(nodes, rows)
        else:
            node_prev, node_next = swap(node_head, node_tail)
        f_all, a1, a1_head, a1_tail = call(
            nodes_kernel,
            (nodes, node_prev, node_next, lop_fine, xt) + scalars,
            (False,) * 5 + scalar_kinds,
            (jax.ShapeDtypeStruct((3, fields, span, columns), f32), fine_state, fine_plane,
             fine_plane),
            [fine_scratch(3)],
            fine_cost[0] * 3, fine_cost[1] * 3,
        )
        a1_prev, a1_next = swap(a1_head, a1_tail)
        g1, a2, a2_head, a2_tail = call(
            middle_kernel,
            (a1, a1_prev, a1_next, lop_fine, xt) + scalars + (f_all,),
            (False,) * 5 + scalar_kinds + (False,),
            (fine_state, fine_state, fine_plane, fine_plane),
            [fine_scratch(1)],
            *fine_cost,
        )
        a2_prev, a2_next = swap(a2_head, a2_tail)
        rint, c1, c0 = call(
            ending_kernel,
            (a2, a2_prev, a2_next, lop_fine, xt) + scalars + (f_all, g1, nodes, rmat),
            (False,) * 5 + scalar_kinds + (False,) * 4,
            (coarse_state, coarse_state, coarse_state),
            [pltpu.VMEM((1, fields, span, columns), f32), fine_scratch(1)],
            *fine_cost,
        )
        (base,) = call(
            base_kernel,
            (c0[None], node_prev, node_next, restrict_plane, lop_coarse, xt) + coarse_scalars,
            (False,) * 6 + scalar_kinds,
            (jax.ShapeDtypeStruct((1, fields, coarse_span, columns), f32),),
            [pltpu.VMEM((1, fields, coarse_rows, columns), f32),
             pltpu.VMEM((1, fields, coarse_rows, columns), f32), coarse_scratch(1)],
            *coarse_cost,
        )
        last = iteration + 1 == ITERS
        if not last:
            a2_handed = lax.ppermute(a2, "tm", hop_pairs)
        begin = coarse_start[None]
        begin_halo = (start_halo[0][None], start_halo[1][None])
        flag = always
        for n in range(sections):
            finish, w0, _, _, head, tail = coarse_step(flag, begin, begin_halo, base, rint[None])
            if n + 1 < sections:
                begin = lax.ppermute(finish, "tm", hop_pairs)
                begin_halo = (lax.ppermute(tail, both, prev_pairs),
                              lax.ppermute(head, both, next_pairs))
                flag = lead
        w0 = w0[0]
        w1 = finish[0]
        if last:
            (fine_end,) = call(
                finish_kernel,
                (a2, c1, w1, pmat),
                (False,) * 4,
                (fine_state,),
                [],
                2 * fields * span * coarse_span * columns * 6, 0,
            )
            coarse_end = w1
        else:
            nodes, node_head, node_tail = call(
                correct_kernel,
                (a1, a2, c0, c1, w0, w1, a2_handed, u_flat, rmat, pmat, lead),
                (False,) * 10 + (True,),
                (jax.ShapeDtypeStruct((3, fields, span, columns), f32), node_planes,
                 node_planes),
                [],
                8 * fields * span * coarse_span * columns * 6, 0,
            )
    fine_end = fine_end.reshape(1, fields, depth, rows, columns)
    coarse_end = coarse_end.reshape(1, fields, depth, coarse_rows, columns)
    return (fine_end, coarse_end)


def solution(mesh):
    return jax.shard_map(
        per_device,
        mesh=mesh,
        in_specs=(
            P(None, "space", None, None),
            P("tm", None, None, "space", None, None),
            P(),
            P(),
            P(),
            P(),
        ),
        out_specs=(P("tm", None, "space", None, None), P("tm", None, "space", None, None)),
        check_vma=False,
    )
```

```python
import jax
import jax.numpy as jnp
import numpy as np
from jax import lax
from jax.experimental import pallas as pl
from jax.experimental.pallas import tpu as pltpu
from jax.sharding import PartitionSpec as P

ITERS = 2


STEP = 0.01
HIGHEST = lax.Precision.HIGHEST
FINE_NODES = np.array(
    [
        -1.0,
        -0.8717401485096066,
        -0.5917001814331423,
        -0.2092992179024789,
        0.2092992179024789,
        0.5917001814331423,
        0.8717401485096066,
        1.0,
    ]
)
COARSE_NODES = np.array([-1.0, -0.4472135954999579, 0.4472135954999579, 1.0])


def lagrange_table(source, target):
    table = np.ones((len(target), len(source)))
    for j in range(len(source)):
        for m in range(len(source)):
            if m != j:
                table[:, j] *= (target - source[m]) / (source[j] - source[m])
    return table


def derivative_table(points):
    total = len(points)
    weights = np.array(
        [
            1.0 / np.prod([points[j] - points[m] for m in range(total) if m != j])
            for j in range(total)
        ]
    )
    table = np.zeros((total, total))
    for i in range(total):
        for j in range(total):
            if i != j:
                table[i, j] = weights[j] / weights[i] / (points[i] - points[j])
        table[i, i] = -np.sum(table[i])
    return table


def element_tables(length, table, lift):
    per_element = table.shape[0]
    block = np.kron(np.eye(length // per_element), table)
    position = np.arange(length) % per_element
    identity = np.eye(length)
    before = np.roll(identity, -1, axis=1)
    after = np.roll(identity, 1, axis=1)
    first_mask = np.where(position == 0, 1.0, 0.0)
    last_mask = np.where(position == per_element - 1, 1.0, 0.0)
    upwind = lift * first_mask[:, None] * (before - identity)
    downwind = lift * last_mask[:, None] * (after - identity)
    return (block, upwind, downwind)


def widen(matrix):
    length = matrix.shape[0]
    wider = np.zeros((length, matrix.shape[1] + 2))
    wider[:, 1:-1] = matrix
    return wider


def padded_tables(length, table, lift):
    block, upwind, downwind = element_tables(length, table, lift)
    block_wide = widen(block)
    upwind_wide = widen(upwind)
    downwind_wide = widen(downwind)
    upwind_wide[0, length] = 0.0
    upwind_wide[0, 0] = lift
    downwind_wide[length - 1, 1] = 0.0
    downwind_wide[length - 1, length + 1] = lift
    return (block_wide, upwind_wide, downwind_wide)


def field_operators(speed, tables):
    block = jnp.asarray(tables[0], jnp.float32)
    upwind = jnp.asarray(tables[1], jnp.float32)
    downwind = jnp.asarray(tables[2], jnp.float32)
    speeds = speed[:, None, None]
    return (
        -speeds * block + jnp.maximum(speeds, 0.0) * upwind + jnp.maximum(-speeds, 0.0) * downwind
    )


def speed_combination(speed, tables):
    block = jnp.asarray(tables[0], jnp.float32)[None]
    upwind = jnp.asarray(tables[1], jnp.float32)[None]
    downwind = jnp.asarray(tables[2], jnp.float32)[None]
    speeds = speed[:, None, None]
    return (
        -speeds * block + jnp.maximum(speeds, 0.0) * upwind + jnp.maximum(-speeds, 0.0) * downwind
    )


def dot(a, b):
    return jnp.dot(a, b, precision=HIGHEST, preferred_element_type=jnp.float32)


def tdot(a, b):
    return jnp.dot(a, b, precision=lax.Precision.HIGH, preferred_element_type=jnp.float32)


def lanes(parts):
    return jnp.concatenate(parts, axis=1)


def unlanes(wide, width):
    return [wide[:, i * width:(i + 1) * width] for i in range(wide.shape[1] // width)]


def tendency_into(out_ref, v_ref, prev_ref, next_ref, k_ref, d_ref, cf_ref, rx_ref,
                  rate_ref, en_ref, s_ref, y_elem):
    states, fields, span, columns = v_ref.shape
    rows = prev_ref.shape[2]
    planes = span // rows
    f32 = jnp.float32
    row = lax.broadcasted_iota(jnp.int32, (span, columns), 0)
    lane = lax.broadcasted_iota(jnp.int32, (span, columns), 1)
    yy = row % rows
    zz = row // rows
    x_first = lane % 8 == 0
    x_last = lane % 8 == 7
    y_first = yy % y_elem == 0
    y_last = yy % y_elem == y_elem - 1
    z_first = zz % 8 == 0
    z_last = zz % 8 == 7

    def scoped(xd_ref, yz_ref):
        for b in range(states):
            xd_ref[b] = tdot(v_ref[b].reshape(fields * span, columns), d_ref[...]).reshape(
                fields, span, columns)
            yz_ref[b] = tdot(k_ref[...], lanes([v_ref[b, f] for f in range(fields)]))
        for b in range(states):
            for f in range(fields):
                v = v_ref[b, f]
                cols = slice(f * columns, (f + 1) * columns)
                t = (cf_ref[0, f] * xd_ref[b, f] + cf_ref[1, f] * yz_ref[b, :span, cols]
                     + cf_ref[2, f] * yz_ref[b, span:, cols])
                before_x = pltpu.roll(v, 1, 1)
                after_x = pltpu.roll(v, columns - 1, 1)
                t = t + jnp.where(x_first, cf_ref[3, f] * (before_x - v), 0.0)
                t = t + jnp.where(x_last, cf_ref[4, f] * (after_x - v), 0.0)
                before_y = jnp.where(yy == 0, pltpu.roll(v, span - rows + 1, 0),
                                     pltpu.roll(v, 1, 0))
                after_y = jnp.where(yy == rows - 1, pltpu.roll(v, rows - 1, 0),
                                    pltpu.roll(v, span - 1, 0))
                t = t + jnp.where(y_first, cf_ref[5, f] * (before_y - v), 0.0)
                t = t + jnp.where(y_last, cf_ref[6, f] * (after_y - v), 0.0)
                if planes > 8:
                    before_z = pltpu.roll(v, rows, 0)
                    after_z = pltpu.roll(v, span - rows, 0)
                    t = t + jnp.where(z_first & (zz > 0), cf_ref[7, f] * before_z, 0.0)
                    t = t + jnp.where(z_last & (zz < planes - 1), cf_ref[8, f] * after_z, 0.0)
                t = t - jnp.where(z_first, cf_ref[7, f] * v, 0.0)
                t = t - jnp.where(z_last, cf_ref[8, f] * v, 0.0)
                out_ref[b, f] = t
                out_ref[b, f, pl.ds(0, rows), :] = (
                    out_ref[b, f, pl.ds(0, rows), :] + cf_ref[7, f] * prev_ref[b, f]
                )
                out_ref[b, f, pl.ds(span - rows, rows), :] = (
                    out_ref[b, f, pl.ds(span - rows, rows), :] + cf_ref[8, f] * next_ref[b, f]
                )
                s_ref[b, f] = jnp.tanh(v)

    pl.run_scoped(scoped, pltpu.VMEM((states, fields, span, columns), f32),
                  pltpu.VMEM((states, 2 * span, fields * columns), f32))
    for b in range(states):
        cooling = 1.0 / (1.5 + 0.5 * s_ref[b, fields - 1])

        def reaction_body(r, carry):
            first = rx_ref[r, 0]
            second = rx_ref[r, 1]
            product = rx_ref[r, 2]
            progress = (
                rate_ref[r] * jnp.exp(-en_ref[r] * cooling) * s_ref[b, first] * s_ref[b, second]
            )
            out_ref[b, product] = out_ref[b, product] + progress
            out_ref[b, first] = out_ref[b, first] - progress
            out_ref[b, second] = out_ref[b, second] - progress
            return carry

        lax.fori_loop(0, rx_ref.shape[0], reaction_body, 0)


def vmem():
    return pl.BlockSpec(memory_space=pltpu.VMEM)


def smem():
    return pl.BlockSpec(memory_space=pltpu.SMEM)


def tendency_cost(states, fields, span, columns, reactions):
    flops = states * fields * (2 * span * span * columns + 2 * span * columns * columns) * 6
    flops += states * span * columns * (8 * reactions + 4 * fields)
    trans = states * span * columns * (fields + 2 * reactions)
    return flops, trans


def call(kernel, ins, in_kinds, outs, scratch, flops, trans):
    nbytes = sum(int(np.prod(x.shape)) * 4 for x in ins) + sum(
        int(np.prod(o.shape)) * 4 for o in outs
    )
    return pl.pallas_call(
        kernel,
        out_shape=outs,
        in_specs=[smem() if k else vmem() for k in in_kinds],
        out_specs=tuple(vmem() for _ in outs),
        scratch_shapes=scratch,
        cost_estimate=pl.CostEstimate(
            flops=int(flops), transcendentals=int(trans), bytes_accessed=int(nbytes)
        ),
    )(*ins)


def per_device(u_start, guess, velocity, rates, energies, reactions):
    fields, depth, rows, columns = u_start.shape
    coarse_rows = rows // 2
    span = depth * rows
    coarse_span = depth * coarse_rows
    reaction_count = rates.shape[0]
    fine_table = derivative_table(FINE_NODES)
    coarse_table = derivative_table(COARSE_NODES)
    fine_elem = len(FINE_NODES)
    coarse_elem = len(COARSE_NODES)
    xt = jnp.asarray(np.kron(np.eye(columns // fine_elem), fine_table).T, jnp.float32)
    z_block = np.kron(np.eye(depth // fine_elem), fine_table)

    def plane_operator(y_table, plane_rows):
        y_block = np.kron(np.eye(plane_rows // y_table.shape[0]), y_table)
        return jnp.asarray(
            np.concatenate([np.kron(np.eye(depth), y_block), np.kron(z_block, np.eye(plane_rows))]),
            jnp.float32,
        )

    lop_fine = plane_operator(fine_table, rows)
    lop_coarse = plane_operator(coarse_table, coarse_rows)

    def coefficients(y_lift):
        up = jnp.maximum(velocity, 0.0)
        down = jnp.maximum(-velocity, 0.0)
        return jnp.concatenate([
            -velocity,
            28.0 * up[0:1], 28.0 * down[0:1],
            y_lift * up[1:2], y_lift * down[1:2],
            28.0 * up[2:3], 28.0 * down[2:3],
        ])

    cf_fine = coefficients(28.0)
    cf_coarse = coefficients(6.0)
    restrict_rows = np.kron(np.eye(rows // 8), lagrange_table(FINE_NODES, COARSE_NODES))
    prolong_rows = np.kron(np.eye(rows // 8), lagrange_table(COARSE_NODES, FINE_NODES))
    rmat = jnp.asarray(np.kron(np.eye(depth), restrict_rows), jnp.float32)
    pmat = jnp.asarray(np.kron(np.eye(depth), prolong_rows), jnp.float32)
    restrict_plane = jnp.asarray(restrict_rows, jnp.float32)
    scalars = (cf_fine, reactions.astype(jnp.int32), rates, energies)
    coarse_scalars = (cf_coarse, reactions.astype(jnp.int32), rates, energies)
    scalar_kinds = (True, True, True, True)

    space_n = lax.axis_size("space")
    sections = lax.axis_size("tm")
    section = lax.axis_index("tm")
    lead = (section == 0).astype(jnp.int32).reshape(1)

    def halo(x, plane_rows):
        head = x[..., :plane_rows, :]
        tail = x[..., x.shape[-2] - plane_rows:, :]
        return swap(head, tail)

    def swap(head, tail):
        prev = lax.ppermute(tail, "space", [(i, (i + 1) % space_n) for i in range(space_n)])
        nxt = lax.ppermute(head, "space", [((i + 1) % space_n, i) for i in range(space_n)])
        return prev, nxt

    f32 = jnp.float32
    fine_state = jax.ShapeDtypeStruct((1, fields, span, columns), f32)
    coarse_state = jax.ShapeDtypeStruct((fields, coarse_span, columns), f32)

    def nodes_kernel(u_ref, p_ref, n_ref, l_ref, x_ref, zc_ref, rx_ref, ra_ref, en_ref,
                     f_ref, a1_ref, h_ref, t_ref, s_ref):
        tendency_into(f_ref, u_ref, p_ref, n_ref, l_ref, x_ref, zc_ref, rx_ref, ra_ref, en_ref,
                      s_ref, fine_elem)

        def body(f, carry):
            value = u_ref[0, f] + STEP * (
                5.0 * f_ref[0, f] + 8.0 * f_ref[1, f] - f_ref[2, f]
            ) / 24.0
            a1_ref[0, f] = value
            h_ref[0, f] = value[:rows]
            t_ref[0, f] = value[span - rows:]
            return carry

        lax.fori_loop(0, fields, body, 0)

    def middle_kernel(a1_ref, p_ref, n_ref, l_ref, x_ref, zc_ref, rx_ref, ra_ref, en_ref,
                      f_ref, g1_ref, a2_ref, h_ref, t_ref, s_ref):
        tendency_into(g1_ref, a1_ref, p_ref, n_ref, l_ref, x_ref, zc_ref, rx_ref, ra_ref,
                      en_ref, s_ref, fine_elem)

        def body(f, carry):
            value = (
                a1_ref[0, f]
                + 0.5 * STEP * (g1_ref[0, f] - f_ref[1, f])
                + STEP * (-f_ref[0, f] + 8.0 * f_ref[1, f] + 5.0 * f_ref[2, f]) / 24.0
            )
            a2_ref[0, f] = value
            h_ref[0, f] = value[:rows]
            t_ref[0, f] = value[span - rows:]
            return carry

        lax.fori_loop(0, fields, body, 0)

    def ending_kernel(a2_ref, p_ref, n_ref, l_ref, x_ref, zc_ref, rx_ref, ra_ref, en_ref,
                      f_ref, g1_ref, r_ref, rint_ref, c1_ref, g2_ref, s_ref):
        tendency_into(g2_ref, a2_ref, p_ref, n_ref, l_ref, x_ref, zc_ref, rx_ref, ra_ref,
                      en_ref, s_ref, fine_elem)

        def body(f, carry):
            g2_ref[0, f] = STEP * (f_ref[0, f] + 4.0 * g1_ref[0, f] + g2_ref[0, f]) / 6.0
            return carry

        lax.fori_loop(0, fields, body, 0)
        rm = r_ref[...]
        for dst, src_ref, lead_index in ((rint_ref, g2_ref, 0), (c1_ref, a2_ref, 0)):
            wide = dot(rm, lanes([src_ref[lead_index, f] for f in range(fields)]))
            for f, part in enumerate(unlanes(wide, columns)):
                dst[f] = part

    def base_kernel(u_ref, p_ref, n_ref, r_ref, rp_ref, l_ref, x_ref, zc_ref, rx_ref, ra_ref,
                    en_ref, out_ref, c0_ref, bp_ref, bn_ref, s_ref):
        for dst, src_ref, table in ((c0_ref, u_ref, r_ref), (bp_ref, p_ref, rp_ref),
                                    (bn_ref, n_ref, rp_ref)):
            wide = dot(table[...], lanes([src_ref[0, f] for f in range(fields)]))
            for f, part in enumerate(unlanes(wide, columns)):
                dst[0, f] = part
        tendency_into(out_ref, c0_ref, bp_ref, bn_ref, l_ref, x_ref, zc_ref, rx_ref, ra_ref,
                      en_ref, s_ref, coarse_elem)

    def chain_kernel(w_ref, p_ref, n_ref, l_ref, x_ref, zc_ref, rx_ref, ra_ref, en_ref,
                     base_ref, rint_ref, out_ref, h_ref, t_ref, g_ref, s_ref):
        tendency_into(g_ref, w_ref, p_ref, n_ref, l_ref, x_ref, zc_ref, rx_ref, ra_ref,
                      en_ref, s_ref, coarse_elem)

        def body(f, carry):
            value = w_ref[0, f] + STEP * (g_ref[0, f] - base_ref[0, f]) + rint_ref[0, f]
            out_ref[0, f] = value
            h_ref[0, f] = value[:coarse_rows]
            t_ref[0, f] = value[coarse_span - coarse_rows:]
            return carry

        lax.fori_loop(0, fields, body, 0)

    def pick(sec_ref, w_refs, f, offset):
        value = w_refs[offset][0, f]
        for n in range(1, sections):
            value = jnp.where(sec_ref[0] == n, w_refs[n + offset][0, f], value)
        return value

    def correct_kernel(*refs):
        a1_ref, a2_ref, c0_ref, c1_ref = refs[:4]
        w_refs = refs[4:5 + sections]
        prev_ref, us_ref, r_ref, pm_ref, lead_ref, sec_ref, out_ref, h_ref, t_ref = refs[
            5 + sections:]
        pm = pm_ref[...]
        w0 = [pick(sec_ref, w_refs, f, 0) for f in range(fields)]
        first_change = [w0[f] - c0_ref[0, f] for f in range(fields)]
        last_change = [pick(sec_ref, w_refs, f, 1) - c1_ref[f] for f in range(fields)]
        middle_fix = unlanes(
            dot(pm, lanes([0.5 * (first_change[f] + last_change[f]) for f in range(fields)])),
            columns,
        )
        last_fix = unlanes(dot(pm, lanes(last_change)), columns)
        handed = lanes([prev_ref[0, f] for f in range(fields)])
        handed_fix = unlanes(
            dot(pm, lanes(w0) - dot(r_ref[...], handed)),
            columns,
        )
        for f in range(fields):
            values = (
                jnp.where(lead_ref[0] != 0, us_ref[f], prev_ref[0, f] + handed_fix[f]),
                a1_ref[0, f] + middle_fix[f],
                a2_ref[0, f] + last_fix[f],
            )
            for b, value in enumerate(values):
                out_ref[b, f] = value
                h_ref[b, f] = value[:rows]
                t_ref[b, f] = value[span - rows:]

    def finish_kernel(*refs):
        a2_ref, c1_ref = refs[:2]
        w_refs = refs[2:3 + sections]
        pm_ref, sec_ref, out_ref, coarse_ref = refs[3 + sections:]
        w1 = [pick(sec_ref, w_refs, f, 1) for f in range(fields)]
        fix = unlanes(
            dot(pm_ref[...], lanes([w1[f] - c1_ref[f] for f in range(fields)])), columns
        )
        for f in range(fields):
            out_ref[0, f] = a2_ref[0, f] + fix[f]
            coarse_ref[0, f] = w1[f]

    fine_cost = tendency_cost(1, fields, span, columns, reaction_count)
    coarse_cost = tendency_cost(1, fields, coarse_span, columns, reaction_count)

    def fine_scratch(states):
        return pltpu.VMEM((states, fields, span, columns), f32)

    def coarse_scratch(states):
        return pltpu.VMEM((states, fields, coarse_span, columns), f32)

    u_flat = u_start.reshape(fields, span, columns)
    nodes = guess[0].reshape(3, fields, span, columns)
    nodes = jnp.concatenate([jnp.where(section == 0, u_flat, nodes[0])[None], nodes[1:]], axis=0)
    coarse_start = jnp.einsum("cy,fzyx->fzcx", restrict_plane,
                              u_start, precision=HIGHEST).reshape(fields, coarse_span, columns)
    start_halo = halo(coarse_start, coarse_rows)

    coarse_one = jax.ShapeDtypeStruct((1, fields, coarse_span, columns), f32)
    plane_one = jax.ShapeDtypeStruct((1, fields, coarse_rows, columns), f32)
    fine_plane = jax.ShapeDtypeStruct((1, fields, rows, columns), f32)
    node_planes = jax.ShapeDtypeStruct((3, fields, rows, columns), f32)

    def coarse_step(w, w_halo, base, rint):
        return call(
            chain_kernel,
            (w, w_halo[0], w_halo[1], lop_coarse, xt) + coarse_scalars + (base, rint),
            (False,) * 5 + scalar_kinds + (False, False),
            (coarse_one, plane_one, plane_one),
            [pltpu.VMEM((1, fields, coarse_span, columns), f32), coarse_scratch(1)],
            *coarse_cost,
        )

    hop_pairs = [(d, d + 1) for d in range(sections - 1)]
    where_now = section.astype(jnp.int32).reshape(1)

    fine_end = None
    coarse_end = None
    for iteration in range(ITERS):
        if iteration == 0:
            node_prev, node_next = halo(nodes, rows)
        else:
            node_prev, node_next = swap(node_head, node_tail)
        f_all, a1, a1_head, a1_tail = call(
            nodes_kernel,
            (nodes, node_prev, node_next, lop_fine, xt) + scalars,
            (False,) * 5 + scalar_kinds,
            (jax.ShapeDtypeStruct((3, fields, span, columns), f32), fine_state, fine_plane,
             fine_plane),
            [fine_scratch(3)],
            fine_cost[0] * 3, fine_cost[1] * 3,
        )
        a1_prev, a1_next = swap(a1_head, a1_tail)
        g1, a2, a2_head, a2_tail = call(
            middle_kernel,
            (a1, a1_prev, a1_next, lop_fine, xt) + scalars + (f_all,),
            (False,) * 5 + scalar_kinds + (False,),
            (fine_state, fine_state, fine_plane, fine_plane),
            [fine_scratch(1)],
            *fine_cost,
        )
        a2_prev, a2_next = swap(a2_head, a2_tail)
        base, c0 = call(
            base_kernel,
            (nodes, node_prev, node_next, rmat, restrict_plane, lop_coarse, xt) + coarse_scalars,
            (False,) * 7 + scalar_kinds,
            (coarse_one, coarse_one),
            [pltpu.VMEM((1, fields, coarse_rows, columns), f32),
             pltpu.VMEM((1, fields, coarse_rows, columns), f32), coarse_scratch(1)],
            *coarse_cost,
        )
        base_all = lax.all_gather(base, "tm")
        rint, c1 = call(
            ending_kernel,
            (a2, a2_prev, a2_next, lop_fine, xt) + scalars + (f_all, g1, rmat),
            (False,) * 5 + scalar_kinds + (False,) * 3,
            (coarse_state, coarse_state),
            [pltpu.VMEM((1, fields, span, columns), f32), fine_scratch(1)],
            *fine_cost,
        )
        rint_all = lax.all_gather(rint[None], "tm")
        last = iteration + 1 == ITERS
        if not last:
            a2_handed = lax.ppermute(a2, "tm", hop_pairs)
        w = coarse_start[None]
        w_halo = (start_halo[0][None], start_halo[1][None])
        chain = [w]
        for n in range(sections):
            w, head, tail = coarse_step(w, w_halo, base_all[n], rint_all[n])
            chain.append(w)
            if n + 1 < sections:
                w_halo = swap(head, tail)
        if last:
            fine_end, coarse_end = call(
                finish_kernel,
                (a2, c1) + tuple(chain) + (pmat, where_now),
                (False,) * (3 + sections) + (False, True),
                (fine_state, coarse_one),
                [],
                2 * fields * span * coarse_span * columns * 6, 0,
            )
        else:
            nodes, node_head, node_tail = call(
                correct_kernel,
                (a1, a2, c0, c1) + tuple(chain) + (a2_handed, u_flat, rmat, pmat, lead, where_now),
                (False,) * (5 + sections) + (False,) * 4 + (True, True),
                (jax.ShapeDtypeStruct((3, fields, span, columns), f32), node_planes,
                 node_planes),
                [],
                8 * fields * span * coarse_span * columns * 6, 0,
            )
    fine_end = fine_end.reshape(1, fields, depth, rows, columns)
    coarse_end = coarse_end.reshape(1, fields, depth, coarse_rows, columns)
    return (fine_end, coarse_end)


def solution(mesh):
    return jax.shard_map(
        per_device,
        mesh=mesh,
        in_specs=(
            P(None, "space", None, None),
            P("tm", None, None, "space", None, None),
            P(),
            P(),
            P(),
            P(),
        ),
        out_specs=(P("tm", None, "space", None, None), P("tm", None, "space", None, None)),
        check_vma=False,
    )
```

```python
import jax
import jax.numpy as jnp
import numpy as np
from jax import lax
from jax.experimental import pallas as pl
from jax.experimental.pallas import tpu as pltpu
from jax.sharding import PartitionSpec as P

ITERS = 2


STEP = 0.01
HIGHEST = lax.Precision.HIGHEST
FINE_NODES = np.array(
    [
        -1.0,
        -0.8717401485096066,
        -0.5917001814331423,
        -0.2092992179024789,
        0.2092992179024789,
        0.5917001814331423,
        0.8717401485096066,
        1.0,
    ]
)
COARSE_NODES = np.array([-1.0, -0.4472135954999579, 0.4472135954999579, 1.0])


def lagrange_table(source, target):
    table = np.ones((len(target), len(source)))
    for j in range(len(source)):
        for m in range(len(source)):
            if m != j:
                table[:, j] *= (target - source[m]) / (source[j] - source[m])
    return table


def derivative_table(points):
    total = len(points)
    weights = np.array(
        [
            1.0 / np.prod([points[j] - points[m] for m in range(total) if m != j])
            for j in range(total)
        ]
    )
    table = np.zeros((total, total))
    for i in range(total):
        for j in range(total):
            if i != j:
                table[i, j] = weights[j] / weights[i] / (points[i] - points[j])
        table[i, i] = -np.sum(table[i])
    return table


def element_tables(length, table, lift):
    per_element = table.shape[0]
    block = np.kron(np.eye(length // per_element), table)
    position = np.arange(length) % per_element
    identity = np.eye(length)
    before = np.roll(identity, -1, axis=1)
    after = np.roll(identity, 1, axis=1)
    first_mask = np.where(position == 0, 1.0, 0.0)
    last_mask = np.where(position == per_element - 1, 1.0, 0.0)
    upwind = lift * first_mask[:, None] * (before - identity)
    downwind = lift * last_mask[:, None] * (after - identity)
    return (block, upwind, downwind)


def widen(matrix):
    length = matrix.shape[0]
    wider = np.zeros((length, matrix.shape[1] + 2))
    wider[:, 1:-1] = matrix
    return wider


def padded_tables(length, table, lift):
    block, upwind, downwind = element_tables(length, table, lift)
    block_wide = widen(block)
    upwind_wide = widen(upwind)
    downwind_wide = widen(downwind)
    upwind_wide[0, length] = 0.0
    upwind_wide[0, 0] = lift
    downwind_wide[length - 1, 1] = 0.0
    downwind_wide[length - 1, length + 1] = lift
    return (block_wide, upwind_wide, downwind_wide)


def field_operators(speed, tables):
    block = jnp.asarray(tables[0], jnp.float32)
    upwind = jnp.asarray(tables[1], jnp.float32)
    downwind = jnp.asarray(tables[2], jnp.float32)
    speeds = speed[:, None, None]
    return (
        -speeds * block + jnp.maximum(speeds, 0.0) * upwind + jnp.maximum(-speeds, 0.0) * downwind
    )


def speed_combination(speed, tables):
    block = jnp.asarray(tables[0], jnp.float32)[None]
    upwind = jnp.asarray(tables[1], jnp.float32)[None]
    downwind = jnp.asarray(tables[2], jnp.float32)[None]
    speeds = speed[:, None, None]
    return (
        -speeds * block + jnp.maximum(speeds, 0.0) * upwind + jnp.maximum(-speeds, 0.0) * downwind
    )


def dot(a, b):
    return jnp.dot(a, b, precision=HIGHEST, preferred_element_type=jnp.float32)


def tdot(a, b):
    return jnp.dot(a, b, precision=lax.Precision.HIGH, preferred_element_type=jnp.float32)


def lanes(parts):
    return jnp.concatenate(parts, axis=1)


def unlanes(wide, width):
    return [wide[:, i * width:(i + 1) * width] for i in range(wide.shape[1] // width)]


def tendency_into(out_ref, v_ref, prev_ref, next_ref, k_ref, d_ref, cf_ref, rx_ref,
                  rate_ref, en_ref, s_ref, y_elem):
    states, fields, span, columns = v_ref.shape
    rows = prev_ref.shape[2]
    planes = span // rows
    f32 = jnp.float32
    row = lax.broadcasted_iota(jnp.int32, (span, columns), 0)
    lane = lax.broadcasted_iota(jnp.int32, (span, columns), 1)
    yy = row % rows
    zz = row // rows
    x_first = lane % 8 == 0
    x_last = lane % 8 == 7
    y_first = yy % y_elem == 0
    y_last = yy % y_elem == y_elem - 1
    z_first = zz % 8 == 0
    z_last = zz % 8 == 7

    def scoped(xd_ref, yz_ref):
        for b in range(states):
            xd_ref[b] = tdot(v_ref[b].reshape(fields * span, columns), d_ref[...]).reshape(
                fields, span, columns)
            yz_ref[b] = tdot(k_ref[...], lanes([v_ref[b, f] for f in range(fields)]))
        for b in range(states):
            for f in range(fields):
                v = v_ref[b, f]
                cols = slice(f * columns, (f + 1) * columns)
                t = (cf_ref[0, f] * xd_ref[b, f] + cf_ref[1, f] * yz_ref[b, :span, cols]
                     + cf_ref[2, f] * yz_ref[b, span:, cols])
                before_x = pltpu.roll(v, 1, 1)
                after_x = pltpu.roll(v, columns - 1, 1)
                t = t + jnp.where(x_first, cf_ref[3, f] * (before_x - v), 0.0)
                t = t + jnp.where(x_last, cf_ref[4, f] * (after_x - v), 0.0)
                before_y = jnp.where(yy == 0, pltpu.roll(v, span - rows + 1, 0),
                                     pltpu.roll(v, 1, 0))
                after_y = jnp.where(yy == rows - 1, pltpu.roll(v, rows - 1, 0),
                                    pltpu.roll(v, span - 1, 0))
                t = t + jnp.where(y_first, cf_ref[5, f] * (before_y - v), 0.0)
                t = t + jnp.where(y_last, cf_ref[6, f] * (after_y - v), 0.0)
                if planes > 8:
                    before_z = pltpu.roll(v, rows, 0)
                    after_z = pltpu.roll(v, span - rows, 0)
                    t = t + jnp.where(z_first & (zz > 0), cf_ref[7, f] * before_z, 0.0)
                    t = t + jnp.where(z_last & (zz < planes - 1), cf_ref[8, f] * after_z, 0.0)
                t = t - jnp.where(z_first, cf_ref[7, f] * v, 0.0)
                t = t - jnp.where(z_last, cf_ref[8, f] * v, 0.0)
                out_ref[b, f] = t
                out_ref[b, f, pl.ds(0, rows), :] = (
                    out_ref[b, f, pl.ds(0, rows), :] + cf_ref[7, f] * prev_ref[b, f]
                )
                out_ref[b, f, pl.ds(span - rows, rows), :] = (
                    out_ref[b, f, pl.ds(span - rows, rows), :] + cf_ref[8, f] * next_ref[b, f]
                )
                s_ref[b, f] = jnp.tanh(v)

    pl.run_scoped(scoped, pltpu.VMEM((states, fields, span, columns), f32),
                  pltpu.VMEM((states, 2 * span, fields * columns), f32))
    for b in range(states):
        cooling = 1.0 / (1.5 + 0.5 * s_ref[b, fields - 1])

        def reaction_body(r, carry):
            first = rx_ref[r, 0]
            second = rx_ref[r, 1]
            product = rx_ref[r, 2]
            progress = (
                rate_ref[r] * jnp.exp(-en_ref[r] * cooling) * s_ref[b, first] * s_ref[b, second]
            )
            out_ref[b, product] = out_ref[b, product] + progress
            out_ref[b, first] = out_ref[b, first] - progress
            out_ref[b, second] = out_ref[b, second] - progress
            return carry

        lax.fori_loop(0, rx_ref.shape[0], reaction_body, 0)


def vmem():
    return pl.BlockSpec(memory_space=pltpu.VMEM)


def smem():
    return pl.BlockSpec(memory_space=pltpu.SMEM)


def tendency_cost(states, fields, span, columns, reactions):
    flops = states * fields * (2 * span * span * columns + 2 * span * columns * columns) * 6
    flops += states * span * columns * (8 * reactions + 4 * fields)
    trans = states * span * columns * (fields + 2 * reactions)
    return flops, trans


def call(kernel, ins, in_kinds, outs, scratch, flops, trans, blocks=None):
    nbytes = sum(int(np.prod(x.shape)) * 4 for x in ins) + sum(
        int(np.prod(o.shape)) * 4 for o in outs
    )
    return pl.pallas_call(
        kernel,
        out_shape=outs,
        in_specs=[
            (blocks[i] if blocks is not None and i in blocks else smem() if k else vmem())
            for i, k in enumerate(in_kinds)
        ],
        out_specs=tuple(vmem() for _ in outs),
        scratch_shapes=scratch,
        grid=() if blocks is None else (1,),
        cost_estimate=pl.CostEstimate(
            flops=int(flops), transcendentals=int(trans), bytes_accessed=int(nbytes)
        ),
    )(*ins)


def per_device(u_start, guess, velocity, rates, energies, reactions):
    fields, depth, rows, columns = u_start.shape
    coarse_rows = rows // 2
    span = depth * rows
    coarse_span = depth * coarse_rows
    reaction_count = rates.shape[0]
    fine_table = derivative_table(FINE_NODES)
    coarse_table = derivative_table(COARSE_NODES)
    fine_elem = len(FINE_NODES)
    coarse_elem = len(COARSE_NODES)
    xt = jnp.asarray(np.kron(np.eye(columns // fine_elem), fine_table).T, jnp.float32)
    z_block = np.kron(np.eye(depth // fine_elem), fine_table)

    def plane_operator(y_table, plane_rows):
        y_block = np.kron(np.eye(plane_rows // y_table.shape[0]), y_table)
        return jnp.asarray(
            np.concatenate([np.kron(np.eye(depth), y_block), np.kron(z_block, np.eye(plane_rows))]),
            jnp.float32,
        )

    lop_fine = plane_operator(fine_table, rows)
    lop_coarse = plane_operator(coarse_table, coarse_rows)

    def coefficients(y_lift):
        up = jnp.maximum(velocity, 0.0)
        down = jnp.maximum(-velocity, 0.0)
        return jnp.concatenate([
            -velocity,
            28.0 * up[0:1], 28.0 * down[0:1],
            y_lift * up[1:2], y_lift * down[1:2],
            28.0 * up[2:3], 28.0 * down[2:3],
        ])

    cf_fine = coefficients(28.0)
    cf_coarse = coefficients(6.0)
    restrict_rows = np.kron(np.eye(rows // 8), lagrange_table(FINE_NODES, COARSE_NODES))
    prolong_rows = np.kron(np.eye(rows // 8), lagrange_table(COARSE_NODES, FINE_NODES))
    rmat = jnp.asarray(np.kron(np.eye(depth), restrict_rows), jnp.float32)
    pmat = jnp.asarray(np.kron(np.eye(depth), prolong_rows), jnp.float32)
    restrict_plane = jnp.asarray(restrict_rows, jnp.float32)
    scalars = (cf_fine, reactions.astype(jnp.int32), rates, energies)
    coarse_scalars = (cf_coarse, reactions.astype(jnp.int32), rates, energies)
    scalar_kinds = (True, True, True, True)

    space_n = lax.axis_size("space")
    sections = lax.axis_size("tm")
    section = lax.axis_index("tm")
    lead = (section == 0).astype(jnp.int32).reshape(1)

    def halo(x, plane_rows):
        head = x[..., :plane_rows, :]
        tail = x[..., x.shape[-2] - plane_rows:, :]
        return swap(head, tail)

    def swap(head, tail):
        prev = lax.ppermute(tail, "space", [(i, (i + 1) % space_n) for i in range(space_n)])
        nxt = lax.ppermute(head, "space", [((i + 1) % space_n, i) for i in range(space_n)])
        return prev, nxt

    f32 = jnp.float32
    fine_state = jax.ShapeDtypeStruct((1, fields, span, columns), f32)
    coarse_state = jax.ShapeDtypeStruct((fields, coarse_span, columns), f32)

    def nodes_kernel(u_ref, p_ref, n_ref, l_ref, x_ref, zc_ref, rx_ref, ra_ref, en_ref,
                     f_ref, a1_ref, h_ref, t_ref, s_ref):
        tendency_into(f_ref, u_ref, p_ref, n_ref, l_ref, x_ref, zc_ref, rx_ref, ra_ref, en_ref,
                      s_ref, fine_elem)

        def body(f, carry):
            value = u_ref[0, f] + STEP * (
                5.0 * f_ref[0, f] + 8.0 * f_ref[1, f] - f_ref[2, f]
            ) / 24.0
            a1_ref[0, f] = value
            h_ref[0, f] = value[:rows]
            t_ref[0, f] = value[span - rows:]
            return carry

        lax.fori_loop(0, fields, body, 0)

    def middle_kernel(a1_ref, p_ref, n_ref, l_ref, x_ref, zc_ref, rx_ref, ra_ref, en_ref,
                      f_ref, g1_ref, a2_ref, h_ref, t_ref, s_ref):
        tendency_into(g1_ref, a1_ref, p_ref, n_ref, l_ref, x_ref, zc_ref, rx_ref, ra_ref,
                      en_ref, s_ref, fine_elem)

        def body(f, carry):
            value = (
                a1_ref[0, f]
                + 0.5 * STEP * (g1_ref[0, f] - f_ref[1, f])
                + STEP * (-f_ref[0, f] + 8.0 * f_ref[1, f] + 5.0 * f_ref[2, f]) / 24.0
            )
            a2_ref[0, f] = value
            h_ref[0, f] = value[:rows]
            t_ref[0, f] = value[span - rows:]
            return carry

        lax.fori_loop(0, fields, body, 0)

    def ending_kernel(a2_ref, p_ref, n_ref, l_ref, x_ref, zc_ref, rx_ref, ra_ref, en_ref,
                      f_ref, g1_ref, r_ref, rint_ref, c1_ref, g2_ref, s_ref):
        tendency_into(g2_ref, a2_ref, p_ref, n_ref, l_ref, x_ref, zc_ref, rx_ref, ra_ref,
                      en_ref, s_ref, fine_elem)

        def body(f, carry):
            g2_ref[0, f] = STEP * (f_ref[0, f] + 4.0 * g1_ref[0, f] + g2_ref[0, f]) / 6.0
            return carry

        lax.fori_loop(0, fields, body, 0)
        rm = r_ref[...]
        for dst, src_ref, lead_index in ((rint_ref, g2_ref, 0), (c1_ref, a2_ref, 0)):
            wide = dot(rm, lanes([src_ref[lead_index, f] for f in range(fields)]))
            for f, part in enumerate(unlanes(wide, columns)):
                dst[f] = part

    def base_kernel(u_ref, p_ref, n_ref, r_ref, rp_ref, l_ref, x_ref, zc_ref, rx_ref, ra_ref,
                    en_ref, out_ref, c0_ref, bp_ref, bn_ref, s_ref):
        for dst, src_ref, table in ((c0_ref, u_ref, r_ref), (bp_ref, p_ref, rp_ref),
                                    (bn_ref, n_ref, rp_ref)):
            wide = dot(table[...], lanes([src_ref[0, f] for f in range(fields)]))
            for f, part in enumerate(unlanes(wide, columns)):
                dst[0, f] = part
        tendency_into(out_ref, c0_ref, bp_ref, bn_ref, l_ref, x_ref, zc_ref, rx_ref, ra_ref,
                      en_ref, s_ref, coarse_elem)

    def chain_kernel(w_ref, p_ref, n_ref, l_ref, x_ref, zc_ref, rx_ref, ra_ref, en_ref,
                     base_ref, rint_ref, out_ref, h_ref, t_ref, g_ref, s_ref):
        tendency_into(g_ref, w_ref, p_ref, n_ref, l_ref, x_ref, zc_ref, rx_ref, ra_ref,
                      en_ref, s_ref, coarse_elem)

        def body(f, carry):
            value = w_ref[0, f] + STEP * (g_ref[0, f] - base_ref[0, 0, f]) + rint_ref[0, 0, f]
            out_ref[0, f] = value
            h_ref[0, f] = value[:coarse_rows]
            t_ref[0, f] = value[coarse_span - coarse_rows:]
            return carry

        lax.fori_loop(0, fields, body, 0)

    def pick(sec_ref, w_refs, f, offset):
        value = w_refs[offset][0, f]
        for n in range(1, sections):
            value = jnp.where(sec_ref[0] == n, w_refs[n + offset][0, f], value)
        return value

    def correct_kernel(*refs):
        a1_ref, a2_ref, c0_ref, c1_ref = refs[:4]
        w_refs = refs[4:5 + sections]
        prev_ref, us_ref, r_ref, pm_ref, lead_ref, sec_ref, out_ref, h_ref, t_ref = refs[
            5 + sections:]
        pm = pm_ref[...]
        w0 = [pick(sec_ref, w_refs, f, 0) for f in range(fields)]
        first_change = [w0[f] - c0_ref[0, f] for f in range(fields)]
        last_change = [pick(sec_ref, w_refs, f, 1) - c1_ref[f] for f in range(fields)]
        middle_fix = unlanes(
            dot(pm, lanes([0.5 * (first_change[f] + last_change[f]) for f in range(fields)])),
            columns,
        )
        last_fix = unlanes(dot(pm, lanes(last_change)), columns)
        handed = lanes([prev_ref[0, f] for f in range(fields)])
        handed_fix = unlanes(
            dot(pm, lanes(w0) - dot(r_ref[...], handed)),
            columns,
        )
        for f in range(fields):
            values = (
                jnp.where(lead_ref[0] != 0, us_ref[f], prev_ref[0, f] + handed_fix[f]),
                a1_ref[0, f] + middle_fix[f],
                a2_ref[0, f] + last_fix[f],
            )
            for b, value in enumerate(values):
                out_ref[b, f] = value
                h_ref[b, f] = value[:rows]
                t_ref[b, f] = value[span - rows:]

    def finish_kernel(*refs):
        a2_ref, c1_ref = refs[:2]
        w_refs = refs[2:3 + sections]
        pm_ref, sec_ref, out_ref, coarse_ref = refs[3 + sections:]
        w1 = [pick(sec_ref, w_refs, f, 1) for f in range(fields)]
        fix = unlanes(
            dot(pm_ref[...], lanes([w1[f] - c1_ref[f] for f in range(fields)])), columns
        )
        for f in range(fields):
            out_ref[0, f] = a2_ref[0, f] + fix[f]
            coarse_ref[0, f] = w1[f]

    fine_cost = tendency_cost(1, fields, span, columns, reaction_count)
    coarse_cost = tendency_cost(1, fields, coarse_span, columns, reaction_count)

    def fine_scratch(states):
        return pltpu.VMEM((states, fields, span, columns), f32)

    def coarse_scratch(states):
        return pltpu.VMEM((states, fields, coarse_span, columns), f32)

    u_flat = u_start.reshape(fields, span, columns)
    nodes = guess[0].reshape(3, fields, span, columns)
    nodes = jnp.concatenate([jnp.where(section == 0, u_flat, nodes[0])[None], nodes[1:]], axis=0)
    coarse_start = jnp.einsum("cy,fzyx->fzcx", restrict_plane,
                              u_start, precision=HIGHEST).reshape(fields, coarse_span, columns)
    start_halo = halo(coarse_start, coarse_rows)

    coarse_one = jax.ShapeDtypeStruct((1, fields, coarse_span, columns), f32)
    plane_one = jax.ShapeDtypeStruct((1, fields, coarse_rows, columns), f32)
    fine_plane = jax.ShapeDtypeStruct((1, fields, rows, columns), f32)
    node_planes = jax.ShapeDtypeStruct((3, fields, rows, columns), f32)

    def coarse_step(w, w_halo, base_all, rint_all, n):
        def section_block():
            return pl.BlockSpec((1, 1, fields, coarse_span, columns), lambda i: (n, 0, 0, 0, 0),
                                memory_space=pltpu.VMEM)

        return call(
            chain_kernel,
            (w, w_halo[0], w_halo[1], lop_coarse, xt) + coarse_scalars + (base_all, rint_all),
            (False,) * 5 + scalar_kinds + (False, False),
            (coarse_one, plane_one, plane_one),
            [pltpu.VMEM((1, fields, coarse_span, columns), f32), coarse_scratch(1)],
            *coarse_cost,
            blocks={9: section_block(), 10: section_block()},
        )

    hop_pairs = [(d, d + 1) for d in range(sections - 1)]
    where_now = section.astype(jnp.int32).reshape(1)

    fine_end = None
    coarse_end = None
    for iteration in range(ITERS):
        if iteration == 0:
            node_prev, node_next = halo(nodes, rows)
        else:
            node_prev, node_next = swap(node_head, node_tail)
        f_all, a1, a1_head, a1_tail = call(
            nodes_kernel,
            (nodes, node_prev, node_next, lop_fine, xt) + scalars,
            (False,) * 5 + scalar_kinds,
            (jax.ShapeDtypeStruct((3, fields, span, columns), f32), fine_state, fine_plane,
             fine_plane),
            [fine_scratch(3)],
            fine_cost[0] * 3, fine_cost[1] * 3,
        )
        a1_prev, a1_next = swap(a1_head, a1_tail)
        g1, a2, a2_head, a2_tail = call(
            middle_kernel,
            (a1, a1_prev, a1_next, lop_fine, xt) + scalars + (f_all,),
            (False,) * 5 + scalar_kinds + (False,),
            (fine_state, fine_state, fine_plane, fine_plane),
            [fine_scratch(1)],
            *fine_cost,
        )
        a2_prev, a2_next = swap(a2_head, a2_tail)
        base, c0 = call(
            base_kernel,
            (nodes, node_prev, node_next, rmat, restrict_plane, lop_coarse, xt) + coarse_scalars,
            (False,) * 7 + scalar_kinds,
            (coarse_one, coarse_one),
            [pltpu.VMEM((1, fields, coarse_rows, columns), f32),
             pltpu.VMEM((1, fields, coarse_rows, columns), f32), coarse_scratch(1)],
            *coarse_cost,
        )
        base_all = lax.all_gather(base, "tm")
        rint, c1 = call(
            ending_kernel,
            (a2, a2_prev, a2_next, lop_fine, xt) + scalars + (f_all, g1, rmat),
            (False,) * 5 + scalar_kinds + (False,) * 3,
            (coarse_state, coarse_state),
            [pltpu.VMEM((1, fields, span, columns), f32), fine_scratch(1)],
            *fine_cost,
        )
        rint_all = lax.all_gather(rint[None], "tm")
        last = iteration + 1 == ITERS
        if not last:
            a2_handed = lax.ppermute(a2, "tm", hop_pairs)
        w = coarse_start[None]
        w_halo = (start_halo[0][None], start_halo[1][None])
        chain = [w]
        for n in range(sections):
            w, head, tail = coarse_step(w, w_halo, base_all, rint_all, n)
            chain.append(w)
            if n + 1 < sections:
                w_halo = swap(head, tail)
        if last:
            fine_end, coarse_end = call(
                finish_kernel,
                (a2, c1) + tuple(chain) + (pmat, where_now),
                (False,) * (3 + sections) + (False, True),
                (fine_state, coarse_one),
                [],
                2 * fields * span * coarse_span * columns * 6, 0,
            )
        else:
            nodes, node_head, node_tail = call(
                correct_kernel,
                (a1, a2, c0, c1) + tuple(chain) + (a2_handed, u_flat, rmat, pmat, lead, where_now),
                (False,) * (5 + sections) + (False,) * 4 + (True, True),
                (jax.ShapeDtypeStruct((3, fields, span, columns), f32), node_planes,
                 node_planes),
                [],
                8 * fields * span * coarse_span * columns * 6, 0,
            )
    fine_end = fine_end.reshape(1, fields, depth, rows, columns)
    coarse_end = coarse_end.reshape(1, fields, depth, coarse_rows, columns)
    return (fine_end, coarse_end)


def solution(mesh):
    return jax.shard_map(
        per_device,
        mesh=mesh,
        in_specs=(
            P(None, "space", None, None),
            P("tm", None, None, "space", None, None),
            P(),
            P(),
            P(),
            P(),
        ),
        out_specs=(P("tm", None, "space", None, None), P("tm", None, "space", None, None)),
        check_vma=False,
    )
```

```python
import jax
import jax.numpy as jnp
import numpy as np
from jax import lax
from jax.experimental import pallas as pl
from jax.experimental.pallas import tpu as pltpu
from jax.sharding import PartitionSpec as P

ITERS = 2


STEP = 0.01
HIGHEST = lax.Precision.HIGHEST
FINE_NODES = np.array(
    [
        -1.0,
        -0.8717401485096066,
        -0.5917001814331423,
        -0.2092992179024789,
        0.2092992179024789,
        0.5917001814331423,
        0.8717401485096066,
        1.0,
    ]
)
COARSE_NODES = np.array([-1.0, -0.4472135954999579, 0.4472135954999579, 1.0])


def lagrange_table(source, target):
    table = np.ones((len(target), len(source)))
    for j in range(len(source)):
        for m in range(len(source)):
            if m != j:
                table[:, j] *= (target - source[m]) / (source[j] - source[m])
    return table


def derivative_table(points):
    total = len(points)
    weights = np.array(
        [
            1.0 / np.prod([points[j] - points[m] for m in range(total) if m != j])
            for j in range(total)
        ]
    )
    table = np.zeros((total, total))
    for i in range(total):
        for j in range(total):
            if i != j:
                table[i, j] = weights[j] / weights[i] / (points[i] - points[j])
        table[i, i] = -np.sum(table[i])
    return table


def element_tables(length, table, lift):
    per_element = table.shape[0]
    block = np.kron(np.eye(length // per_element), table)
    position = np.arange(length) % per_element
    identity = np.eye(length)
    before = np.roll(identity, -1, axis=1)
    after = np.roll(identity, 1, axis=1)
    first_mask = np.where(position == 0, 1.0, 0.0)
    last_mask = np.where(position == per_element - 1, 1.0, 0.0)
    upwind = lift * first_mask[:, None] * (before - identity)
    downwind = lift * last_mask[:, None] * (after - identity)
    return (block, upwind, downwind)


def widen(matrix):
    length = matrix.shape[0]
    wider = np.zeros((length, matrix.shape[1] + 2))
    wider[:, 1:-1] = matrix
    return wider


def padded_tables(length, table, lift):
    block, upwind, downwind = element_tables(length, table, lift)
    block_wide = widen(block)
    upwind_wide = widen(upwind)
    downwind_wide = widen(downwind)
    upwind_wide[0, length] = 0.0
    upwind_wide[0, 0] = lift
    downwind_wide[length - 1, 1] = 0.0
    downwind_wide[length - 1, length + 1] = lift
    return (block_wide, upwind_wide, downwind_wide)


def field_operators(speed, tables):
    block = jnp.asarray(tables[0], jnp.float32)
    upwind = jnp.asarray(tables[1], jnp.float32)
    downwind = jnp.asarray(tables[2], jnp.float32)
    speeds = speed[:, None, None]
    return (
        -speeds * block + jnp.maximum(speeds, 0.0) * upwind + jnp.maximum(-speeds, 0.0) * downwind
    )


def speed_combination(speed, tables):
    block = jnp.asarray(tables[0], jnp.float32)[None]
    upwind = jnp.asarray(tables[1], jnp.float32)[None]
    downwind = jnp.asarray(tables[2], jnp.float32)[None]
    speeds = speed[:, None, None]
    return (
        -speeds * block + jnp.maximum(speeds, 0.0) * upwind + jnp.maximum(-speeds, 0.0) * downwind
    )


def dot(a, b):
    return jnp.dot(a, b, precision=HIGHEST, preferred_element_type=jnp.float32)


def tdot(a, b):
    return jnp.dot(a, b, precision=lax.Precision.HIGH, preferred_element_type=jnp.float32)


def lanes(parts):
    return jnp.concatenate(parts, axis=1)


def unlanes(wide, width):
    return [wide[:, i * width:(i + 1) * width] for i in range(wide.shape[1] // width)]


def tendency_into(out_ref, v_ref, prev_ref, next_ref, k_ref, d_ref, cf_ref, rx_ref,
                  rate_ref, en_ref, s_ref, y_elem):
    states, fields, span, columns = v_ref.shape
    rows = prev_ref.shape[2]
    planes = span // rows
    f32 = jnp.float32
    row = lax.broadcasted_iota(jnp.int32, (span, columns), 0)
    lane = lax.broadcasted_iota(jnp.int32, (span, columns), 1)
    yy = row % rows
    zz = row // rows
    x_first = lane % 8 == 0
    x_last = lane % 8 == 7
    y_first = yy % y_elem == 0
    y_last = yy % y_elem == y_elem - 1
    z_first = zz % 8 == 0
    z_last = zz % 8 == 7

    def scoped(xd_ref, yz_ref):
        for b in range(states):
            xd_ref[b] = tdot(v_ref[b].reshape(fields * span, columns), d_ref[...]).reshape(
                fields, span, columns)
            yz_ref[b] = tdot(k_ref[...], lanes([v_ref[b, f] for f in range(fields)]))
        for b in range(states):
            for f in range(fields):
                v = v_ref[b, f]
                cols = slice(f * columns, (f + 1) * columns)
                t = (cf_ref[0, f] * xd_ref[b, f] + cf_ref[1, f] * yz_ref[b, :span, cols]
                     + cf_ref[2, f] * yz_ref[b, span:, cols])
                before_x = pltpu.roll(v, 1, 1)
                after_x = pltpu.roll(v, columns - 1, 1)
                t = t + jnp.where(x_first, cf_ref[3, f] * (before_x - v), 0.0)
                t = t + jnp.where(x_last, cf_ref[4, f] * (after_x - v), 0.0)
                before_y = jnp.where(yy == 0, pltpu.roll(v, span - rows + 1, 0),
                                     pltpu.roll(v, 1, 0))
                after_y = jnp.where(yy == rows - 1, pltpu.roll(v, rows - 1, 0),
                                    pltpu.roll(v, span - 1, 0))
                t = t + jnp.where(y_first, cf_ref[5, f] * (before_y - v), 0.0)
                t = t + jnp.where(y_last, cf_ref[6, f] * (after_y - v), 0.0)
                if planes > 8:
                    before_z = pltpu.roll(v, rows, 0)
                    after_z = pltpu.roll(v, span - rows, 0)
                    t = t + jnp.where(z_first & (zz > 0), cf_ref[7, f] * before_z, 0.0)
                    t = t + jnp.where(z_last & (zz < planes - 1), cf_ref[8, f] * after_z, 0.0)
                t = t - jnp.where(z_first, cf_ref[7, f] * v, 0.0)
                t = t - jnp.where(z_last, cf_ref[8, f] * v, 0.0)
                out_ref[b, f] = t
                out_ref[b, f, pl.ds(0, rows), :] = (
                    out_ref[b, f, pl.ds(0, rows), :] + cf_ref[7, f] * prev_ref[b, f]
                )
                out_ref[b, f, pl.ds(span - rows, rows), :] = (
                    out_ref[b, f, pl.ds(span - rows, rows), :] + cf_ref[8, f] * next_ref[b, f]
                )
                s_ref[b, f] = jnp.tanh(v)

    pl.run_scoped(scoped, pltpu.VMEM((states, fields, span, columns), f32),
                  pltpu.VMEM((states, 2 * span, fields * columns), f32))
    for b in range(states):
        cooling = 1.0 / (1.5 + 0.5 * s_ref[b, fields - 1])

        def reaction_body(r, carry):
            first = rx_ref[r, 0]
            second = rx_ref[r, 1]
            product = rx_ref[r, 2]
            progress = (
                rate_ref[r] * jnp.exp(-en_ref[r] * cooling) * s_ref[b, first] * s_ref[b, second]
            )
            out_ref[b, product] = out_ref[b, product] + progress
            out_ref[b, first] = out_ref[b, first] - progress
            out_ref[b, second] = out_ref[b, second] - progress
            return carry

        lax.fori_loop(0, rx_ref.shape[0], reaction_body, 0)


def vmem():
    return pl.BlockSpec(memory_space=pltpu.VMEM)


def smem():
    return pl.BlockSpec(memory_space=pltpu.SMEM)


def tendency_cost(states, fields, span, columns, reactions):
    flops = states * fields * (2 * span * span * columns + 2 * span * columns * columns) * 6
    flops += states * span * columns * (8 * reactions + 4 * fields)
    trans = states * span * columns * (fields + 2 * reactions)
    return flops, trans


def call(kernel, ins, in_kinds, outs, scratch, flops, trans, blocks=None):
    nbytes = sum(int(np.prod(x.shape)) * 4 for x in ins) + sum(
        int(np.prod(o.shape)) * 4 for o in outs
    )
    return pl.pallas_call(
        kernel,
        out_shape=outs,
        in_specs=[
            (blocks[i] if blocks is not None and i in blocks else smem() if k else vmem())
            for i, k in enumerate(in_kinds)
        ],
        out_specs=tuple(vmem() for _ in outs),
        scratch_shapes=scratch,
        grid=() if blocks is None else (1,),
        cost_estimate=pl.CostEstimate(
            flops=int(flops), transcendentals=int(trans), bytes_accessed=int(nbytes)
        ),
    )(*ins)


def per_device(u_start, guess, velocity, rates, energies, reactions):
    fields, depth, rows, columns = u_start.shape
    coarse_rows = rows // 2
    span = depth * rows
    coarse_span = depth * coarse_rows
    reaction_count = rates.shape[0]
    fine_table = derivative_table(FINE_NODES)
    coarse_table = derivative_table(COARSE_NODES)
    fine_elem = len(FINE_NODES)
    coarse_elem = len(COARSE_NODES)
    xt = jnp.asarray(np.kron(np.eye(columns // fine_elem), fine_table).T, jnp.float32)
    z_block = np.kron(np.eye(depth // fine_elem), fine_table)

    def plane_operator(y_table, plane_rows):
        y_block = np.kron(np.eye(plane_rows // y_table.shape[0]), y_table)
        return jnp.asarray(
            np.concatenate([np.kron(np.eye(depth), y_block), np.kron(z_block, np.eye(plane_rows))]),
            jnp.float32,
        )

    lop_fine = plane_operator(fine_table, rows)
    lop_coarse = plane_operator(coarse_table, coarse_rows)

    def coefficients(y_lift):
        up = jnp.maximum(velocity, 0.0)
        down = jnp.maximum(-velocity, 0.0)
        return jnp.concatenate([
            -velocity,
            28.0 * up[0:1], 28.0 * down[0:1],
            y_lift * up[1:2], y_lift * down[1:2],
            28.0 * up[2:3], 28.0 * down[2:3],
        ])

    cf_fine = coefficients(28.0)
    cf_coarse = coefficients(6.0)
    restrict_rows = np.kron(np.eye(rows // 8), lagrange_table(FINE_NODES, COARSE_NODES))
    prolong_rows = np.kron(np.eye(rows // 8), lagrange_table(COARSE_NODES, FINE_NODES))
    rmat = jnp.asarray(np.kron(np.eye(depth), restrict_rows), jnp.float32)
    pmat = jnp.asarray(np.kron(np.eye(depth), prolong_rows), jnp.float32)
    restrict_plane = jnp.asarray(restrict_rows, jnp.float32)
    scalars = (cf_fine, reactions.astype(jnp.int32), rates, energies)
    coarse_scalars = (cf_coarse, reactions.astype(jnp.int32), rates, energies)
    scalar_kinds = (True, True, True, True)

    space_n = lax.axis_size("space")
    sections = lax.axis_size("tm")
    section = lax.axis_index("tm")
    lead = (section == 0).astype(jnp.int32).reshape(1)

    def halo(x, plane_rows):
        head = x[..., :plane_rows, :]
        tail = x[..., x.shape[-2] - plane_rows:, :]
        return swap(head, tail)

    def swap(head, tail):
        prev = lax.ppermute(tail, "space", [(i, (i + 1) % space_n) for i in range(space_n)])
        nxt = lax.ppermute(head, "space", [((i + 1) % space_n, i) for i in range(space_n)])
        return prev, nxt

    f32 = jnp.float32
    fine_state = jax.ShapeDtypeStruct((1, fields, span, columns), f32)
    coarse_state = jax.ShapeDtypeStruct((fields, coarse_span, columns), f32)

    def nodes_kernel(u_ref, p_ref, n_ref, l_ref, x_ref, zc_ref, rx_ref, ra_ref, en_ref,
                     f_ref, a1_ref, h_ref, t_ref, s_ref):
        tendency_into(f_ref, u_ref, p_ref, n_ref, l_ref, x_ref, zc_ref, rx_ref, ra_ref, en_ref,
                      s_ref, fine_elem)

        def body(f, carry):
            value = u_ref[0, f] + STEP * (
                5.0 * f_ref[0, f] + 8.0 * f_ref[1, f] - f_ref[2, f]
            ) / 24.0
            a1_ref[0, f] = value
            h_ref[0, f] = value[:rows]
            t_ref[0, f] = value[span - rows:]
            return carry

        lax.fori_loop(0, fields, body, 0)

    def middle_kernel(a1_ref, p_ref, n_ref, l_ref, x_ref, zc_ref, rx_ref, ra_ref, en_ref,
                      f_ref, g1_ref, a2_ref, h_ref, t_ref, s_ref):
        tendency_into(g1_ref, a1_ref, p_ref, n_ref, l_ref, x_ref, zc_ref, rx_ref, ra_ref,
                      en_ref, s_ref, fine_elem)

        def body(f, carry):
            value = (
                a1_ref[0, f]
                + 0.5 * STEP * (g1_ref[0, f] - f_ref[1, f])
                + STEP * (-f_ref[0, f] + 8.0 * f_ref[1, f] + 5.0 * f_ref[2, f]) / 24.0
            )
            a2_ref[0, f] = value
            h_ref[0, f] = value[:rows]
            t_ref[0, f] = value[span - rows:]
            return carry

        lax.fori_loop(0, fields, body, 0)

    def ending_kernel(a2_ref, p_ref, n_ref, l_ref, x_ref, zc_ref, rx_ref, ra_ref, en_ref,
                      f_ref, g1_ref, r_ref, base_ref, rint_ref, c1_ref, g2_ref, s_ref):
        tendency_into(g2_ref, a2_ref, p_ref, n_ref, l_ref, x_ref, zc_ref, rx_ref, ra_ref,
                      en_ref, s_ref, fine_elem)

        def body(f, carry):
            g2_ref[0, f] = STEP * (f_ref[0, f] + 4.0 * g1_ref[0, f] + g2_ref[0, f]) / 6.0
            return carry

        lax.fori_loop(0, fields, body, 0)
        rm = r_ref[...]
        for dst, src_ref, lead_index in ((rint_ref, g2_ref, 0), (c1_ref, a2_ref, 0)):
            wide = dot(rm, lanes([src_ref[lead_index, f] for f in range(fields)]))
            for f, part in enumerate(unlanes(wide, columns)):
                dst[f] = part
        for f in range(fields):
            rint_ref[f] = rint_ref[f] - STEP * base_ref[0, f]

    def base_kernel(u_ref, p_ref, n_ref, r_ref, rp_ref, l_ref, x_ref, zc_ref, rx_ref, ra_ref,
                    en_ref, out_ref, c0_ref, bp_ref, bn_ref, s_ref):
        for dst, src_ref, table in ((c0_ref, u_ref, r_ref), (bp_ref, p_ref, rp_ref),
                                    (bn_ref, n_ref, rp_ref)):
            wide = dot(table[...], lanes([src_ref[0, f] for f in range(fields)]))
            for f, part in enumerate(unlanes(wide, columns)):
                dst[0, f] = part
        tendency_into(out_ref, c0_ref, bp_ref, bn_ref, l_ref, x_ref, zc_ref, rx_ref, ra_ref,
                      en_ref, s_ref, coarse_elem)

    def chain_kernel(w_ref, p_ref, n_ref, l_ref, x_ref, zc_ref, rx_ref, ra_ref, en_ref,
                     rint_ref, out_ref, h_ref, t_ref, g_ref, s_ref):
        tendency_into(g_ref, w_ref, p_ref, n_ref, l_ref, x_ref, zc_ref, rx_ref, ra_ref,
                      en_ref, s_ref, coarse_elem)

        def body(f, carry):
            value = w_ref[0, f] + STEP * g_ref[0, f] + rint_ref[0, 0, f]
            out_ref[0, f] = value
            h_ref[0, f] = value[:coarse_rows]
            t_ref[0, f] = value[coarse_span - coarse_rows:]
            return carry

        lax.fori_loop(0, fields, body, 0)

    def pick(sec_ref, w_refs, f, offset):
        value = w_refs[offset][0, f]
        for n in range(1, sections):
            value = jnp.where(sec_ref[0] == n, w_refs[n + offset][0, f], value)
        return value

    def correct_kernel(*refs):
        a1_ref, a2_ref, c0_ref, c1_ref = refs[:4]
        w_refs = refs[4:5 + sections]
        prev_ref, us_ref, r_ref, pm_ref, lead_ref, sec_ref, out_ref, h_ref, t_ref = refs[
            5 + sections:]
        pm = pm_ref[...]
        w0 = [pick(sec_ref, w_refs, f, 0) for f in range(fields)]
        first_change = [w0[f] - c0_ref[0, f] for f in range(fields)]
        last_change = [pick(sec_ref, w_refs, f, 1) - c1_ref[f] for f in range(fields)]
        middle_fix = unlanes(
            dot(pm, lanes([0.5 * (first_change[f] + last_change[f]) for f in range(fields)])),
            columns,
        )
        last_fix = unlanes(dot(pm, lanes(last_change)), columns)
        handed = lanes([prev_ref[0, f] for f in range(fields)])
        handed_fix = unlanes(
            dot(pm, lanes(w0) - dot(r_ref[...], handed)),
            columns,
        )
        for f in range(fields):
            values = (
                jnp.where(lead_ref[0] != 0, us_ref[f], prev_ref[0, f] + handed_fix[f]),
                a1_ref[0, f] + middle_fix[f],
                a2_ref[0, f] + last_fix[f],
            )
            for b, value in enumerate(values):
                out_ref[b, f] = value
                h_ref[b, f] = value[:rows]
                t_ref[b, f] = value[span - rows:]

    def finish_kernel(*refs):
        a2_ref, c1_ref = refs[:2]
        w_refs = refs[2:3 + sections]
        pm_ref, sec_ref, out_ref, coarse_ref = refs[3 + sections:]
        w1 = [pick(sec_ref, w_refs, f, 1) for f in range(fields)]
        fix = unlanes(
            dot(pm_ref[...], lanes([w1[f] - c1_ref[f] for f in range(fields)])), columns
        )
        for f in range(fields):
            out_ref[0, f] = a2_ref[0, f] + fix[f]
            coarse_ref[0, f] = w1[f]

    fine_cost = tendency_cost(1, fields, span, columns, reaction_count)
    coarse_cost = tendency_cost(1, fields, coarse_span, columns, reaction_count)

    def fine_scratch(states):
        return pltpu.VMEM((states, fields, span, columns), f32)

    def coarse_scratch(states):
        return pltpu.VMEM((states, fields, coarse_span, columns), f32)

    u_flat = u_start.reshape(fields, span, columns)
    nodes = guess[0].reshape(3, fields, span, columns)
    nodes = jnp.concatenate([jnp.where(section == 0, u_flat, nodes[0])[None], nodes[1:]], axis=0)
    coarse_start = jnp.einsum("cy,fzyx->fzcx", restrict_plane,
                              u_start, precision=HIGHEST).reshape(fields, coarse_span, columns)
    start_halo = halo(coarse_start, coarse_rows)

    coarse_one = jax.ShapeDtypeStruct((1, fields, coarse_span, columns), f32)
    plane_one = jax.ShapeDtypeStruct((1, fields, coarse_rows, columns), f32)
    fine_plane = jax.ShapeDtypeStruct((1, fields, rows, columns), f32)
    node_planes = jax.ShapeDtypeStruct((3, fields, rows, columns), f32)

    def coarse_step(w, w_halo, rint_all, n):
        def section_block():
            return pl.BlockSpec((1, 1, fields, coarse_span, columns), lambda i: (n, 0, 0, 0, 0),
                                memory_space=pltpu.VMEM)

        return call(
            chain_kernel,
            (w, w_halo[0], w_halo[1], lop_coarse, xt) + coarse_scalars + (rint_all,),
            (False,) * 5 + scalar_kinds + (False,),
            (coarse_one, plane_one, plane_one),
            [pltpu.VMEM((1, fields, coarse_span, columns), f32), coarse_scratch(1)],
            *coarse_cost,
            blocks={9: section_block()},
        )

    hop_pairs = [(d, d + 1) for d in range(sections - 1)]
    where_now = section.astype(jnp.int32).reshape(1)

    fine_end = None
    coarse_end = None
    for iteration in range(ITERS):
        if iteration == 0:
            node_prev, node_next = halo(nodes, rows)
        else:
            node_prev, node_next = swap(node_head, node_tail)
        f_all, a1, a1_head, a1_tail = call(
            nodes_kernel,
            (nodes, node_prev, node_next, lop_fine, xt) + scalars,
            (False,) * 5 + scalar_kinds,
            (jax.ShapeDtypeStruct((3, fields, span, columns), f32), fine_state, fine_plane,
             fine_plane),
            [fine_scratch(3)],
            fine_cost[0] * 3, fine_cost[1] * 3,
        )
        a1_prev, a1_next = swap(a1_head, a1_tail)
        g1, a2, a2_head, a2_tail = call(
            middle_kernel,
            (a1, a1_prev, a1_next, lop_fine, xt) + scalars + (f_all,),
            (False,) * 5 + scalar_kinds + (False,),
            (fine_state, fine_state, fine_plane, fine_plane),
            [fine_scratch(1)],
            *fine_cost,
        )
        a2_prev, a2_next = swap(a2_head, a2_tail)
        base, c0 = call(
            base_kernel,
            (nodes, node_prev, node_next, rmat, restrict_plane, lop_coarse, xt) + coarse_scalars,
            (False,) * 7 + scalar_kinds,
            (coarse_one, coarse_one),
            [pltpu.VMEM((1, fields, coarse_rows, columns), f32),
             pltpu.VMEM((1, fields, coarse_rows, columns), f32), coarse_scratch(1)],
            *coarse_cost,
        )
        rint, c1 = call(
            ending_kernel,
            (a2, a2_prev, a2_next, lop_fine, xt) + scalars + (f_all, g1, rmat, base),
            (False,) * 5 + scalar_kinds + (False,) * 4,
            (coarse_state, coarse_state),
            [pltpu.VMEM((1, fields, span, columns), f32), fine_scratch(1)],
            *fine_cost,
        )
        rint_all = lax.all_gather(rint[None], "tm")
        last = iteration + 1 == ITERS
        if not last:
            a2_handed = lax.ppermute(a2, "tm", hop_pairs)
        w = coarse_start[None]
        w_halo = (start_halo[0][None], start_halo[1][None])
        chain = [w]
        for n in range(sections):
            w, head, tail = coarse_step(w, w_halo, rint_all, n)
            chain.append(w)
            if n + 1 < sections:
                w_halo = swap(head, tail)
        if last:
            fine_end, coarse_end = call(
                finish_kernel,
                (a2, c1) + tuple(chain) + (pmat, where_now),
                (False,) * (3 + sections) + (False, True),
                (fine_state, coarse_one),
                [],
                2 * fields * span * coarse_span * columns * 6, 0,
            )
        else:
            nodes, node_head, node_tail = call(
                correct_kernel,
                (a1, a2, c0, c1) + tuple(chain) + (a2_handed, u_flat, rmat, pmat, lead, where_now),
                (False,) * (5 + sections) + (False,) * 4 + (True, True),
                (jax.ShapeDtypeStruct((3, fields, span, columns), f32), node_planes,
                 node_planes),
                [],
                8 * fields * span * coarse_span * columns * 6, 0,
            )
    fine_end = fine_end.reshape(1, fields, depth, rows, columns)
    coarse_end = coarse_end.reshape(1, fields, depth, coarse_rows, columns)
    return (fine_end, coarse_end)


def solution(mesh):
    return jax.shard_map(
        per_device,
        mesh=mesh,
        in_specs=(
            P(None, "space", None, None),
            P("tm", None, None, "space", None, None),
            P(),
            P(),
            P(),
            P(),
        ),
        out_specs=(P("tm", None, "space", None, None), P("tm", None, "space", None, None)),
        check_vma=False,
    )
```

```python
import jax
import jax.numpy as jnp
import numpy as np
from jax import lax
from jax.experimental import pallas as pl
from jax.experimental.pallas import tpu as pltpu
from jax.sharding import PartitionSpec as P

ITERS = 2


STEP = 0.01
HIGHEST = lax.Precision.HIGHEST
FINE_NODES = np.array(
    [
        -1.0,
        -0.8717401485096066,
        -0.5917001814331423,
        -0.2092992179024789,
        0.2092992179024789,
        0.5917001814331423,
        0.8717401485096066,
        1.0,
    ]
)
COARSE_NODES = np.array([-1.0, -0.4472135954999579, 0.4472135954999579, 1.0])


def lagrange_table(source, target):
    table = np.ones((len(target), len(source)))
    for j in range(len(source)):
        for m in range(len(source)):
            if m != j:
                table[:, j] *= (target - source[m]) / (source[j] - source[m])
    return table


def derivative_table(points):
    total = len(points)
    weights = np.array(
        [
            1.0 / np.prod([points[j] - points[m] for m in range(total) if m != j])
            for j in range(total)
        ]
    )
    table = np.zeros((total, total))
    for i in range(total):
        for j in range(total):
            if i != j:
                table[i, j] = weights[j] / weights[i] / (points[i] - points[j])
        table[i, i] = -np.sum(table[i])
    return table


def element_tables(length, table, lift):
    per_element = table.shape[0]
    block = np.kron(np.eye(length // per_element), table)
    position = np.arange(length) % per_element
    identity = np.eye(length)
    before = np.roll(identity, -1, axis=1)
    after = np.roll(identity, 1, axis=1)
    first_mask = np.where(position == 0, 1.0, 0.0)
    last_mask = np.where(position == per_element - 1, 1.0, 0.0)
    upwind = lift * first_mask[:, None] * (before - identity)
    downwind = lift * last_mask[:, None] * (after - identity)
    return (block, upwind, downwind)


def widen(matrix):
    length = matrix.shape[0]
    wider = np.zeros((length, matrix.shape[1] + 2))
    wider[:, 1:-1] = matrix
    return wider


def padded_tables(length, table, lift):
    block, upwind, downwind = element_tables(length, table, lift)
    block_wide = widen(block)
    upwind_wide = widen(upwind)
    downwind_wide = widen(downwind)
    upwind_wide[0, length] = 0.0
    upwind_wide[0, 0] = lift
    downwind_wide[length - 1, 1] = 0.0
    downwind_wide[length - 1, length + 1] = lift
    return (block_wide, upwind_wide, downwind_wide)


def field_operators(speed, tables):
    block = jnp.asarray(tables[0], jnp.float32)
    upwind = jnp.asarray(tables[1], jnp.float32)
    downwind = jnp.asarray(tables[2], jnp.float32)
    speeds = speed[:, None, None]
    return (
        -speeds * block + jnp.maximum(speeds, 0.0) * upwind + jnp.maximum(-speeds, 0.0) * downwind
    )


def speed_combination(speed, tables):
    block = jnp.asarray(tables[0], jnp.float32)[None]
    upwind = jnp.asarray(tables[1], jnp.float32)[None]
    downwind = jnp.asarray(tables[2], jnp.float32)[None]
    speeds = speed[:, None, None]
    return (
        -speeds * block + jnp.maximum(speeds, 0.0) * upwind + jnp.maximum(-speeds, 0.0) * downwind
    )


def dot(a, b):
    return jnp.dot(a, b, precision=HIGHEST, preferred_element_type=jnp.float32)


def tdot(a, b):
    return jnp.dot(a, b, precision=lax.Precision.HIGH, preferred_element_type=jnp.float32)


def lanes(parts):
    return jnp.concatenate(parts, axis=1)


def unlanes(wide, width):
    return [wide[:, i * width:(i + 1) * width] for i in range(wide.shape[1] // width)]


def tendency_into(out_ref, v_ref, prev_ref, next_ref, k_ref, d_ref, cf_ref, rx_ref,
                  rate_ref, en_ref, s_ref, y_elem):
    states, fields, span, columns = v_ref.shape
    rows = prev_ref.shape[2]
    planes = span // rows
    f32 = jnp.float32
    row = lax.broadcasted_iota(jnp.int32, (span, columns), 0)
    lane = lax.broadcasted_iota(jnp.int32, (span, columns), 1)
    yy = row % rows
    zz = row // rows
    x_first = lane % 8 == 0
    x_last = lane % 8 == 7
    y_first = yy % y_elem == 0
    y_last = yy % y_elem == y_elem - 1
    z_first = zz % 8 == 0
    z_last = zz % 8 == 7

    def scoped(xd_ref, yz_ref):
        for b in range(states):
            xd_ref[b] = tdot(v_ref[b].reshape(fields * span, columns), d_ref[...]).reshape(
                fields, span, columns)
            yz_ref[b] = tdot(k_ref[...], lanes([v_ref[b, f] for f in range(fields)]))
        for b in range(states):
            for f in range(fields):
                v = v_ref[b, f]
                cols = slice(f * columns, (f + 1) * columns)
                t = (cf_ref[0, f] * xd_ref[b, f] + cf_ref[1, f] * yz_ref[b, :span, cols]
                     + cf_ref[2, f] * yz_ref[b, span:, cols])
                before_x = pltpu.roll(v, 1, 1)
                after_x = pltpu.roll(v, columns - 1, 1)
                t = t + jnp.where(x_first, cf_ref[3, f] * (before_x - v), 0.0)
                t = t + jnp.where(x_last, cf_ref[4, f] * (after_x - v), 0.0)
                before_y = jnp.where(yy == 0, pltpu.roll(v, span - rows + 1, 0),
                                     pltpu.roll(v, 1, 0))
                after_y = jnp.where(yy == rows - 1, pltpu.roll(v, rows - 1, 0),
                                    pltpu.roll(v, span - 1, 0))
                t = t + jnp.where(y_first, cf_ref[5, f] * (before_y - v), 0.0)
                t = t + jnp.where(y_last, cf_ref[6, f] * (after_y - v), 0.0)
                if planes > 8:
                    before_z = pltpu.roll(v, rows, 0)
                    after_z = pltpu.roll(v, span - rows, 0)
                    t = t + jnp.where(z_first & (zz > 0), cf_ref[7, f] * before_z, 0.0)
                    t = t + jnp.where(z_last & (zz < planes - 1), cf_ref[8, f] * after_z, 0.0)
                t = t - jnp.where(z_first, cf_ref[7, f] * v, 0.0)
                t = t - jnp.where(z_last, cf_ref[8, f] * v, 0.0)
                out_ref[b, f] = t
                out_ref[b, f, pl.ds(0, rows), :] = (
                    out_ref[b, f, pl.ds(0, rows), :] + cf_ref[7, f] * prev_ref[b, f]
                )
                out_ref[b, f, pl.ds(span - rows, rows), :] = (
                    out_ref[b, f, pl.ds(span - rows, rows), :] + cf_ref[8, f] * next_ref[b, f]
                )
                s_ref[b, f] = jnp.tanh(v)

    pl.run_scoped(scoped, pltpu.VMEM((states, fields, span, columns), f32),
                  pltpu.VMEM((states, 2 * span, fields * columns), f32))
    for b in range(states):
        cooling = 1.0 / (1.5 + 0.5 * s_ref[b, fields - 1])

        def reaction_body(r, carry):
            first = rx_ref[r, 0]
            second = rx_ref[r, 1]
            product = rx_ref[r, 2]
            progress = (
                rate_ref[r] * jnp.exp(-en_ref[r] * cooling) * s_ref[b, first] * s_ref[b, second]
            )
            out_ref[b, product] = out_ref[b, product] + progress
            out_ref[b, first] = out_ref[b, first] - progress
            out_ref[b, second] = out_ref[b, second] - progress
            return carry

        lax.fori_loop(0, rx_ref.shape[0], reaction_body, 0)


def vmem():
    return pl.BlockSpec(memory_space=pltpu.VMEM)


def smem():
    return pl.BlockSpec(memory_space=pltpu.SMEM)


def tendency_cost(states, fields, span, columns, reactions):
    flops = states * fields * (2 * span * span * columns + 2 * span * columns * columns) * 6
    flops += states * span * columns * (8 * reactions + 4 * fields)
    trans = states * span * columns * (fields + 2 * reactions)
    return flops, trans


def call(kernel, ins, in_kinds, outs, scratch, flops, trans, blocks=None):
    nbytes = sum(int(np.prod(x.shape)) * 4 for x in ins) + sum(
        int(np.prod(o.shape)) * 4 for o in outs
    )
    return pl.pallas_call(
        kernel,
        out_shape=outs,
        in_specs=[
            (blocks[i] if blocks is not None and i in blocks else smem() if k else vmem())
            for i, k in enumerate(in_kinds)
        ],
        out_specs=tuple(vmem() for _ in outs),
        scratch_shapes=scratch,
        grid=() if blocks is None else (1,),
        cost_estimate=pl.CostEstimate(
            flops=int(flops), transcendentals=int(trans), bytes_accessed=int(nbytes)
        ),
    )(*ins)


def per_device(u_start, guess, velocity, rates, energies, reactions):
    fields, depth, rows, columns = u_start.shape
    coarse_rows = rows // 2
    span = depth * rows
    coarse_span = depth * coarse_rows
    reaction_count = rates.shape[0]
    fine_table = derivative_table(FINE_NODES)
    coarse_table = derivative_table(COARSE_NODES)
    fine_elem = len(FINE_NODES)
    coarse_elem = len(COARSE_NODES)
    xt = jnp.asarray(np.kron(np.eye(columns // fine_elem), fine_table).T, jnp.float32)
    z_block = np.kron(np.eye(depth // fine_elem), fine_table)

    def plane_operator(y_table, plane_rows):
        y_block = np.kron(np.eye(plane_rows // y_table.shape[0]), y_table)
        return jnp.asarray(
            np.concatenate([np.kron(np.eye(depth), y_block), np.kron(z_block, np.eye(plane_rows))]),
            jnp.float32,
        )

    lop_fine = plane_operator(fine_table, rows)
    lop_coarse = plane_operator(coarse_table, coarse_rows)

    def coefficients(y_lift):
        up = jnp.maximum(velocity, 0.0)
        down = jnp.maximum(-velocity, 0.0)
        return jnp.concatenate([
            -velocity,
            28.0 * up[0:1], 28.0 * down[0:1],
            y_lift * up[1:2], y_lift * down[1:2],
            28.0 * up[2:3], 28.0 * down[2:3],
        ])

    cf_fine = coefficients(28.0)
    cf_coarse = coefficients(6.0)
    restrict_rows = np.kron(np.eye(rows // 8), lagrange_table(FINE_NODES, COARSE_NODES))
    prolong_rows = np.kron(np.eye(rows // 8), lagrange_table(COARSE_NODES, FINE_NODES))
    rmat = jnp.asarray(np.kron(np.eye(depth), restrict_rows), jnp.float32)
    pmat = jnp.asarray(np.kron(np.eye(depth), prolong_rows), jnp.float32)
    restrict_plane = jnp.asarray(restrict_rows, jnp.float32)
    scalars = (cf_fine, reactions.astype(jnp.int32), rates, energies)
    coarse_scalars = (cf_coarse, reactions.astype(jnp.int32), rates, energies)
    scalar_kinds = (True, True, True, True)

    space_n = lax.axis_size("space")
    sections = lax.axis_size("tm")
    section = lax.axis_index("tm")
    lead = (section == 0).astype(jnp.int32).reshape(1)

    def halo(x, plane_rows):
        head = x[..., :plane_rows, :]
        tail = x[..., x.shape[-2] - plane_rows:, :]
        return swap(head, tail)

    def swap(head, tail):
        prev = lax.ppermute(tail, "space", [(i, (i + 1) % space_n) for i in range(space_n)])
        nxt = lax.ppermute(head, "space", [((i + 1) % space_n, i) for i in range(space_n)])
        return prev, nxt

    f32 = jnp.float32
    fine_state = jax.ShapeDtypeStruct((1, fields, span, columns), f32)
    coarse_state = jax.ShapeDtypeStruct((fields, coarse_span, columns), f32)

    def nodes_kernel(u_ref, p_ref, n_ref, l_ref, x_ref, zc_ref, rx_ref, ra_ref, en_ref,
                     f_ref, a1_ref, h_ref, t_ref, s_ref):
        tendency_into(f_ref, u_ref, p_ref, n_ref, l_ref, x_ref, zc_ref, rx_ref, ra_ref, en_ref,
                      s_ref, fine_elem)

        def body(f, carry):
            value = u_ref[0, f] + STEP * (
                5.0 * f_ref[0, f] + 8.0 * f_ref[1, f] - f_ref[2, f]
            ) / 24.0
            a1_ref[0, f] = value
            h_ref[0, f] = value[:rows]
            t_ref[0, f] = value[span - rows:]
            return carry

        lax.fori_loop(0, fields, body, 0)

    def middle_kernel(a1_ref, p_ref, n_ref, l_ref, x_ref, zc_ref, rx_ref, ra_ref, en_ref,
                      f_ref, g1_ref, a2_ref, h_ref, t_ref, s_ref):
        tendency_into(g1_ref, a1_ref, p_ref, n_ref, l_ref, x_ref, zc_ref, rx_ref, ra_ref,
                      en_ref, s_ref, fine_elem)

        def body(f, carry):
            value = (
                a1_ref[0, f]
                + 0.5 * STEP * (g1_ref[0, f] - f_ref[1, f])
                + STEP * (-f_ref[0, f] + 8.0 * f_ref[1, f] + 5.0 * f_ref[2, f]) / 24.0
            )
            a2_ref[0, f] = value
            h_ref[0, f] = value[:rows]
            t_ref[0, f] = value[span - rows:]
            return carry

        lax.fori_loop(0, fields, body, 0)

    def ending_kernel(a2_ref, p_ref, n_ref, l_ref, x_ref, zc_ref, rx_ref, ra_ref, en_ref,
                      f_ref, g1_ref, r_ref, base_ref, rint_ref, c1_ref, g2_ref, s_ref):
        tendency_into(g2_ref, a2_ref, p_ref, n_ref, l_ref, x_ref, zc_ref, rx_ref, ra_ref,
                      en_ref, s_ref, fine_elem)

        def body(f, carry):
            g2_ref[0, f] = STEP * (f_ref[0, f] + 4.0 * g1_ref[0, f] + g2_ref[0, f]) / 6.0
            return carry

        lax.fori_loop(0, fields, body, 0)
        rm = r_ref[...]
        for dst, src_ref, lead_index in ((rint_ref, g2_ref, 0), (c1_ref, a2_ref, 0)):
            wide = dot(rm, lanes([src_ref[lead_index, f] for f in range(fields)]))
            for f, part in enumerate(unlanes(wide, columns)):
                dst[f] = part
        for f in range(fields):
            rint_ref[f] = rint_ref[f] - STEP * base_ref[0, f]

    def base_kernel(u_ref, p_ref, n_ref, r_ref, rp_ref, l_ref, x_ref, zc_ref, rx_ref, ra_ref,
                    en_ref, out_ref, c0_ref, bp_ref, bn_ref, s_ref):
        for dst, src_ref, table in ((c0_ref, u_ref, r_ref), (bp_ref, p_ref, rp_ref),
                                    (bn_ref, n_ref, rp_ref)):
            wide = dot(table[...], lanes([src_ref[0, f] for f in range(fields)]))
            for f, part in enumerate(unlanes(wide, columns)):
                dst[0, f] = part
        tendency_into(out_ref, c0_ref, bp_ref, bn_ref, l_ref, x_ref, zc_ref, rx_ref, ra_ref,
                      en_ref, s_ref, coarse_elem)

    def chain_kernel(w_ref, p_ref, n_ref, l_ref, x_ref, zc_ref, rx_ref, ra_ref, en_ref,
                     rint_ref, out_ref, h_ref, t_ref, g_ref, s_ref):
        tendency_into(g_ref, w_ref, p_ref, n_ref, l_ref, x_ref, zc_ref, rx_ref, ra_ref,
                      en_ref, s_ref, coarse_elem)

        def body(f, carry):
            value = w_ref[0, f] + STEP * g_ref[0, f] + rint_ref[0, 0, f]
            out_ref[0, f] = value
            h_ref[0, f] = value[:coarse_rows]
            t_ref[0, f] = value[coarse_span - coarse_rows:]
            return carry

        lax.fori_loop(0, fields, body, 0)

    def plain_kernel(w_ref, p_ref, n_ref, l_ref, x_ref, zc_ref, rx_ref, ra_ref, en_ref,
                     out_ref, s_ref):
        tendency_into(out_ref, w_ref, p_ref, n_ref, l_ref, x_ref, zc_ref, rx_ref, ra_ref,
                      en_ref, s_ref, coarse_elem)

    def first_kernel(w_ref, g_ref, rint_ref, out_ref, h_ref, t_ref):
        for f in range(fields):
            value = w_ref[0, f] + STEP * g_ref[0, f] + rint_ref[0, 0, f]
            out_ref[0, f] = value
            h_ref[0, f] = value[:coarse_rows]
            t_ref[0, f] = value[coarse_span - coarse_rows:]

    def pick(sec_ref, w_refs, f, offset):
        value = w_refs[offset][0, f]
        for n in range(1, sections):
            value = jnp.where(sec_ref[0] == n, w_refs[n + offset][0, f], value)
        return value

    def correct_kernel(*refs):
        a1_ref, a2_ref, c0_ref, c1_ref = refs[:4]
        w_refs = refs[4:5 + sections]
        prev_ref, us_ref, r_ref, pm_ref, lead_ref, sec_ref, out_ref, h_ref, t_ref = refs[
            5 + sections:]
        pm = pm_ref[...]
        w0 = [pick(sec_ref, w_refs, f, 0) for f in range(fields)]
        first_change = [w0[f] - c0_ref[0, f] for f in range(fields)]
        last_change = [pick(sec_ref, w_refs, f, 1) - c1_ref[f] for f in range(fields)]
        middle_fix = unlanes(
            dot(pm, lanes([0.5 * (first_change[f] + last_change[f]) for f in range(fields)])),
            columns,
        )
        last_fix = unlanes(dot(pm, lanes(last_change)), columns)
        handed = lanes([prev_ref[0, f] for f in range(fields)])
        handed_fix = unlanes(
            dot(pm, lanes(w0) - dot(r_ref[...], handed)),
            columns,
        )
        for f in range(fields):
            values = (
                jnp.where(lead_ref[0] != 0, us_ref[f], prev_ref[0, f] + handed_fix[f]),
                a1_ref[0, f] + middle_fix[f],
                a2_ref[0, f] + last_fix[f],
            )
            for b, value in enumerate(values):
                out_ref[b, f] = value
                h_ref[b, f] = value[:rows]
                t_ref[b, f] = value[span - rows:]

    def finish_kernel(*refs):
        a2_ref, c1_ref = refs[:2]
        w_refs = refs[2:3 + sections]
        pm_ref, sec_ref, out_ref, coarse_ref = refs[3 + sections:]
        w1 = [pick(sec_ref, w_refs, f, 1) for f in range(fields)]
        fix = unlanes(
            dot(pm_ref[...], lanes([w1[f] - c1_ref[f] for f in range(fields)])), columns
        )
        for f in range(fields):
            out_ref[0, f] = a2_ref[0, f] + fix[f]
            coarse_ref[0, f] = w1[f]

    fine_cost = tendency_cost(1, fields, span, columns, reaction_count)
    coarse_cost = tendency_cost(1, fields, coarse_span, columns, reaction_count)

    def fine_scratch(states):
        return pltpu.VMEM((states, fields, span, columns), f32)

    def coarse_scratch(states):
        return pltpu.VMEM((states, fields, coarse_span, columns), f32)

    u_flat = u_start.reshape(fields, span, columns)
    nodes = guess[0].reshape(3, fields, span, columns)
    nodes = jnp.concatenate([jnp.where(section == 0, u_flat, nodes[0])[None], nodes[1:]], axis=0)
    coarse_start = jnp.einsum("cy,fzyx->fzcx", restrict_plane,
                              u_start, precision=HIGHEST).reshape(fields, coarse_span, columns)
    start_halo = halo(coarse_start, coarse_rows)

    coarse_one = jax.ShapeDtypeStruct((1, fields, coarse_span, columns), f32)
    plane_one = jax.ShapeDtypeStruct((1, fields, coarse_rows, columns), f32)
    fine_plane = jax.ShapeDtypeStruct((1, fields, rows, columns), f32)
    node_planes = jax.ShapeDtypeStruct((3, fields, rows, columns), f32)

    def coarse_step(w, w_halo, rint_all, n):
        def section_block():
            return pl.BlockSpec((1, 1, fields, coarse_span, columns), lambda i: (n, 0, 0, 0, 0),
                                memory_space=pltpu.VMEM)

        return call(
            chain_kernel,
            (w, w_halo[0], w_halo[1], lop_coarse, xt) + coarse_scalars + (rint_all,),
            (False,) * 5 + scalar_kinds + (False,),
            (coarse_one, plane_one, plane_one),
            [pltpu.VMEM((1, fields, coarse_span, columns), f32), coarse_scratch(1)],
            *coarse_cost,
            blocks={9: section_block()},
        )

    hop_pairs = [(d, d + 1) for d in range(sections - 1)]
    (start_tendency,) = call(
        plain_kernel,
        (coarse_start[None], start_halo[0][None], start_halo[1][None], lop_coarse, xt)
        + coarse_scalars,
        (False,) * 5 + scalar_kinds,
        (coarse_one,),
        [coarse_scratch(1)],
        *coarse_cost,
    )
    where_now = section.astype(jnp.int32).reshape(1)

    fine_end = None
    coarse_end = None
    for iteration in range(ITERS):
        if iteration == 0:
            node_prev, node_next = halo(nodes, rows)
        else:
            node_prev, node_next = swap(node_head, node_tail)
        f_all, a1, a1_head, a1_tail = call(
            nodes_kernel,
            (nodes, node_prev, node_next, lop_fine, xt) + scalars,
            (False,) * 5 + scalar_kinds,
            (jax.ShapeDtypeStruct((3, fields, span, columns), f32), fine_state, fine_plane,
             fine_plane),
            [fine_scratch(3)],
            fine_cost[0] * 3, fine_cost[1] * 3,
        )
        a1_prev, a1_next = swap(a1_head, a1_tail)
        g1, a2, a2_head, a2_tail = call(
            middle_kernel,
            (a1, a1_prev, a1_next, lop_fine, xt) + scalars + (f_all,),
            (False,) * 5 + scalar_kinds + (False,),
            (fine_state, fine_state, fine_plane, fine_plane),
            [fine_scratch(1)],
            *fine_cost,
        )
        a2_prev, a2_next = swap(a2_head, a2_tail)
        base, c0 = call(
            base_kernel,
            (nodes, node_prev, node_next, rmat, restrict_plane, lop_coarse, xt) + coarse_scalars,
            (False,) * 7 + scalar_kinds,
            (coarse_one, coarse_one),
            [pltpu.VMEM((1, fields, coarse_rows, columns), f32),
             pltpu.VMEM((1, fields, coarse_rows, columns), f32), coarse_scratch(1)],
            *coarse_cost,
        )
        rint, c1 = call(
            ending_kernel,
            (a2, a2_prev, a2_next, lop_fine, xt) + scalars + (f_all, g1, rmat, base),
            (False,) * 5 + scalar_kinds + (False,) * 4,
            (coarse_state, coarse_state),
            [pltpu.VMEM((1, fields, span, columns), f32), fine_scratch(1)],
            *fine_cost,
        )
        rint_all = lax.all_gather(rint[None], "tm")
        last = iteration + 1 == ITERS
        if not last:
            a2_handed = lax.ppermute(a2, "tm", hop_pairs)
        w = coarse_start[None]
        w_halo = (start_halo[0][None], start_halo[1][None])
        chain = [w]
        for n in range(sections):
            if n == 0:
                w, head, tail = call(
                    first_kernel,
                    (w, start_tendency, rint_all),
                    (False,) * 3,
                    (coarse_one, plane_one, plane_one),
                    [],
                    4 * fields * coarse_span * columns, 0,
                    blocks={2: pl.BlockSpec((1, 1, fields, coarse_span, columns),
                                            lambda i: (0, 0, 0, 0, 0),
                                            memory_space=pltpu.VMEM)},
                )
            else:
                w, head, tail = coarse_step(w, w_halo, rint_all, n)
            chain.append(w)
            if n + 1 < sections:
                w_halo = swap(head, tail)
        if last:
            fine_end, coarse_end = call(
                finish_kernel,
                (a2, c1) + tuple(chain) + (pmat, where_now),
                (False,) * (3 + sections) + (False, True),
                (fine_state, coarse_one),
                [],
                2 * fields * span * coarse_span * columns * 6, 0,
            )
        else:
            nodes, node_head, node_tail = call(
                correct_kernel,
                (a1, a2, c0, c1) + tuple(chain) + (a2_handed, u_flat, rmat, pmat, lead, where_now),
                (False,) * (5 + sections) + (False,) * 4 + (True, True),
                (jax.ShapeDtypeStruct((3, fields, span, columns), f32), node_planes,
                 node_planes),
                [],
                8 * fields * span * coarse_span * columns * 6, 0,
            )
    fine_end = fine_end.reshape(1, fields, depth, rows, columns)
    coarse_end = coarse_end.reshape(1, fields, depth, coarse_rows, columns)
    return (fine_end, coarse_end)


def solution(mesh):
    return jax.shard_map(
        per_device,
        mesh=mesh,
        in_specs=(
            P(None, "space", None, None),
            P("tm", None, None, "space", None, None),
            P(),
            P(),
            P(),
            P(),
        ),
        out_specs=(P("tm", None, "space", None, None), P("tm", None, "space", None, None)),
        check_vma=False,
    )
```

```python
import jax
import jax.numpy as jnp
import numpy as np
from jax import lax
from jax.experimental import pallas as pl
from jax.experimental.pallas import tpu as pltpu
from jax.sharding import PartitionSpec as P

ITERS = 2


STEP = 0.01
HIGHEST = lax.Precision.HIGHEST
FINE_NODES = np.array(
    [
        -1.0,
        -0.8717401485096066,
        -0.5917001814331423,
        -0.2092992179024789,
        0.2092992179024789,
        0.5917001814331423,
        0.8717401485096066,
        1.0,
    ]
)
COARSE_NODES = np.array([-1.0, -0.4472135954999579, 0.4472135954999579, 1.0])


def lagrange_table(source, target):
    table = np.ones((len(target), len(source)))
    for j in range(len(source)):
        for m in range(len(source)):
            if m != j:
                table[:, j] *= (target - source[m]) / (source[j] - source[m])
    return table


def derivative_table(points):
    total = len(points)
    weights = np.array(
        [
            1.0 / np.prod([points[j] - points[m] for m in range(total) if m != j])
            for j in range(total)
        ]
    )
    table = np.zeros((total, total))
    for i in range(total):
        for j in range(total):
            if i != j:
                table[i, j] = weights[j] / weights[i] / (points[i] - points[j])
        table[i, i] = -np.sum(table[i])
    return table


def element_tables(length, table, lift):
    per_element = table.shape[0]
    block = np.kron(np.eye(length // per_element), table)
    position = np.arange(length) % per_element
    identity = np.eye(length)
    before = np.roll(identity, -1, axis=1)
    after = np.roll(identity, 1, axis=1)
    first_mask = np.where(position == 0, 1.0, 0.0)
    last_mask = np.where(position == per_element - 1, 1.0, 0.0)
    upwind = lift * first_mask[:, None] * (before - identity)
    downwind = lift * last_mask[:, None] * (after - identity)
    return (block, upwind, downwind)


def widen(matrix):
    length = matrix.shape[0]
    wider = np.zeros((length, matrix.shape[1] + 2))
    wider[:, 1:-1] = matrix
    return wider


def padded_tables(length, table, lift):
    block, upwind, downwind = element_tables(length, table, lift)
    block_wide = widen(block)
    upwind_wide = widen(upwind)
    downwind_wide = widen(downwind)
    upwind_wide[0, length] = 0.0
    upwind_wide[0, 0] = lift
    downwind_wide[length - 1, 1] = 0.0
    downwind_wide[length - 1, length + 1] = lift
    return (block_wide, upwind_wide, downwind_wide)


def field_operators(speed, tables):
    block = jnp.asarray(tables[0], jnp.float32)
    upwind = jnp.asarray(tables[1], jnp.float32)
    downwind = jnp.asarray(tables[2], jnp.float32)
    speeds = speed[:, None, None]
    return (
        -speeds * block + jnp.maximum(speeds, 0.0) * upwind + jnp.maximum(-speeds, 0.0) * downwind
    )


def speed_combination(speed, tables):
    block = jnp.asarray(tables[0], jnp.float32)[None]
    upwind = jnp.asarray(tables[1], jnp.float32)[None]
    downwind = jnp.asarray(tables[2], jnp.float32)[None]
    speeds = speed[:, None, None]
    return (
        -speeds * block + jnp.maximum(speeds, 0.0) * upwind + jnp.maximum(-speeds, 0.0) * downwind
    )


def dot(a, b):
    return jnp.dot(a, b, precision=HIGHEST, preferred_element_type=jnp.float32)


def tdot(a, b):
    return jnp.dot(a, b, precision=lax.Precision.HIGH, preferred_element_type=jnp.float32)


def lanes(parts):
    return jnp.concatenate(parts, axis=1)


def unlanes(wide, width):
    return [wide[:, i * width:(i + 1) * width] for i in range(wide.shape[1] // width)]


def tendency_into(out_ref, v_ref, prev_ref, next_ref, k_ref, d_ref, cf_ref, rx_ref,
                  rate_ref, en_ref, s_ref, y_elem):
    states, fields, span, columns = v_ref.shape
    rows = prev_ref.shape[2]
    planes = span // rows
    f32 = jnp.float32
    row = lax.broadcasted_iota(jnp.int32, (span, columns), 0)
    lane = lax.broadcasted_iota(jnp.int32, (span, columns), 1)
    yy = row % rows
    zz = row // rows
    x_first = lane % 8 == 0
    x_last = lane % 8 == 7
    y_first = yy % y_elem == 0
    y_last = yy % y_elem == y_elem - 1
    z_first = zz % 8 == 0
    z_last = zz % 8 == 7

    def scoped(xd_ref, yz_ref):
        for b in range(states):
            xd_ref[b] = tdot(v_ref[b].reshape(fields * span, columns), d_ref[...]).reshape(
                fields, span, columns)
            yz_ref[b] = tdot(k_ref[...], lanes([v_ref[b, f] for f in range(fields)]))
        for b in range(states):
            for f in range(fields):
                v = v_ref[b, f]
                cols = slice(f * columns, (f + 1) * columns)
                t = (cf_ref[0, f] * xd_ref[b, f] + cf_ref[1, f] * yz_ref[b, :span, cols]
                     + cf_ref[2, f] * yz_ref[b, span:, cols])
                before_x = pltpu.roll(v, 1, 1)
                after_x = pltpu.roll(v, columns - 1, 1)
                t = t + jnp.where(x_first, cf_ref[3, f] * (before_x - v), 0.0)
                t = t + jnp.where(x_last, cf_ref[4, f] * (after_x - v), 0.0)
                before_y = jnp.where(yy == 0, pltpu.roll(v, span - rows + 1, 0),
                                     pltpu.roll(v, 1, 0))
                after_y = jnp.where(yy == rows - 1, pltpu.roll(v, rows - 1, 0),
                                    pltpu.roll(v, span - 1, 0))
                t = t + jnp.where(y_first, cf_ref[5, f] * (before_y - v), 0.0)
                t = t + jnp.where(y_last, cf_ref[6, f] * (after_y - v), 0.0)
                if planes > 8:
                    before_z = pltpu.roll(v, rows, 0)
                    after_z = pltpu.roll(v, span - rows, 0)
                    t = t + jnp.where(z_first & (zz > 0), cf_ref[7, f] * before_z, 0.0)
                    t = t + jnp.where(z_last & (zz < planes - 1), cf_ref[8, f] * after_z, 0.0)
                t = t - jnp.where(z_first, cf_ref[7, f] * v, 0.0)
                t = t - jnp.where(z_last, cf_ref[8, f] * v, 0.0)
                out_ref[b, f] = t
                out_ref[b, f, pl.ds(0, rows), :] = (
                    out_ref[b, f, pl.ds(0, rows), :] + cf_ref[7, f] * prev_ref[b, f]
                )
                out_ref[b, f, pl.ds(span - rows, rows), :] = (
                    out_ref[b, f, pl.ds(span - rows, rows), :] + cf_ref[8, f] * next_ref[b, f]
                )
                s_ref[b, f] = jnp.tanh(v)

    pl.run_scoped(scoped, pltpu.VMEM((states, fields, span, columns), f32),
                  pltpu.VMEM((states, 2 * span, fields * columns), f32))
    for b in range(states):
        cooling = 1.0 / (1.5 + 0.5 * s_ref[b, fields - 1])

        def reaction_body(r, carry):
            first = rx_ref[r, 0]
            second = rx_ref[r, 1]
            product = rx_ref[r, 2]
            progress = (
                rate_ref[r] * jnp.exp(-en_ref[r] * cooling) * s_ref[b, first] * s_ref[b, second]
            )
            out_ref[b, product] = out_ref[b, product] + progress
            out_ref[b, first] = out_ref[b, first] - progress
            out_ref[b, second] = out_ref[b, second] - progress
            return carry

        lax.fori_loop(0, rx_ref.shape[0], reaction_body, 0)


def vmem():
    return pl.BlockSpec(memory_space=pltpu.VMEM)


def smem():
    return pl.BlockSpec(memory_space=pltpu.SMEM)


def tendency_cost(states, fields, span, columns, reactions):
    flops = states * fields * (2 * span * span * columns + 2 * span * columns * columns) * 6
    flops += states * span * columns * (8 * reactions + 4 * fields)
    trans = states * span * columns * (fields + 2 * reactions)
    return flops, trans


def call(kernel, ins, in_kinds, outs, scratch, flops, trans, blocks=None):
    nbytes = sum(int(np.prod(x.shape)) * 4 for x in ins) + sum(
        int(np.prod(o.shape)) * 4 for o in outs
    )
    return pl.pallas_call(
        kernel,
        out_shape=outs,
        in_specs=[
            (blocks[i] if blocks is not None and i in blocks else smem() if k else vmem())
            for i, k in enumerate(in_kinds)
        ],
        out_specs=tuple(vmem() for _ in outs),
        scratch_shapes=scratch,
        grid=() if blocks is None else (1,),
        cost_estimate=pl.CostEstimate(
            flops=int(flops), transcendentals=int(trans), bytes_accessed=int(nbytes)
        ),
    )(*ins)


def per_device(u_start, guess, velocity, rates, energies, reactions):
    fields, depth, rows, columns = u_start.shape
    coarse_rows = rows // 2
    span = depth * rows
    coarse_span = depth * coarse_rows
    reaction_count = rates.shape[0]
    fine_table = derivative_table(FINE_NODES)
    coarse_table = derivative_table(COARSE_NODES)
    fine_elem = len(FINE_NODES)
    coarse_elem = len(COARSE_NODES)
    xt = jnp.asarray(np.kron(np.eye(columns // fine_elem), fine_table).T, jnp.float32)
    z_block = np.kron(np.eye(depth // fine_elem), fine_table)

    def plane_operator(y_table, plane_rows):
        y_block = np.kron(np.eye(plane_rows // y_table.shape[0]), y_table)
        return jnp.asarray(
            np.concatenate([np.kron(np.eye(depth), y_block), np.kron(z_block, np.eye(plane_rows))]),
            jnp.float32,
        )

    lop_fine = plane_operator(fine_table, rows)
    lop_coarse = plane_operator(coarse_table, coarse_rows)

    def coefficients(y_lift):
        up = jnp.maximum(velocity, 0.0)
        down = jnp.maximum(-velocity, 0.0)
        return jnp.concatenate([
            -velocity,
            28.0 * up[0:1], 28.0 * down[0:1],
            y_lift * up[1:2], y_lift * down[1:2],
            28.0 * up[2:3], 28.0 * down[2:3],
        ])

    cf_fine = coefficients(28.0)
    cf_coarse = coefficients(6.0)
    restrict_rows = np.kron(np.eye(rows // 8), lagrange_table(FINE_NODES, COARSE_NODES))
    prolong_rows = np.kron(np.eye(rows // 8), lagrange_table(COARSE_NODES, FINE_NODES))
    rmat = jnp.asarray(np.kron(np.eye(depth), restrict_rows), jnp.float32)
    pmat = jnp.asarray(np.kron(np.eye(depth), prolong_rows), jnp.float32)
    restrict_plane = jnp.asarray(restrict_rows, jnp.float32)
    scalars = (cf_fine, reactions.astype(jnp.int32), rates, energies)
    coarse_scalars = (cf_coarse, reactions.astype(jnp.int32), rates, energies)
    scalar_kinds = (True, True, True, True)

    space_n = lax.axis_size("space")
    sections = lax.axis_size("tm")
    section = lax.axis_index("tm")
    lead = (section == 0).astype(jnp.int32).reshape(1)

    def halo(x, plane_rows):
        head = x[..., :plane_rows, :]
        tail = x[..., x.shape[-2] - plane_rows:, :]
        return swap(head, tail)

    def swap(head, tail):
        prev = lax.ppermute(tail, "space", [(i, (i + 1) % space_n) for i in range(space_n)])
        nxt = lax.ppermute(head, "space", [((i + 1) % space_n, i) for i in range(space_n)])
        return prev, nxt

    f32 = jnp.float32
    fine_state = jax.ShapeDtypeStruct((1, fields, span, columns), f32)
    coarse_state = jax.ShapeDtypeStruct((fields, coarse_span, columns), f32)

    def nodes_kernel(u_ref, p_ref, n_ref, l_ref, x_ref, zc_ref, rx_ref, ra_ref, en_ref,
                     f_ref, a1_ref, h_ref, t_ref, s_ref):
        tendency_into(f_ref, u_ref, p_ref, n_ref, l_ref, x_ref, zc_ref, rx_ref, ra_ref, en_ref,
                      s_ref, fine_elem)

        def body(f, carry):
            value = u_ref[0, f] + STEP * (
                5.0 * f_ref[0, f] + 8.0 * f_ref[1, f] - f_ref[2, f]
            ) / 24.0
            a1_ref[0, f] = value
            h_ref[0, f] = value[:rows]
            t_ref[0, f] = value[span - rows:]
            return carry

        lax.fori_loop(0, fields, body, 0)

    def middle_kernel(a1_ref, p_ref, n_ref, l_ref, x_ref, zc_ref, rx_ref, ra_ref, en_ref,
                      f_ref, g1_ref, a2_ref, h_ref, t_ref, s_ref):
        tendency_into(g1_ref, a1_ref, p_ref, n_ref, l_ref, x_ref, zc_ref, rx_ref, ra_ref,
                      en_ref, s_ref, fine_elem)

        def body(f, carry):
            value = (
                a1_ref[0, f]
                + 0.5 * STEP * (g1_ref[0, f] - f_ref[1, f])
                + STEP * (-f_ref[0, f] + 8.0 * f_ref[1, f] + 5.0 * f_ref[2, f]) / 24.0
            )
            a2_ref[0, f] = value
            h_ref[0, f] = value[:rows]
            t_ref[0, f] = value[span - rows:]
            return carry

        lax.fori_loop(0, fields, body, 0)

    def ending_kernel(a2_ref, p_ref, n_ref, l_ref, x_ref, zc_ref, rx_ref, ra_ref, en_ref,
                      f_ref, g1_ref, r_ref, base_ref, rint_ref, c1_ref, g2_ref, s_ref):
        tendency_into(g2_ref, a2_ref, p_ref, n_ref, l_ref, x_ref, zc_ref, rx_ref, ra_ref,
                      en_ref, s_ref, fine_elem)

        def body(f, carry):
            g2_ref[0, f] = STEP * (f_ref[0, f] + 4.0 * g1_ref[0, f] + g2_ref[0, f]) / 6.0
            return carry

        lax.fori_loop(0, fields, body, 0)
        rm = r_ref[...]
        for dst, src_ref, lead_index in ((rint_ref, g2_ref, 0), (c1_ref, a2_ref, 0)):
            wide = dot(rm, lanes([src_ref[lead_index, f] for f in range(fields)]))
            for f, part in enumerate(unlanes(wide, columns)):
                dst[f] = part
        for f in range(fields):
            rint_ref[f] = rint_ref[f] - STEP * base_ref[0, f]

    def base_kernel(u_ref, p_ref, n_ref, r_ref, rp_ref, l_ref, x_ref, zc_ref, rx_ref, ra_ref,
                    en_ref, out_ref, c0_ref, bp_ref, bn_ref, s_ref):
        for dst, src_ref, table in ((c0_ref, u_ref, r_ref), (bp_ref, p_ref, rp_ref),
                                    (bn_ref, n_ref, rp_ref)):
            wide = dot(table[...], lanes([src_ref[0, f] for f in range(fields)]))
            for f, part in enumerate(unlanes(wide, columns)):
                dst[0, f] = part
        tendency_into(out_ref, c0_ref, bp_ref, bn_ref, l_ref, x_ref, zc_ref, rx_ref, ra_ref,
                      en_ref, s_ref, coarse_elem)

    def chain_kernel(w_ref, p_ref, n_ref, l_ref, x_ref, zc_ref, rx_ref, ra_ref, en_ref,
                     rint_ref, out_ref, h_ref, t_ref, g_ref, s_ref):
        tendency_into(g_ref, w_ref, p_ref, n_ref, l_ref, x_ref, zc_ref, rx_ref, ra_ref,
                      en_ref, s_ref, coarse_elem)

        def body(f, carry):
            value = w_ref[0, f] + STEP * g_ref[0, f] + rint_ref[0, 0, f]
            out_ref[0, f] = value
            h_ref[0, f] = value[:coarse_rows]
            t_ref[0, f] = value[coarse_span - coarse_rows:]
            return carry

        lax.fori_loop(0, fields, body, 0)

    def plain_kernel(w_ref, p_ref, n_ref, rp_ref, l_ref, x_ref, zc_ref, rx_ref, ra_ref, en_ref,
                     out_ref, bp_ref, bn_ref, s_ref):
        last = p_ref.shape[0] - 1
        for dst, src_ref in ((bp_ref, p_ref), (bn_ref, n_ref)):
            wide = dot(rp_ref[...], lanes([src_ref[last, f] for f in range(fields)]))
            for f, part in enumerate(unlanes(wide, columns)):
                dst[0, f] = part
        tendency_into(out_ref, w_ref, bp_ref, bn_ref, l_ref, x_ref, zc_ref, rx_ref, ra_ref,
                      en_ref, s_ref, coarse_elem)

    def first_kernel(w_ref, g_ref, rint_ref, out_ref, h_ref, t_ref):
        for f in range(fields):
            value = w_ref[0, f] + STEP * g_ref[0, f] + rint_ref[0, 0, f]
            out_ref[0, f] = value
            h_ref[0, f] = value[:coarse_rows]
            t_ref[0, f] = value[coarse_span - coarse_rows:]

    def pick(sec_ref, w_refs, f, offset):
        value = w_refs[offset][0, f]
        for n in range(1, sections):
            value = jnp.where(sec_ref[0] == n, w_refs[n + offset][0, f], value)
        return value

    def correct_kernel(*refs):
        a1_ref, a2_ref, c0_ref, c1_ref = refs[:4]
        w_refs = refs[4:5 + sections]
        prev_ref, us_ref, r_ref, pm_ref, lead_ref, sec_ref, out_ref, h_ref, t_ref = refs[
            5 + sections:]
        pm = pm_ref[...]
        w0 = [pick(sec_ref, w_refs, f, 0) for f in range(fields)]
        first_change = [w0[f] - c0_ref[0, f] for f in range(fields)]
        last_change = [pick(sec_ref, w_refs, f, 1) - c1_ref[f] for f in range(fields)]
        middle_fix = unlanes(
            dot(pm, lanes([0.5 * (first_change[f] + last_change[f]) for f in range(fields)])),
            columns,
        )
        last_fix = unlanes(dot(pm, lanes(last_change)), columns)
        handed = lanes([prev_ref[0, f] for f in range(fields)])
        handed_fix = unlanes(
            dot(pm, lanes(w0) - dot(r_ref[...], handed)),
            columns,
        )
        for f in range(fields):
            values = (
                jnp.where(lead_ref[0] != 0, us_ref[f], prev_ref[0, f] + handed_fix[f]),
                a1_ref[0, f] + middle_fix[f],
                a2_ref[0, f] + last_fix[f],
            )
            for b, value in enumerate(values):
                out_ref[b, f] = value
                h_ref[b, f] = value[:rows]
                t_ref[b, f] = value[span - rows:]

    def finish_kernel(*refs):
        a2_ref, c1_ref = refs[:2]
        w_refs = refs[2:3 + sections]
        pm_ref, sec_ref, out_ref, coarse_ref = refs[3 + sections:]
        w1 = [pick(sec_ref, w_refs, f, 1) for f in range(fields)]
        fix = unlanes(
            dot(pm_ref[...], lanes([w1[f] - c1_ref[f] for f in range(fields)])), columns
        )
        for f in range(fields):
            out_ref[0, f] = a2_ref[0, f] + fix[f]
            coarse_ref[0, f] = w1[f]

    fine_cost = tendency_cost(1, fields, span, columns, reaction_count)
    coarse_cost = tendency_cost(1, fields, coarse_span, columns, reaction_count)

    def fine_scratch(states):
        return pltpu.VMEM((states, fields, span, columns), f32)

    def coarse_scratch(states):
        return pltpu.VMEM((states, fields, coarse_span, columns), f32)

    u_flat = u_start.reshape(fields, span, columns)
    nodes = guess[0].reshape(3, fields, span, columns)
    nodes = jnp.concatenate([jnp.where(section == 0, u_flat, nodes[0])[None], nodes[1:]], axis=0)
    coarse_start = jnp.einsum("cy,fzyx->fzcx", restrict_plane,
                              u_start, precision=HIGHEST).reshape(fields, coarse_span, columns)

    coarse_one = jax.ShapeDtypeStruct((1, fields, coarse_span, columns), f32)
    plane_one = jax.ShapeDtypeStruct((1, fields, coarse_rows, columns), f32)
    fine_plane = jax.ShapeDtypeStruct((1, fields, rows, columns), f32)
    node_planes = jax.ShapeDtypeStruct((3, fields, rows, columns), f32)

    def coarse_step(w, w_halo, rint_all, n):
        def section_block():
            return pl.BlockSpec((1, 1, fields, coarse_span, columns), lambda i: (n, 0, 0, 0, 0),
                                memory_space=pltpu.VMEM)

        return call(
            chain_kernel,
            (w, w_halo[0], w_halo[1], lop_coarse, xt) + coarse_scalars + (rint_all,),
            (False,) * 5 + scalar_kinds + (False,),
            (coarse_one, plane_one, plane_one),
            [pltpu.VMEM((1, fields, coarse_span, columns), f32), coarse_scratch(1)],
            *coarse_cost,
            blocks={9: section_block()},
        )

    hop_pairs = [(d, d + 1) for d in range(sections - 1)]
    first_head = jnp.concatenate([nodes[:, :, :rows], u_flat[None, :, :rows]])
    first_tail = jnp.concatenate([nodes[:, :, span - rows:], u_flat[None, :, span - rows:]])
    first_prev, first_next = swap(first_head, first_tail)
    (start_tendency,) = call(
        plain_kernel,
        (coarse_start[None], first_prev, first_next, restrict_plane, lop_coarse, xt)
        + coarse_scalars,
        (False,) * 6 + scalar_kinds,
        (coarse_one,),
        [pltpu.VMEM((1, fields, coarse_rows, columns), f32),
         pltpu.VMEM((1, fields, coarse_rows, columns), f32), coarse_scratch(1)],
        *coarse_cost,
    )
    where_now = section.astype(jnp.int32).reshape(1)

    fine_end = None
    coarse_end = None
    for iteration in range(ITERS):
        if iteration == 0:
            node_prev, node_next = first_prev, first_next
        else:
            node_prev, node_next = swap(node_head, node_tail)
        f_all, a1, a1_head, a1_tail = call(
            nodes_kernel,
            (nodes, node_prev, node_next, lop_fine, xt) + scalars,
            (False,) * 5 + scalar_kinds,
            (jax.ShapeDtypeStruct((3, fields, span, columns), f32), fine_state, fine_plane,
             fine_plane),
            [fine_scratch(3)],
            fine_cost[0] * 3, fine_cost[1] * 3,
        )
        a1_prev, a1_next = swap(a1_head, a1_tail)
        g1, a2, a2_head, a2_tail = call(
            middle_kernel,
            (a1, a1_prev, a1_next, lop_fine, xt) + scalars + (f_all,),
            (False,) * 5 + scalar_kinds + (False,),
            (fine_state, fine_state, fine_plane, fine_plane),
            [fine_scratch(1)],
            *fine_cost,
        )
        a2_prev, a2_next = swap(a2_head, a2_tail)
        base, c0 = call(
            base_kernel,
            (nodes, node_prev, node_next, rmat, restrict_plane, lop_coarse, xt) + coarse_scalars,
            (False,) * 7 + scalar_kinds,
            (coarse_one, coarse_one),
            [pltpu.VMEM((1, fields, coarse_rows, columns), f32),
             pltpu.VMEM((1, fields, coarse_rows, columns), f32), coarse_scratch(1)],
            *coarse_cost,
        )
        rint, c1 = call(
            ending_kernel,
            (a2, a2_prev, a2_next, lop_fine, xt) + scalars + (f_all, g1, rmat, base),
            (False,) * 5 + scalar_kinds + (False,) * 4,
            (coarse_state, coarse_state),
            [pltpu.VMEM((1, fields, span, columns), f32), fine_scratch(1)],
            *fine_cost,
        )
        rint_all = lax.all_gather(rint[None], "tm")
        last = iteration + 1 == ITERS
        if not last:
            a2_handed = lax.ppermute(a2, "tm", hop_pairs)
        w = coarse_start[None]
        w_halo = None
        chain = [w]
        for n in range(sections):
            if n == 0:
                w, head, tail = call(
                    first_kernel,
                    (w, start_tendency, rint_all),
                    (False,) * 3,
                    (coarse_one, plane_one, plane_one),
                    [],
                    4 * fields * coarse_span * columns, 0,
                    blocks={2: pl.BlockSpec((1, 1, fields, coarse_span, columns),
                                            lambda i: (0, 0, 0, 0, 0),
                                            memory_space=pltpu.VMEM)},
                )
            else:
                w, head, tail = coarse_step(w, w_halo, rint_all, n)
            chain.append(w)
            if n + 1 < sections:
                w_halo = swap(head, tail)
        if last:
            fine_end, coarse_end = call(
                finish_kernel,
                (a2, c1) + tuple(chain) + (pmat, where_now),
                (False,) * (3 + sections) + (False, True),
                (fine_state, coarse_one),
                [],
                2 * fields * span * coarse_span * columns * 6, 0,
            )
        else:
            nodes, node_head, node_tail = call(
                correct_kernel,
                (a1, a2, c0, c1) + tuple(chain) + (a2_handed, u_flat, rmat, pmat, lead, where_now),
                (False,) * (5 + sections) + (False,) * 4 + (True, True),
                (jax.ShapeDtypeStruct((3, fields, span, columns), f32), node_planes,
                 node_planes),
                [],
                8 * fields * span * coarse_span * columns * 6, 0,
            )
    fine_end = fine_end.reshape(1, fields, depth, rows, columns)
    coarse_end = coarse_end.reshape(1, fields, depth, coarse_rows, columns)
    return (fine_end, coarse_end)


def solution(mesh):
    return jax.shard_map(
        per_device,
        mesh=mesh,
        in_specs=(
            P(None, "space", None, None),
            P("tm", None, None, "space", None, None),
            P(),
            P(),
            P(),
            P(),
        ),
        out_specs=(P("tm", None, "space", None, None), P("tm", None, "space", None, None)),
        check_vma=False,
    )
```

```python
import jax
import jax.numpy as jnp
import numpy as np
from jax import lax
from jax.experimental import pallas as pl
from jax.experimental.pallas import tpu as pltpu
from jax.sharding import PartitionSpec as P

ITERS = 2


STEP = 0.01
HIGHEST = lax.Precision.HIGHEST
FINE_NODES = np.array(
    [
        -1.0,
        -0.8717401485096066,
        -0.5917001814331423,
        -0.2092992179024789,
        0.2092992179024789,
        0.5917001814331423,
        0.8717401485096066,
        1.0,
    ]
)
COARSE_NODES = np.array([-1.0, -0.4472135954999579, 0.4472135954999579, 1.0])


def lagrange_table(source, target):
    table = np.ones((len(target), len(source)))
    for j in range(len(source)):
        for m in range(len(source)):
            if m != j:
                table[:, j] *= (target - source[m]) / (source[j] - source[m])
    return table


def derivative_table(points):
    total = len(points)
    weights = np.array(
        [
            1.0 / np.prod([points[j] - points[m] for m in range(total) if m != j])
            for j in range(total)
        ]
    )
    table = np.zeros((total, total))
    for i in range(total):
        for j in range(total):
            if i != j:
                table[i, j] = weights[j] / weights[i] / (points[i] - points[j])
        table[i, i] = -np.sum(table[i])
    return table


def element_tables(length, table, lift):
    per_element = table.shape[0]
    block = np.kron(np.eye(length // per_element), table)
    position = np.arange(length) % per_element
    identity = np.eye(length)
    before = np.roll(identity, -1, axis=1)
    after = np.roll(identity, 1, axis=1)
    first_mask = np.where(position == 0, 1.0, 0.0)
    last_mask = np.where(position == per_element - 1, 1.0, 0.0)
    upwind = lift * first_mask[:, None] * (before - identity)
    downwind = lift * last_mask[:, None] * (after - identity)
    return (block, upwind, downwind)


def widen(matrix):
    length = matrix.shape[0]
    wider = np.zeros((length, matrix.shape[1] + 2))
    wider[:, 1:-1] = matrix
    return wider


def padded_tables(length, table, lift):
    block, upwind, downwind = element_tables(length, table, lift)
    block_wide = widen(block)
    upwind_wide = widen(upwind)
    downwind_wide = widen(downwind)
    upwind_wide[0, length] = 0.0
    upwind_wide[0, 0] = lift
    downwind_wide[length - 1, 1] = 0.0
    downwind_wide[length - 1, length + 1] = lift
    return (block_wide, upwind_wide, downwind_wide)


def field_operators(speed, tables):
    block = jnp.asarray(tables[0], jnp.float32)
    upwind = jnp.asarray(tables[1], jnp.float32)
    downwind = jnp.asarray(tables[2], jnp.float32)
    speeds = speed[:, None, None]
    return (
        -speeds * block + jnp.maximum(speeds, 0.0) * upwind + jnp.maximum(-speeds, 0.0) * downwind
    )


def speed_combination(speed, tables):
    block = jnp.asarray(tables[0], jnp.float32)[None]
    upwind = jnp.asarray(tables[1], jnp.float32)[None]
    downwind = jnp.asarray(tables[2], jnp.float32)[None]
    speeds = speed[:, None, None]
    return (
        -speeds * block + jnp.maximum(speeds, 0.0) * upwind + jnp.maximum(-speeds, 0.0) * downwind
    )


def dot(a, b):
    return jnp.dot(a, b, precision=HIGHEST, preferred_element_type=jnp.float32)


def tdot(a, b):
    return jnp.dot(a, b, precision=lax.Precision.HIGH, preferred_element_type=jnp.float32)


def lanes(parts):
    return jnp.concatenate(parts, axis=1)


def unlanes(wide, width):
    return [wide[:, i * width:(i + 1) * width] for i in range(wide.shape[1] // width)]


def tendency_into(out_ref, v_ref, prev_ref, next_ref, k_ref, d_ref, cf_ref, rx_ref,
                  rate_ref, en_ref, s_ref, y_elem):
    states, fields, span, columns = v_ref.shape
    rows = prev_ref.shape[2]
    planes = span // rows
    f32 = jnp.float32
    y_lift = 28.0 if y_elem == len(FINE_NODES) else 6.0
    lifts = (28.0, y_lift, 28.0)

    class Speeds:
        def __getitem__(self, key):
            k, f = key
            if k < 3:
                return -cf_ref[k, f]
            d = (k - 3) // 2
            if (k - 3) % 2 == 0:
                return lifts[d] * jnp.maximum(cf_ref[d, f], 0.0)
            return lifts[d] * jnp.maximum(-cf_ref[d, f], 0.0)

    speeds = Speeds()
    row = lax.broadcasted_iota(jnp.int32, (span, columns), 0)
    lane = lax.broadcasted_iota(jnp.int32, (span, columns), 1)
    yy = row % rows
    zz = row // rows
    x_first = lane % 8 == 0
    x_last = lane % 8 == 7
    y_first = yy % y_elem == 0
    y_last = yy % y_elem == y_elem - 1
    z_first = zz % 8 == 0
    z_last = zz % 8 == 7

    def scoped(xd_ref, yz_ref):
        for b in range(states):
            xd_ref[b] = tdot(v_ref[b].reshape(fields * span, columns), d_ref[...]).reshape(
                fields, span, columns)
            yz_ref[b] = tdot(k_ref[...], lanes([v_ref[b, f] for f in range(fields)]))
        for b in range(states):
            for f in range(fields):
                v = v_ref[b, f]
                cols = slice(f * columns, (f + 1) * columns)
                t = (speeds[0, f] * xd_ref[b, f] + speeds[1, f] * yz_ref[b, :span, cols]
                     + speeds[2, f] * yz_ref[b, span:, cols])
                before_x = pltpu.roll(v, 1, 1)
                after_x = pltpu.roll(v, columns - 1, 1)
                t = t + jnp.where(x_first, speeds[3, f] * (before_x - v), 0.0)
                t = t + jnp.where(x_last, speeds[4, f] * (after_x - v), 0.0)
                before_y = jnp.where(yy == 0, pltpu.roll(v, span - rows + 1, 0),
                                     pltpu.roll(v, 1, 0))
                after_y = jnp.where(yy == rows - 1, pltpu.roll(v, rows - 1, 0),
                                    pltpu.roll(v, span - 1, 0))
                t = t + jnp.where(y_first, speeds[5, f] * (before_y - v), 0.0)
                t = t + jnp.where(y_last, speeds[6, f] * (after_y - v), 0.0)
                if planes > 8:
                    before_z = pltpu.roll(v, rows, 0)
                    after_z = pltpu.roll(v, span - rows, 0)
                    t = t + jnp.where(z_first & (zz > 0), speeds[7, f] * before_z, 0.0)
                    t = t + jnp.where(z_last & (zz < planes - 1), speeds[8, f] * after_z, 0.0)
                t = t - jnp.where(z_first, speeds[7, f] * v, 0.0)
                t = t - jnp.where(z_last, speeds[8, f] * v, 0.0)
                out_ref[b, f] = t
                out_ref[b, f, pl.ds(0, rows), :] = (
                    out_ref[b, f, pl.ds(0, rows), :] + speeds[7, f] * prev_ref[b, f]
                )
                out_ref[b, f, pl.ds(span - rows, rows), :] = (
                    out_ref[b, f, pl.ds(span - rows, rows), :] + speeds[8, f] * next_ref[b, f]
                )
                s_ref[b, f] = jnp.tanh(v)

    pl.run_scoped(scoped, pltpu.VMEM((states, fields, span, columns), f32),
                  pltpu.VMEM((states, 2 * span, fields * columns), f32))
    for b in range(states):
        cooling = 1.0 / (1.5 + 0.5 * s_ref[b, fields - 1])

        def reaction_body(r, carry):
            first = rx_ref[r, 0]
            second = rx_ref[r, 1]
            product = rx_ref[r, 2]
            progress = (
                rate_ref[r] * jnp.exp(-en_ref[r] * cooling) * s_ref[b, first] * s_ref[b, second]
            )
            out_ref[b, product] = out_ref[b, product] + progress
            out_ref[b, first] = out_ref[b, first] - progress
            out_ref[b, second] = out_ref[b, second] - progress
            return carry

        lax.fori_loop(0, rx_ref.shape[0], reaction_body, 0)


def vmem():
    return pl.BlockSpec(memory_space=pltpu.VMEM)


def smem():
    return pl.BlockSpec(memory_space=pltpu.SMEM)


def tendency_cost(states, fields, span, columns, reactions):
    flops = states * fields * (2 * span * span * columns + 2 * span * columns * columns) * 6
    flops += states * span * columns * (8 * reactions + 4 * fields)
    trans = states * span * columns * (fields + 2 * reactions)
    return flops, trans


def call(kernel, ins, in_kinds, outs, scratch, flops, trans, blocks=None):
    nbytes = sum(int(np.prod(x.shape)) * 4 for x in ins) + sum(
        int(np.prod(o.shape)) * 4 for o in outs
    )
    return pl.pallas_call(
        kernel,
        out_shape=outs,
        in_specs=[
            (blocks[i] if blocks is not None and i in blocks else smem() if k else vmem())
            for i, k in enumerate(in_kinds)
        ],
        out_specs=tuple(vmem() for _ in outs),
        scratch_shapes=scratch,
        grid=() if blocks is None else (1,),
        cost_estimate=pl.CostEstimate(
            flops=int(flops), transcendentals=int(trans), bytes_accessed=int(nbytes)
        ),
    )(*ins)


def per_device(u_start, guess, velocity, rates, energies, reactions):
    fields, depth, rows, columns = u_start.shape
    coarse_rows = rows // 2
    span = depth * rows
    coarse_span = depth * coarse_rows
    reaction_count = rates.shape[0]
    fine_table = derivative_table(FINE_NODES)
    coarse_table = derivative_table(COARSE_NODES)
    fine_elem = len(FINE_NODES)
    coarse_elem = len(COARSE_NODES)
    xt = jnp.asarray(np.kron(np.eye(columns // fine_elem), fine_table).T, jnp.float32)
    z_block = np.kron(np.eye(depth // fine_elem), fine_table)

    def plane_operator(y_table, plane_rows):
        y_block = np.kron(np.eye(plane_rows // y_table.shape[0]), y_table)
        return jnp.asarray(
            np.concatenate([np.kron(np.eye(depth), y_block), np.kron(z_block, np.eye(plane_rows))]),
            jnp.float32,
        )

    lop_fine = plane_operator(fine_table, rows)
    lop_coarse = plane_operator(coarse_table, coarse_rows)

    def coefficients(y_lift):
        up = jnp.maximum(velocity, 0.0)
        down = jnp.maximum(-velocity, 0.0)
        return jnp.concatenate([
            -velocity,
            28.0 * up[0:1], 28.0 * down[0:1],
            y_lift * up[1:2], y_lift * down[1:2],
            28.0 * up[2:3], 28.0 * down[2:3],
        ])

    cf_fine = coefficients(28.0)
    cf_coarse = coefficients(6.0)
    restrict_rows = np.kron(np.eye(rows // 8), lagrange_table(FINE_NODES, COARSE_NODES))
    prolong_rows = np.kron(np.eye(rows // 8), lagrange_table(COARSE_NODES, FINE_NODES))
    rmat = jnp.asarray(np.kron(np.eye(depth), restrict_rows), jnp.float32)
    pmat = jnp.asarray(np.kron(np.eye(depth), prolong_rows), jnp.float32)
    restrict_plane = jnp.asarray(restrict_rows, jnp.float32)
    scalars = (velocity, reactions, rates, energies)
    coarse_scalars = scalars
    scalar_kinds = (True, True, True, True)

    space_n = lax.axis_size("space")
    sections = lax.axis_size("tm")
    section = lax.axis_index("tm")
    lead = (section == 0).astype(jnp.int32).reshape(1)

    def halo(x, plane_rows):
        head = x[..., :plane_rows, :]
        tail = x[..., x.shape[-2] - plane_rows:, :]
        return swap(head, tail)

    def swap(head, tail):
        prev = lax.ppermute(tail, "space", [(i, (i + 1) % space_n) for i in range(space_n)])
        nxt = lax.ppermute(head, "space", [((i + 1) % space_n, i) for i in range(space_n)])
        return prev, nxt

    f32 = jnp.float32
    fine_state = jax.ShapeDtypeStruct((1, fields, span, columns), f32)
    coarse_state = jax.ShapeDtypeStruct((fields, coarse_span, columns), f32)

    def nodes_kernel(u_ref, p_ref, n_ref, l_ref, x_ref, zc_ref, rx_ref, ra_ref, en_ref,
                     f_ref, a1_ref, h_ref, t_ref, s_ref):
        tendency_into(f_ref, u_ref, p_ref, n_ref, l_ref, x_ref, zc_ref, rx_ref, ra_ref, en_ref,
                      s_ref, fine_elem)

        def body(f, carry):
            value = u_ref[0, f] + STEP * (
                5.0 * f_ref[0, f] + 8.0 * f_ref[1, f] - f_ref[2, f]
            ) / 24.0
            a1_ref[0, f] = value
            h_ref[0, f] = value[:rows]
            t_ref[0, f] = value[span - rows:]
            return carry

        lax.fori_loop(0, fields, body, 0)

    def middle_kernel(a1_ref, p_ref, n_ref, l_ref, x_ref, zc_ref, rx_ref, ra_ref, en_ref,
                      f_ref, g1_ref, a2_ref, h_ref, t_ref, s_ref):
        tendency_into(g1_ref, a1_ref, p_ref, n_ref, l_ref, x_ref, zc_ref, rx_ref, ra_ref,
                      en_ref, s_ref, fine_elem)

        def body(f, carry):
            value = (
                a1_ref[0, f]
                + 0.5 * STEP * (g1_ref[0, f] - f_ref[1, f])
                + STEP * (-f_ref[0, f] + 8.0 * f_ref[1, f] + 5.0 * f_ref[2, f]) / 24.0
            )
            a2_ref[0, f] = value
            h_ref[0, f] = value[:rows]
            t_ref[0, f] = value[span - rows:]
            return carry

        lax.fori_loop(0, fields, body, 0)

    def ending_kernel(a2_ref, p_ref, n_ref, l_ref, x_ref, zc_ref, rx_ref, ra_ref, en_ref,
                      f_ref, g1_ref, r_ref, base_ref, rint_ref, c1_ref, g2_ref, s_ref):
        tendency_into(g2_ref, a2_ref, p_ref, n_ref, l_ref, x_ref, zc_ref, rx_ref, ra_ref,
                      en_ref, s_ref, fine_elem)

        def body(f, carry):
            g2_ref[0, f] = STEP * (f_ref[0, f] + 4.0 * g1_ref[0, f] + g2_ref[0, f]) / 6.0
            return carry

        lax.fori_loop(0, fields, body, 0)
        rm = r_ref[...]
        for dst, src_ref, lead_index in ((rint_ref, g2_ref, 0), (c1_ref, a2_ref, 0)):
            wide = dot(rm, lanes([src_ref[lead_index, f] for f in range(fields)]))
            for f, part in enumerate(unlanes(wide, columns)):
                dst[f] = part
        for f in range(fields):
            rint_ref[f] = rint_ref[f] - STEP * base_ref[0, f]

    def base_kernel(u_ref, p_ref, n_ref, r_ref, rp_ref, l_ref, x_ref, zc_ref, rx_ref, ra_ref,
                    en_ref, out_ref, c0_ref, bp_ref, bn_ref, s_ref):
        for dst, src_ref, table in ((c0_ref, u_ref, r_ref), (bp_ref, p_ref, rp_ref),
                                    (bn_ref, n_ref, rp_ref)):
            wide = dot(table[...], lanes([src_ref[0, f] for f in range(fields)]))
            for f, part in enumerate(unlanes(wide, columns)):
                dst[0, f] = part
        tendency_into(out_ref, c0_ref, bp_ref, bn_ref, l_ref, x_ref, zc_ref, rx_ref, ra_ref,
                      en_ref, s_ref, coarse_elem)

    def chain_kernel(w_ref, p_ref, n_ref, l_ref, x_ref, zc_ref, rx_ref, ra_ref, en_ref,
                     rint_ref, out_ref, h_ref, t_ref, g_ref, s_ref):
        tendency_into(g_ref, w_ref, p_ref, n_ref, l_ref, x_ref, zc_ref, rx_ref, ra_ref,
                      en_ref, s_ref, coarse_elem)

        def body(f, carry):
            value = w_ref[0, f] + STEP * g_ref[0, f] + rint_ref[0, 0, f]
            out_ref[0, f] = value
            h_ref[0, f] = value[:coarse_rows]
            t_ref[0, f] = value[coarse_span - coarse_rows:]
            return carry

        lax.fori_loop(0, fields, body, 0)

    def plain_kernel(w_ref, p_ref, n_ref, l_ref, x_ref, zc_ref, rx_ref, ra_ref, en_ref,
                     out_ref, s_ref):
        tendency_into(out_ref, w_ref, p_ref, n_ref, l_ref, x_ref, zc_ref, rx_ref, ra_ref,
                      en_ref, s_ref, coarse_elem)

    def first_kernel(w_ref, g_ref, rint_ref, out_ref, h_ref, t_ref):
        for f in range(fields):
            value = w_ref[0, f] + STEP * g_ref[0, f] + rint_ref[0, 0, f]
            out_ref[0, f] = value
            h_ref[0, f] = value[:coarse_rows]
            t_ref[0, f] = value[coarse_span - coarse_rows:]

    def pick(sec_ref, w_refs, f, offset):
        value = w_refs[offset][0, f]
        for n in range(1, sections):
            value = jnp.where(sec_ref[0] == n, w_refs[n + offset][0, f], value)
        return value

    def correct_kernel(*refs):
        a1_ref, a2_ref, c0_ref, c1_ref = refs[:4]
        w_refs = refs[4:5 + sections]
        prev_ref, us_ref, r_ref, pm_ref, lead_ref, sec_ref, out_ref, h_ref, t_ref = refs[
            5 + sections:]
        pm = pm_ref[...]
        w0 = [pick(sec_ref, w_refs, f, 0) for f in range(fields)]
        first_change = [w0[f] - c0_ref[0, f] for f in range(fields)]
        last_change = [pick(sec_ref, w_refs, f, 1) - c1_ref[f] for f in range(fields)]
        middle_fix = unlanes(
            dot(pm, lanes([0.5 * (first_change[f] + last_change[f]) for f in range(fields)])),
            columns,
        )
        last_fix = unlanes(dot(pm, lanes(last_change)), columns)
        handed = lanes([prev_ref[0, f] for f in range(fields)])
        handed_fix = unlanes(
            dot(pm, lanes(w0) - dot(r_ref[...], handed)),
            columns,
        )
        for f in range(fields):
            values = (
                jnp.where(lead_ref[0] != 0, us_ref[f], prev_ref[0, f] + handed_fix[f]),
                a1_ref[0, f] + middle_fix[f],
                a2_ref[0, f] + last_fix[f],
            )
            for b, value in enumerate(values):
                out_ref[b, f] = value
                h_ref[b, f] = value[:rows]
                t_ref[b, f] = value[span - rows:]

    def finish_kernel(*refs):
        a2_ref, c1_ref = refs[:2]
        w_refs = refs[2:3 + sections]
        pm_ref, sec_ref, out_ref, coarse_ref = refs[3 + sections:]
        w1 = [pick(sec_ref, w_refs, f, 1) for f in range(fields)]
        fix = unlanes(
            dot(pm_ref[...], lanes([w1[f] - c1_ref[f] for f in range(fields)])), columns
        )
        for f in range(fields):
            out_ref[0, f] = a2_ref[0, f] + fix[f]
            coarse_ref[0, f] = w1[f]

    fine_cost = tendency_cost(1, fields, span, columns, reaction_count)
    coarse_cost = tendency_cost(1, fields, coarse_span, columns, reaction_count)

    def fine_scratch(states):
        return pltpu.VMEM((states, fields, span, columns), f32)

    def coarse_scratch(states):
        return pltpu.VMEM((states, fields, coarse_span, columns), f32)

    u_flat = u_start.reshape(fields, span, columns)
    nodes = guess[0].reshape(3, fields, span, columns)
    nodes = jnp.concatenate([jnp.where(section == 0, u_flat, nodes[0])[None], nodes[1:]], axis=0)
    coarse_start = jnp.einsum("cy,fzyx->fzcx", restrict_plane,
                              u_start, precision=HIGHEST).reshape(fields, coarse_span, columns)
    start_halo = halo(coarse_start, coarse_rows)

    coarse_one = jax.ShapeDtypeStruct((1, fields, coarse_span, columns), f32)
    plane_one = jax.ShapeDtypeStruct((1, fields, coarse_rows, columns), f32)
    fine_plane = jax.ShapeDtypeStruct((1, fields, rows, columns), f32)
    node_planes = jax.ShapeDtypeStruct((3, fields, rows, columns), f32)

    def coarse_step(w, w_halo, rint_all, n):
        def section_block():
            return pl.BlockSpec((1, 1, fields, coarse_span, columns), lambda i: (n, 0, 0, 0, 0),
                                memory_space=pltpu.VMEM)

        return call(
            chain_kernel,
            (w, w_halo[0], w_halo[1], lop_coarse, xt) + coarse_scalars + (rint_all,),
            (False,) * 5 + scalar_kinds + (False,),
            (coarse_one, plane_one, plane_one),
            [pltpu.VMEM((1, fields, coarse_span, columns), f32), coarse_scratch(1)],
            *coarse_cost,
            blocks={9: section_block()},
        )

    hop_pairs = [(d, d + 1) for d in range(sections - 1)]
    (start_tendency,) = call(
        plain_kernel,
        (coarse_start[None], start_halo[0][None], start_halo[1][None], lop_coarse, xt)
        + coarse_scalars,
        (False,) * 5 + scalar_kinds,
        (coarse_one,),
        [coarse_scratch(1)],
        *coarse_cost,
    )
    where_now = section.astype(jnp.int32).reshape(1)

    fine_end = None
    coarse_end = None
    for iteration in range(ITERS):
        if iteration == 0:
            node_prev, node_next = halo(nodes, rows)
        else:
            node_prev, node_next = swap(node_head, node_tail)
        f_all, a1, a1_head, a1_tail = call(
            nodes_kernel,
            (nodes, node_prev, node_next, lop_fine, xt) + scalars,
            (False,) * 5 + scalar_kinds,
            (jax.ShapeDtypeStruct((3, fields, span, columns), f32), fine_state, fine_plane,
             fine_plane),
            [fine_scratch(3)],
            fine_cost[0] * 3, fine_cost[1] * 3,
        )
        a1_prev, a1_next = swap(a1_head, a1_tail)
        g1, a2, a2_head, a2_tail = call(
            middle_kernel,
            (a1, a1_prev, a1_next, lop_fine, xt) + scalars + (f_all,),
            (False,) * 5 + scalar_kinds + (False,),
            (fine_state, fine_state, fine_plane, fine_plane),
            [fine_scratch(1)],
            *fine_cost,
        )
        a2_prev, a2_next = swap(a2_head, a2_tail)
        base, c0 = call(
            base_kernel,
            (nodes, node_prev, node_next, rmat, restrict_plane, lop_coarse, xt) + coarse_scalars,
            (False,) * 7 + scalar_kinds,
            (coarse_one, coarse_one),
            [pltpu.VMEM((1, fields, coarse_rows, columns), f32),
             pltpu.VMEM((1, fields, coarse_rows, columns), f32), coarse_scratch(1)],
            *coarse_cost,
        )
        rint, c1 = call(
            ending_kernel,
            (a2, a2_prev, a2_next, lop_fine, xt) + scalars + (f_all, g1, rmat, base),
            (False,) * 5 + scalar_kinds + (False,) * 4,
            (coarse_state, coarse_state),
            [pltpu.VMEM((1, fields, span, columns), f32), fine_scratch(1)],
            *fine_cost,
        )
        rint_all = lax.all_gather(rint[None], "tm")
        last = iteration + 1 == ITERS
        if not last:
            a2_handed = lax.ppermute(a2, "tm", hop_pairs)
        w = coarse_start[None]
        w_halo = (start_halo[0][None], start_halo[1][None])
        chain = [w]
        for n in range(sections):
            if n == 0:
                w, head, tail = call(
                    first_kernel,
                    (w, start_tendency, rint_all),
                    (False,) * 3,
                    (coarse_one, plane_one, plane_one),
                    [],
                    4 * fields * coarse_span * columns, 0,
                    blocks={2: pl.BlockSpec((1, 1, fields, coarse_span, columns),
                                            lambda i: (0, 0, 0, 0, 0),
                                            memory_space=pltpu.VMEM)},
                )
            else:
                w, head, tail = coarse_step(w, w_halo, rint_all, n)
            chain.append(w)
            if n + 1 < sections:
                w_halo = swap(head, tail)
        if last:
            fine_end, coarse_end = call(
                finish_kernel,
                (a2, c1) + tuple(chain) + (pmat, where_now),
                (False,) * (3 + sections) + (False, True),
                (fine_state, coarse_one),
                [],
                2 * fields * span * coarse_span * columns * 6, 0,
            )
        else:
            nodes, node_head, node_tail = call(
                correct_kernel,
                (a1, a2, c0, c1) + tuple(chain) + (a2_handed, u_flat, rmat, pmat, lead, where_now),
                (False,) * (5 + sections) + (False,) * 4 + (True, True),
                (jax.ShapeDtypeStruct((3, fields, span, columns), f32), node_planes,
                 node_planes),
                [],
                8 * fields * span * coarse_span * columns * 6, 0,
            )
    fine_end = fine_end.reshape(1, fields, depth, rows, columns)
    coarse_end = coarse_end.reshape(1, fields, depth, coarse_rows, columns)
    return (fine_end, coarse_end)


def solution(mesh):
    return jax.shard_map(
        per_device,
        mesh=mesh,
        in_specs=(
            P(None, "space", None, None),
            P("tm", None, None, "space", None, None),
            P(),
            P(),
            P(),
            P(),
        ),
        out_specs=(P("tm", None, "space", None, None), P("tm", None, "space", None, None)),
        check_vma=False,
    )
```

```python
import jax
import jax.numpy as jnp
import numpy as np
from jax import lax
from jax.experimental import pallas as pl
from jax.experimental.pallas import tpu as pltpu
from jax.sharding import PartitionSpec as P

ITERS = 2


STEP = 0.01
HIGHEST = lax.Precision.HIGHEST
FINE_NODES = np.array(
    [
        -1.0,
        -0.8717401485096066,
        -0.5917001814331423,
        -0.2092992179024789,
        0.2092992179024789,
        0.5917001814331423,
        0.8717401485096066,
        1.0,
    ]
)
COARSE_NODES = np.array([-1.0, -0.4472135954999579, 0.4472135954999579, 1.0])


def lagrange_table(source, target):
    table = np.ones((len(target), len(source)))
    for j in range(len(source)):
        for m in range(len(source)):
            if m != j:
                table[:, j] *= (target - source[m]) / (source[j] - source[m])
    return table


def derivative_table(points):
    total = len(points)
    weights = np.array(
        [
            1.0 / np.prod([points[j] - points[m] for m in range(total) if m != j])
            for j in range(total)
        ]
    )
    table = np.zeros((total, total))
    for i in range(total):
        for j in range(total):
            if i != j:
                table[i, j] = weights[j] / weights[i] / (points[i] - points[j])
        table[i, i] = -np.sum(table[i])
    return table


def element_tables(length, table, lift):
    per_element = table.shape[0]
    block = np.kron(np.eye(length // per_element), table)
    position = np.arange(length) % per_element
    identity = np.eye(length)
    before = np.roll(identity, -1, axis=1)
    after = np.roll(identity, 1, axis=1)
    first_mask = np.where(position == 0, 1.0, 0.0)
    last_mask = np.where(position == per_element - 1, 1.0, 0.0)
    upwind = lift * first_mask[:, None] * (before - identity)
    downwind = lift * last_mask[:, None] * (after - identity)
    return (block, upwind, downwind)


def widen(matrix):
    length = matrix.shape[0]
    wider = np.zeros((length, matrix.shape[1] + 2))
    wider[:, 1:-1] = matrix
    return wider


def padded_tables(length, table, lift):
    block, upwind, downwind = element_tables(length, table, lift)
    block_wide = widen(block)
    upwind_wide = widen(upwind)
    downwind_wide = widen(downwind)
    upwind_wide[0, length] = 0.0
    upwind_wide[0, 0] = lift
    downwind_wide[length - 1, 1] = 0.0
    downwind_wide[length - 1, length + 1] = lift
    return (block_wide, upwind_wide, downwind_wide)


def field_operators(speed, tables):
    block = jnp.asarray(tables[0], jnp.float32)
    upwind = jnp.asarray(tables[1], jnp.float32)
    downwind = jnp.asarray(tables[2], jnp.float32)
    speeds = speed[:, None, None]
    return (
        -speeds * block + jnp.maximum(speeds, 0.0) * upwind + jnp.maximum(-speeds, 0.0) * downwind
    )


def speed_combination(speed, tables):
    block = jnp.asarray(tables[0], jnp.float32)[None]
    upwind = jnp.asarray(tables[1], jnp.float32)[None]
    downwind = jnp.asarray(tables[2], jnp.float32)[None]
    speeds = speed[:, None, None]
    return (
        -speeds * block + jnp.maximum(speeds, 0.0) * upwind + jnp.maximum(-speeds, 0.0) * downwind
    )


def dot(a, b):
    return jnp.dot(a, b, precision=HIGHEST, preferred_element_type=jnp.float32)


def tdot(a, b):
    return jnp.dot(a, b, precision=lax.Precision.HIGH, preferred_element_type=jnp.float32)


def lanes(parts):
    return jnp.concatenate(parts, axis=1)


def unlanes(wide, width):
    return [wide[:, i * width:(i + 1) * width] for i in range(wide.shape[1] // width)]


def tendency_into(out_ref, v_ref, prev_ref, next_ref, k_ref, d_ref, cf_ref, rx_ref,
                  rate_ref, en_ref, s_ref, y_elem):
    states, fields, span, columns = v_ref.shape
    rows = prev_ref.shape[2]
    planes = span // rows
    f32 = jnp.float32
    row = lax.broadcasted_iota(jnp.int32, (span, columns), 0)
    lane = lax.broadcasted_iota(jnp.int32, (span, columns), 1)
    yy = row % rows
    zz = row // rows
    x_first = lane % 8 == 0
    x_last = lane % 8 == 7
    y_first = yy % y_elem == 0
    y_last = yy % y_elem == y_elem - 1
    z_first = zz % 8 == 0
    z_last = zz % 8 == 7

    def scoped(xd_ref, yz_ref):
        for b in range(states):
            xd_ref[b] = tdot(v_ref[b].reshape(fields * span, columns), d_ref[...]).reshape(
                fields, span, columns)
            yz_ref[b] = tdot(k_ref[...], lanes([v_ref[b, f] for f in range(fields)]))
        for b in range(states):
            for f in range(fields):
                v = v_ref[b, f]
                cols = slice(f * columns, (f + 1) * columns)
                t = (cf_ref[0, f] * xd_ref[b, f] + cf_ref[1, f] * yz_ref[b, :span, cols]
                     + cf_ref[2, f] * yz_ref[b, span:, cols])
                before_x = pltpu.roll(v, 1, 1)
                after_x = pltpu.roll(v, columns - 1, 1)
                t = t + jnp.where(x_first, cf_ref[3, f] * (before_x - v), 0.0)
                t = t + jnp.where(x_last, cf_ref[4, f] * (after_x - v), 0.0)
                before_y = jnp.where(yy == 0, pltpu.roll(v, span - rows + 1, 0),
                                     pltpu.roll(v, 1, 0))
                after_y = jnp.where(yy == rows - 1, pltpu.roll(v, rows - 1, 0),
                                    pltpu.roll(v, span - 1, 0))
                t = t + jnp.where(y_first, cf_ref[5, f] * (before_y - v), 0.0)
                t = t + jnp.where(y_last, cf_ref[6, f] * (after_y - v), 0.0)
                if planes > 8:
                    before_z = pltpu.roll(v, rows, 0)
                    after_z = pltpu.roll(v, span - rows, 0)
                    t = t + jnp.where(z_first & (zz > 0), cf_ref[7, f] * before_z, 0.0)
                    t = t + jnp.where(z_last & (zz < planes - 1), cf_ref[8, f] * after_z, 0.0)
                t = t - jnp.where(z_first, cf_ref[7, f] * v, 0.0)
                t = t - jnp.where(z_last, cf_ref[8, f] * v, 0.0)
                out_ref[b, f] = t
                out_ref[b, f, pl.ds(0, rows), :] = (
                    out_ref[b, f, pl.ds(0, rows), :] + cf_ref[7, f] * prev_ref[b, f]
                )
                out_ref[b, f, pl.ds(span - rows, rows), :] = (
                    out_ref[b, f, pl.ds(span - rows, rows), :] + cf_ref[8, f] * next_ref[b, f]
                )
                s_ref[b, f] = jnp.tanh(v)

    pl.run_scoped(scoped, pltpu.VMEM((states, fields, span, columns), f32),
                  pltpu.VMEM((states, 2 * span, fields * columns), f32))
    for b in range(states):
        cooling = 1.0 / (1.5 + 0.5 * s_ref[b, fields - 1])

        def reaction_body(r, carry):
            first = rx_ref[r, 0]
            second = rx_ref[r, 1]
            product = rx_ref[r, 2]
            progress = (
                rate_ref[r] * jnp.exp(-en_ref[r] * cooling) * s_ref[b, first] * s_ref[b, second]
            )
            out_ref[b, product] = out_ref[b, product] + progress
            out_ref[b, first] = out_ref[b, first] - progress
            out_ref[b, second] = out_ref[b, second] - progress
            return carry

        lax.fori_loop(0, rx_ref.shape[0], reaction_body, 0)


def vmem():
    return pl.BlockSpec(memory_space=pltpu.VMEM)


def smem():
    return pl.BlockSpec(memory_space=pltpu.SMEM)


def tendency_cost(states, fields, span, columns, reactions):
    flops = states * fields * (2 * span * span * columns + 2 * span * columns * columns) * 6
    flops += states * span * columns * (8 * reactions + 4 * fields)
    trans = states * span * columns * (fields + 2 * reactions)
    return flops, trans


def call(kernel, ins, in_kinds, outs, scratch, flops, trans, blocks=None):
    nbytes = sum(int(np.prod(x.shape)) * 4 for x in ins) + sum(
        int(np.prod(o.shape)) * 4 for o in outs
    )
    return pl.pallas_call(
        kernel,
        out_shape=outs,
        in_specs=[
            (blocks[i] if blocks is not None and i in blocks else smem() if k else vmem())
            for i, k in enumerate(in_kinds)
        ],
        out_specs=tuple(vmem() for _ in outs),
        scratch_shapes=scratch,
        grid=() if blocks is None else (1,),
        cost_estimate=pl.CostEstimate(
            flops=int(flops), transcendentals=int(trans), bytes_accessed=int(nbytes)
        ),
    )(*ins)


def per_device(u_start, guess, velocity, rates, energies, reactions):
    fields, depth, rows, columns = u_start.shape
    coarse_rows = rows // 2
    span = depth * rows
    coarse_span = depth * coarse_rows
    reaction_count = rates.shape[0]
    fine_table = derivative_table(FINE_NODES)
    coarse_table = derivative_table(COARSE_NODES)
    fine_elem = len(FINE_NODES)
    coarse_elem = len(COARSE_NODES)
    xt = jnp.asarray(np.kron(np.eye(columns // fine_elem), fine_table).T, jnp.float32)
    z_block = np.kron(np.eye(depth // fine_elem), fine_table)

    def plane_operator(y_table, plane_rows):
        y_block = np.kron(np.eye(plane_rows // y_table.shape[0]), y_table)
        return jnp.asarray(
            np.concatenate([np.kron(np.eye(depth), y_block), np.kron(z_block, np.eye(plane_rows))]),
            jnp.float32,
        )

    lop_fine = plane_operator(fine_table, rows)
    lop_coarse = plane_operator(coarse_table, coarse_rows)

    def coefficients(y_lift):
        up = jnp.maximum(velocity, 0.0)
        down = jnp.maximum(-velocity, 0.0)
        return jnp.concatenate([
            -velocity,
            28.0 * up[0:1], 28.0 * down[0:1],
            y_lift * up[1:2], y_lift * down[1:2],
            28.0 * up[2:3], 28.0 * down[2:3],
        ])

    cf_fine = coefficients(28.0)
    cf_coarse = coefficients(6.0)
    restrict_rows = np.kron(np.eye(rows // 8), lagrange_table(FINE_NODES, COARSE_NODES))
    prolong_rows = np.kron(np.eye(rows // 8), lagrange_table(COARSE_NODES, FINE_NODES))
    rmat = jnp.asarray(np.kron(np.eye(depth), restrict_rows), jnp.float32)
    pmat = jnp.asarray(np.kron(np.eye(depth), prolong_rows), jnp.float32)
    restrict_plane = jnp.asarray(restrict_rows, jnp.float32)
    scalars = (cf_fine, reactions.astype(jnp.int32), rates, energies)
    coarse_scalars = (cf_coarse, reactions.astype(jnp.int32), rates, energies)
    scalar_kinds = (True, True, True, True)

    space_n = lax.axis_size("space")
    sections = lax.axis_size("tm")
    section = lax.axis_index("tm")
    lead = (section == 0).astype(jnp.int32).reshape(1)

    def halo(x, plane_rows):
        head = x[..., :plane_rows, :]
        tail = x[..., x.shape[-2] - plane_rows:, :]
        return swap(head, tail)

    def swap(head, tail):
        prev = lax.ppermute(tail, "space", [(i, (i + 1) % space_n) for i in range(space_n)])
        nxt = lax.ppermute(head, "space", [((i + 1) % space_n, i) for i in range(space_n)])
        return prev, nxt

    f32 = jnp.float32
    fine_state = jax.ShapeDtypeStruct((1, fields, span, columns), f32)
    coarse_state = jax.ShapeDtypeStruct((fields, coarse_span, columns), f32)

    def nodes_kernel(u_ref, p_ref, n_ref, l_ref, x_ref, zc_ref, rx_ref, ra_ref, en_ref,
                     f_ref, a1_ref, h_ref, t_ref, s_ref):
        tendency_into(f_ref, u_ref, p_ref, n_ref, l_ref, x_ref, zc_ref, rx_ref, ra_ref, en_ref,
                      s_ref, fine_elem)

        def body(f, carry):
            value = u_ref[0, f] + STEP * (
                5.0 * f_ref[0, f] + 8.0 * f_ref[1, f] - f_ref[2, f]
            ) / 24.0
            a1_ref[0, f] = value
            h_ref[0, f] = value[:rows]
            t_ref[0, f] = value[span - rows:]
            return carry

        lax.fori_loop(0, fields, body, 0)

    def middle_kernel(a1_ref, p_ref, n_ref, l_ref, x_ref, zc_ref, rx_ref, ra_ref, en_ref,
                      f_ref, g1_ref, a2_ref, h_ref, t_ref, s_ref):
        tendency_into(g1_ref, a1_ref, p_ref, n_ref, l_ref, x_ref, zc_ref, rx_ref, ra_ref,
                      en_ref, s_ref, fine_elem)

        def body(f, carry):
            value = (
                a1_ref[0, f]
                + 0.5 * STEP * (g1_ref[0, f] - f_ref[1, f])
                + STEP * (-f_ref[0, f] + 8.0 * f_ref[1, f] + 5.0 * f_ref[2, f]) / 24.0
            )
            a2_ref[0, f] = value
            h_ref[0, f] = value[:rows]
            t_ref[0, f] = value[span - rows:]
            return carry

        lax.fori_loop(0, fields, body, 0)

    def ending_kernel(a2_ref, p_ref, n_ref, l_ref, x_ref, zc_ref, rx_ref, ra_ref, en_ref,
                      f_ref, g1_ref, r_ref, base_ref, rint_ref, c1_ref, g2_ref, s_ref):
        tendency_into(g2_ref, a2_ref, p_ref, n_ref, l_ref, x_ref, zc_ref, rx_ref, ra_ref,
                      en_ref, s_ref, fine_elem)

        def body(f, carry):
            g2_ref[0, f] = STEP * (f_ref[0, f] + 4.0 * g1_ref[0, f] + g2_ref[0, f]) / 6.0
            return carry

        lax.fori_loop(0, fields, body, 0)
        rm = r_ref[...]
        for dst, src_ref, lead_index in ((rint_ref, g2_ref, 0), (c1_ref, a2_ref, 0)):
            wide = dot(rm, lanes([src_ref[lead_index, f] for f in range(fields)]))
            for f, part in enumerate(unlanes(wide, columns)):
                dst[f] = part
        for f in range(fields):
            rint_ref[f] = rint_ref[f] - STEP * base_ref[0, f]

    def base_kernel(u_ref, p_ref, n_ref, r_ref, rp_ref, l_ref, x_ref, zc_ref, rx_ref, ra_ref,
                    en_ref, out_ref, c0_ref, bp_ref, bn_ref, s_ref):
        for dst, src_ref, table in ((c0_ref, u_ref, r_ref), (bp_ref, p_ref, rp_ref),
                                    (bn_ref, n_ref, rp_ref)):
            wide = dot(table[...], lanes([src_ref[0, f] for f in range(fields)]))
            for f, part in enumerate(unlanes(wide, columns)):
                dst[0, f] = part
        tendency_into(out_ref, c0_ref, bp_ref, bn_ref, l_ref, x_ref, zc_ref, rx_ref, ra_ref,
                      en_ref, s_ref, coarse_elem)

    def chain_kernel(w_ref, p_ref, n_ref, l_ref, x_ref, zc_ref, rx_ref, ra_ref, en_ref,
                     rint_ref, out_ref, h_ref, t_ref, g_ref, s_ref):
        tendency_into(g_ref, w_ref, p_ref, n_ref, l_ref, x_ref, zc_ref, rx_ref, ra_ref,
                      en_ref, s_ref, coarse_elem)

        def body(f, carry):
            value = w_ref[0, f] + STEP * g_ref[0, f] + rint_ref[0, 0, f]
            out_ref[0, f] = value
            h_ref[0, f] = value[:coarse_rows]
            t_ref[0, f] = value[coarse_span - coarse_rows:]
            return carry

        lax.fori_loop(0, fields, body, 0)

    def plain_kernel(w_ref, p_ref, n_ref, l_ref, x_ref, zc_ref, rx_ref, ra_ref, en_ref,
                     out_ref, s_ref):
        tendency_into(out_ref, w_ref, p_ref, n_ref, l_ref, x_ref, zc_ref, rx_ref, ra_ref,
                      en_ref, s_ref, coarse_elem)

    def first_kernel(w_ref, g_ref, rint_ref, out_ref, h_ref, t_ref):
        for f in range(fields):
            value = w_ref[0, f] + STEP * g_ref[0, f] + rint_ref[0, 0, f]
            out_ref[0, f] = value
            h_ref[0, f] = value[:coarse_rows]
            t_ref[0, f] = value[coarse_span - coarse_rows:]

    def pick(sec_ref, w_refs, f, offset):
        value = w_refs[offset][0, f]
        for n in range(1, sections):
            value = jnp.where(sec_ref[0] == n, w_refs[n + offset][0, f], value)
        return value

    def correct_kernel(*refs):
        a1_ref, a2_ref, c0_ref, c1_ref = refs[:4]
        w_refs = refs[4:5 + sections]
        prev_ref, us_ref, r_ref, pm_ref, lead_ref, sec_ref, out_ref, h_ref, t_ref = refs[
            5 + sections:]
        pm = pm_ref[...]
        w0 = [pick(sec_ref, w_refs, f, 0) for f in range(fields)]
        first_change = [w0[f] - c0_ref[0, f] for f in range(fields)]
        last_change = [pick(sec_ref, w_refs, f, 1) - c1_ref[f] for f in range(fields)]
        middle_fix = unlanes(
            dot(pm, lanes([0.5 * (first_change[f] + last_change[f]) for f in range(fields)])),
            columns,
        )
        last_fix = unlanes(dot(pm, lanes(last_change)), columns)
        handed = lanes([prev_ref[0, f] for f in range(fields)])
        handed_fix = unlanes(
            dot(pm, lanes(w0) - dot(r_ref[...], handed)),
            columns,
        )
        for f in range(fields):
            values = (
                jnp.where(lead_ref[0] != 0, us_ref[f], prev_ref[0, f] + handed_fix[f]),
                a1_ref[0, f] + middle_fix[f],
                a2_ref[0, f] + last_fix[f],
            )
            for b, value in enumerate(values):
                out_ref[b, f] = value
                h_ref[b, f] = value[:rows]
                t_ref[b, f] = value[span - rows:]

    def finish_kernel(*refs):
        a2_ref, c1_ref = refs[:2]
        w_refs = refs[2:3 + sections]
        pm_ref, sec_ref, out_ref, coarse_ref = refs[3 + sections:]
        w1 = [pick(sec_ref, w_refs, f, 1) for f in range(fields)]
        fix = unlanes(
            dot(pm_ref[...], lanes([w1[f] - c1_ref[f] for f in range(fields)])), columns
        )
        for f in range(fields):
            out_ref[0, f] = a2_ref[0, f] + fix[f]
            coarse_ref[0, f] = w1[f]

    fine_cost = tendency_cost(1, fields, span, columns, reaction_count)
    coarse_cost = tendency_cost(1, fields, coarse_span, columns, reaction_count)

    def fine_scratch(states):
        return pltpu.VMEM((states, fields, span, columns), f32)

    def coarse_scratch(states):
        return pltpu.VMEM((states, fields, coarse_span, columns), f32)

    u_flat = u_start.reshape(fields, span, columns)
    nodes = guess[0].reshape(3, fields, span, columns)
    nodes = jnp.concatenate([jnp.where(section == 0, u_flat, nodes[0])[None], nodes[1:]], axis=0)
    coarse_start = jnp.einsum("cy,fzyx->fzcx", restrict_plane,
                              u_start, precision=HIGHEST).reshape(fields, coarse_span, columns)
    start_halo = halo(coarse_start, coarse_rows)

    coarse_one = jax.ShapeDtypeStruct((1, fields, coarse_span, columns), f32)
    plane_one = jax.ShapeDtypeStruct((1, fields, coarse_rows, columns), f32)
    fine_plane = jax.ShapeDtypeStruct((1, fields, rows, columns), f32)
    node_planes = jax.ShapeDtypeStruct((3, fields, rows, columns), f32)

    def coarse_step(w, w_halo, rint_all, n):
        def section_block():
            return pl.BlockSpec((1, 1, fields, coarse_span, columns), lambda i: (n, 0, 0, 0, 0),
                                memory_space=pltpu.VMEM)

        return call(
            chain_kernel,
            (w, w_halo[0], w_halo[1], lop_coarse, xt) + coarse_scalars + (rint_all,),
            (False,) * 5 + scalar_kinds + (False,),
            (coarse_one, plane_one, plane_one),
            [pltpu.VMEM((1, fields, coarse_span, columns), f32), coarse_scratch(1)],
            *coarse_cost,
            blocks={9: section_block()},
        )

    hop_pairs = [(d, d + 1) for d in range(sections - 1)]
    (start_tendency,) = call(
        plain_kernel,
        (coarse_start[None], start_halo[0][None], start_halo[1][None], lop_coarse, xt)
        + coarse_scalars,
        (False,) * 5 + scalar_kinds,
        (coarse_one,),
        [coarse_scratch(1)],
        *coarse_cost,
    )
    where_now = section.astype(jnp.int32).reshape(1)

    fine_end = None
    coarse_end = None
    for iteration in range(ITERS):
        if iteration == 0:
            first = guess[0]
            plane_sets = []
            for z in (0, depth - 1):
                plane_sets.append(jnp.concatenate(
                    [jnp.where(section == 0, u_start[:, z], first[0, :, z])[None], first[1:, :, z]]
                ))
            node_prev, node_next = swap(plane_sets[0], plane_sets[1])
        else:
            node_prev, node_next = swap(node_head, node_tail)
        f_all, a1, a1_head, a1_tail = call(
            nodes_kernel,
            (nodes, node_prev, node_next, lop_fine, xt) + scalars,
            (False,) * 5 + scalar_kinds,
            (jax.ShapeDtypeStruct((3, fields, span, columns), f32), fine_state, fine_plane,
             fine_plane),
            [fine_scratch(3)],
            fine_cost[0] * 3, fine_cost[1] * 3,
        )
        a1_prev, a1_next = swap(a1_head, a1_tail)
        g1, a2, a2_head, a2_tail = call(
            middle_kernel,
            (a1, a1_prev, a1_next, lop_fine, xt) + scalars + (f_all,),
            (False,) * 5 + scalar_kinds + (False,),
            (fine_state, fine_state, fine_plane, fine_plane),
            [fine_scratch(1)],
            *fine_cost,
        )
        a2_prev, a2_next = swap(a2_head, a2_tail)
        base, c0 = call(
            base_kernel,
            (nodes, node_prev, node_next, rmat, restrict_plane, lop_coarse, xt) + coarse_scalars,
            (False,) * 7 + scalar_kinds,
            (coarse_one, coarse_one),
            [pltpu.VMEM((1, fields, coarse_rows, columns), f32),
             pltpu.VMEM((1, fields, coarse_rows, columns), f32), coarse_scratch(1)],
            *coarse_cost,
        )
        rint, c1 = call(
            ending_kernel,
            (a2, a2_prev, a2_next, lop_fine, xt) + scalars + (f_all, g1, rmat, base),
            (False,) * 5 + scalar_kinds + (False,) * 4,
            (coarse_state, coarse_state),
            [pltpu.VMEM((1, fields, span, columns), f32), fine_scratch(1)],
            *fine_cost,
        )
        rint_all = lax.all_gather(rint[None], "tm")
        last = iteration + 1 == ITERS
        if not last:
            a2_handed = lax.ppermute(a2, "tm", hop_pairs)
        w = coarse_start[None]
        w_halo = (start_halo[0][None], start_halo[1][None])
        chain = [w]
        for n in range(sections):
            if n == 0:
                w, head, tail = call(
                    first_kernel,
                    (w, start_tendency, rint_all),
                    (False,) * 3,
                    (coarse_one, plane_one, plane_one),
                    [],
                    4 * fields * coarse_span * columns, 0,
                    blocks={2: pl.BlockSpec((1, 1, fields, coarse_span, columns),
                                            lambda i: (0, 0, 0, 0, 0),
                                            memory_space=pltpu.VMEM)},
                )
            else:
                w, head, tail = coarse_step(w, w_halo, rint_all, n)
            chain.append(w)
            if n + 1 < sections:
                w_halo = swap(head, tail)
        if last:
            fine_end, coarse_end = call(
                finish_kernel,
                (a2, c1) + tuple(chain) + (pmat, where_now),
                (False,) * (3 + sections) + (False, True),
                (fine_state, coarse_one),
                [],
                2 * fields * span * coarse_span * columns * 6, 0,
            )
        else:
            nodes, node_head, node_tail = call(
                correct_kernel,
                (a1, a2, c0, c1) + tuple(chain) + (a2_handed, u_flat, rmat, pmat, lead, where_now),
                (False,) * (5 + sections) + (False,) * 4 + (True, True),
                (jax.ShapeDtypeStruct((3, fields, span, columns), f32), node_planes,
                 node_planes),
                [],
                8 * fields * span * coarse_span * columns * 6, 0,
            )
    fine_end = fine_end.reshape(1, fields, depth, rows, columns)
    coarse_end = coarse_end.reshape(1, fields, depth, coarse_rows, columns)
    return (fine_end, coarse_end)


def solution(mesh):
    return jax.shard_map(
        per_device,
        mesh=mesh,
        in_specs=(
            P(None, "space", None, None),
            P("tm", None, None, "space", None, None),
            P(),
            P(),
            P(),
            P(),
        ),
        out_specs=(P("tm", None, "space", None, None), P("tm", None, "space", None, None)),
        check_vma=False,
    )
```

```python
import jax
import jax.numpy as jnp
import numpy as np
from jax import lax
from jax.experimental import pallas as pl
from jax.experimental.pallas import tpu as pltpu
from jax.sharding import PartitionSpec as P

ITERS = 2


STEP = 0.01
HIGHEST = lax.Precision.HIGHEST
FINE_NODES = np.array(
    [
        -1.0,
        -0.8717401485096066,
        -0.5917001814331423,
        -0.2092992179024789,
        0.2092992179024789,
        0.5917001814331423,
        0.8717401485096066,
        1.0,
    ]
)
COARSE_NODES = np.array([-1.0, -0.4472135954999579, 0.4472135954999579, 1.0])


def lagrange_table(source, target):
    table = np.ones((len(target), len(source)))
    for j in range(len(source)):
        for m in range(len(source)):
            if m != j:
                table[:, j] *= (target - source[m]) / (source[j] - source[m])
    return table


def derivative_table(points):
    total = len(points)
    weights = np.array(
        [
            1.0 / np.prod([points[j] - points[m] for m in range(total) if m != j])
            for j in range(total)
        ]
    )
    table = np.zeros((total, total))
    for i in range(total):
        for j in range(total):
            if i != j:
                table[i, j] = weights[j] / weights[i] / (points[i] - points[j])
        table[i, i] = -np.sum(table[i])
    return table


def element_tables(length, table, lift):
    per_element = table.shape[0]
    block = np.kron(np.eye(length // per_element), table)
    position = np.arange(length) % per_element
    identity = np.eye(length)
    before = np.roll(identity, -1, axis=1)
    after = np.roll(identity, 1, axis=1)
    first_mask = np.where(position == 0, 1.0, 0.0)
    last_mask = np.where(position == per_element - 1, 1.0, 0.0)
    upwind = lift * first_mask[:, None] * (before - identity)
    downwind = lift * last_mask[:, None] * (after - identity)
    return (block, upwind, downwind)


def widen(matrix):
    length = matrix.shape[0]
    wider = np.zeros((length, matrix.shape[1] + 2))
    wider[:, 1:-1] = matrix
    return wider


def padded_tables(length, table, lift):
    block, upwind, downwind = element_tables(length, table, lift)
    block_wide = widen(block)
    upwind_wide = widen(upwind)
    downwind_wide = widen(downwind)
    upwind_wide[0, length] = 0.0
    upwind_wide[0, 0] = lift
    downwind_wide[length - 1, 1] = 0.0
    downwind_wide[length - 1, length + 1] = lift
    return (block_wide, upwind_wide, downwind_wide)


def field_operators(speed, tables):
    block = jnp.asarray(tables[0], jnp.float32)
    upwind = jnp.asarray(tables[1], jnp.float32)
    downwind = jnp.asarray(tables[2], jnp.float32)
    speeds = speed[:, None, None]
    return (
        -speeds * block + jnp.maximum(speeds, 0.0) * upwind + jnp.maximum(-speeds, 0.0) * downwind
    )


def speed_combination(speed, tables):
    block = jnp.asarray(tables[0], jnp.float32)[None]
    upwind = jnp.asarray(tables[1], jnp.float32)[None]
    downwind = jnp.asarray(tables[2], jnp.float32)[None]
    speeds = speed[:, None, None]
    return (
        -speeds * block + jnp.maximum(speeds, 0.0) * upwind + jnp.maximum(-speeds, 0.0) * downwind
    )


def dot(a, b):
    return jnp.dot(a, b, precision=HIGHEST, preferred_element_type=jnp.float32)


def tdot(a, b):
    return jnp.dot(a, b, precision=lax.Precision.HIGH, preferred_element_type=jnp.float32)


def lanes(parts):
    return jnp.concatenate(parts, axis=1)


def unlanes(wide, width):
    return [wide[:, i * width:(i + 1) * width] for i in range(wide.shape[1] // width)]


def tendency_into(out_ref, v_ref, prev_ref, next_ref, k_ref, d_ref, cf_ref, rx_ref,
                  rate_ref, en_ref, s_ref, y_elem):
    states, fields, span, columns = v_ref.shape
    rows = prev_ref.shape[2]
    planes = span // rows
    f32 = jnp.float32
    row = lax.broadcasted_iota(jnp.int32, (span, columns), 0)
    lane = lax.broadcasted_iota(jnp.int32, (span, columns), 1)
    yy = row % rows
    zz = row // rows
    x_first = lane % 8 == 0
    x_last = lane % 8 == 7
    y_first = yy % y_elem == 0
    y_last = yy % y_elem == y_elem - 1
    z_first = zz % 8 == 0
    z_last = zz % 8 == 7

    def scoped(xd_ref, yz_ref):
        for b in range(states):
            xd_ref[b] = tdot(v_ref[b].reshape(fields * span, columns), d_ref[...]).reshape(
                fields, span, columns)
            yz_ref[b] = tdot(k_ref[...], lanes([v_ref[b, f] for f in range(fields)]))
        for b in range(states):
            for f in range(fields):
                v = v_ref[b, f]
                cols = slice(f * columns, (f + 1) * columns)
                t = (cf_ref[0, f] * xd_ref[b, f] + cf_ref[1, f] * yz_ref[b, :span, cols]
                     + cf_ref[2, f] * yz_ref[b, span:, cols])
                before_x = pltpu.roll(v, 1, 1)
                after_x = pltpu.roll(v, columns - 1, 1)
                t = t + jnp.where(x_first, cf_ref[3, f] * (before_x - v), 0.0)
                t = t + jnp.where(x_last, cf_ref[4, f] * (after_x - v), 0.0)
                before_y = jnp.where(yy == 0, pltpu.roll(v, span - rows + 1, 0),
                                     pltpu.roll(v, 1, 0))
                after_y = jnp.where(yy == rows - 1, pltpu.roll(v, rows - 1, 0),
                                    pltpu.roll(v, span - 1, 0))
                t = t + jnp.where(y_first, cf_ref[5, f] * (before_y - v), 0.0)
                t = t + jnp.where(y_last, cf_ref[6, f] * (after_y - v), 0.0)
                if planes > 8:
                    before_z = pltpu.roll(v, rows, 0)
                    after_z = pltpu.roll(v, span - rows, 0)
                    t = t + jnp.where(z_first & (zz > 0), cf_ref[7, f] * before_z, 0.0)
                    t = t + jnp.where(z_last & (zz < planes - 1), cf_ref[8, f] * after_z, 0.0)
                t = t - jnp.where(z_first, cf_ref[7, f] * v, 0.0)
                t = t - jnp.where(z_last, cf_ref[8, f] * v, 0.0)
                out_ref[b, f] = t
                out_ref[b, f, pl.ds(0, rows), :] = (
                    out_ref[b, f, pl.ds(0, rows), :] + cf_ref[7, f] * prev_ref[b, f]
                )
                out_ref[b, f, pl.ds(span - rows, rows), :] = (
                    out_ref[b, f, pl.ds(span - rows, rows), :] + cf_ref[8, f] * next_ref[b, f]
                )
                s_ref[b, f] = jnp.tanh(v)

    pl.run_scoped(scoped, pltpu.VMEM((states, fields, span, columns), f32),
                  pltpu.VMEM((states, 2 * span, fields * columns), f32))
    for b in range(states):
        cooling = 1.0 / (1.5 + 0.5 * s_ref[b, fields - 1])

        def reaction_body(r, carry):
            first = rx_ref[r, 0]
            second = rx_ref[r, 1]
            product = rx_ref[r, 2]
            progress = (
                rate_ref[r] * jnp.exp(-en_ref[r] * cooling) * s_ref[b, first] * s_ref[b, second]
            )
            out_ref[b, product] = out_ref[b, product] + progress
            out_ref[b, first] = out_ref[b, first] - progress
            out_ref[b, second] = out_ref[b, second] - progress
            return carry

        lax.fori_loop(0, rx_ref.shape[0], reaction_body, 0)


def vmem():
    return pl.BlockSpec(memory_space=pltpu.VMEM)


def smem():
    return pl.BlockSpec(memory_space=pltpu.SMEM)


def tendency_cost(states, fields, span, columns, reactions):
    flops = states * fields * (2 * span * span * columns + 2 * span * columns * columns) * 6
    flops += states * span * columns * (8 * reactions + 4 * fields)
    trans = states * span * columns * (fields + 2 * reactions)
    return flops, trans


def call(kernel, ins, in_kinds, outs, scratch, flops, trans, blocks=None):
    nbytes = sum(int(np.prod(x.shape)) * 4 for x in ins) + sum(
        int(np.prod(o.shape)) * 4 for o in outs
    )
    return pl.pallas_call(
        kernel,
        out_shape=outs,
        in_specs=[
            (blocks[i] if blocks is not None and i in blocks else smem() if k else vmem())
            for i, k in enumerate(in_kinds)
        ],
        out_specs=tuple(vmem() for _ in outs),
        scratch_shapes=scratch,
        grid=() if blocks is None else (1,),
        cost_estimate=pl.CostEstimate(
            flops=int(flops), transcendentals=int(trans), bytes_accessed=int(nbytes)
        ),
    )(*ins)


def per_device(u_start, guess, velocity, rates, energies, reactions):
    fields, depth, rows, columns = u_start.shape
    coarse_rows = rows // 2
    span = depth * rows
    coarse_span = depth * coarse_rows
    reaction_count = rates.shape[0]
    fine_table = derivative_table(FINE_NODES)
    coarse_table = derivative_table(COARSE_NODES)
    fine_elem = len(FINE_NODES)
    coarse_elem = len(COARSE_NODES)
    xt = jnp.asarray(np.kron(np.eye(columns // fine_elem), fine_table).T, jnp.float32)
    z_block = np.kron(np.eye(depth // fine_elem), fine_table)

    def plane_operator(y_table, plane_rows):
        y_block = np.kron(np.eye(plane_rows // y_table.shape[0]), y_table)
        return jnp.asarray(
            np.concatenate([np.kron(np.eye(depth), y_block), np.kron(z_block, np.eye(plane_rows))]),
            jnp.float32,
        )

    lop_fine = plane_operator(fine_table, rows)
    lop_coarse = plane_operator(coarse_table, coarse_rows)

    def coefficients(y_lift):
        up = jnp.maximum(velocity, 0.0)
        down = jnp.maximum(-velocity, 0.0)
        return jnp.concatenate([
            -velocity,
            28.0 * up[0:1], 28.0 * down[0:1],
            y_lift * up[1:2], y_lift * down[1:2],
            28.0 * up[2:3], 28.0 * down[2:3],
        ])

    cf_fine = coefficients(28.0)
    cf_coarse = coefficients(6.0)
    restrict_rows = np.kron(np.eye(rows // 8), lagrange_table(FINE_NODES, COARSE_NODES))
    prolong_rows = np.kron(np.eye(rows // 8), lagrange_table(COARSE_NODES, FINE_NODES))
    rmat = jnp.asarray(np.kron(np.eye(depth), restrict_rows), jnp.float32)
    pmat = jnp.asarray(np.kron(np.eye(depth), prolong_rows), jnp.float32)
    restrict_plane = jnp.asarray(restrict_rows, jnp.float32)
    scalars = (cf_fine, reactions.astype(jnp.int32), rates, energies)
    coarse_scalars = (cf_coarse, reactions.astype(jnp.int32), rates, energies)
    scalar_kinds = (True, True, True, True)

    space_n = lax.axis_size("space")
    sections = lax.axis_size("tm")
    section = lax.axis_index("tm")
    lead = (section == 0).astype(jnp.int32).reshape(1)

    def halo(x, plane_rows):
        head = x[..., :plane_rows, :]
        tail = x[..., x.shape[-2] - plane_rows:, :]
        return swap(head, tail)

    def swap(head, tail):
        nxt = lax.ppermute(head, "space", [((i + 1) % space_n, i) for i in range(space_n)])
        prev = lax.ppermute(tail, "space", [(i, (i + 1) % space_n) for i in range(space_n)])
        return prev, nxt

    f32 = jnp.float32
    fine_state = jax.ShapeDtypeStruct((1, fields, span, columns), f32)
    coarse_state = jax.ShapeDtypeStruct((fields, coarse_span, columns), f32)

    def nodes_kernel(u_ref, p_ref, n_ref, l_ref, x_ref, zc_ref, rx_ref, ra_ref, en_ref,
                     f_ref, a1_ref, h_ref, t_ref, s_ref):
        tendency_into(f_ref, u_ref, p_ref, n_ref, l_ref, x_ref, zc_ref, rx_ref, ra_ref, en_ref,
                      s_ref, fine_elem)

        def body(f, carry):
            value = u_ref[0, f] + STEP * (
                5.0 * f_ref[0, f] + 8.0 * f_ref[1, f] - f_ref[2, f]
            ) / 24.0
            a1_ref[0, f] = value
            h_ref[0, f] = value[:rows]
            t_ref[0, f] = value[span - rows:]
            return carry

        lax.fori_loop(0, fields, body, 0)

    def middle_kernel(a1_ref, p_ref, n_ref, l_ref, x_ref, zc_ref, rx_ref, ra_ref, en_ref,
                      f_ref, g1_ref, a2_ref, h_ref, t_ref, s_ref):
        tendency_into(g1_ref, a1_ref, p_ref, n_ref, l_ref, x_ref, zc_ref, rx_ref, ra_ref,
                      en_ref, s_ref, fine_elem)

        def body(f, carry):
            value = (
                a1_ref[0, f]
                + 0.5 * STEP * (g1_ref[0, f] - f_ref[1, f])
                + STEP * (-f_ref[0, f] + 8.0 * f_ref[1, f] + 5.0 * f_ref[2, f]) / 24.0
            )
            a2_ref[0, f] = value
            h_ref[0, f] = value[:rows]
            t_ref[0, f] = value[span - rows:]
            return carry

        lax.fori_loop(0, fields, body, 0)

    def ending_kernel(a2_ref, p_ref, n_ref, l_ref, x_ref, zc_ref, rx_ref, ra_ref, en_ref,
                      f_ref, g1_ref, r_ref, base_ref, rint_ref, c1_ref, g2_ref, s_ref):
        tendency_into(g2_ref, a2_ref, p_ref, n_ref, l_ref, x_ref, zc_ref, rx_ref, ra_ref,
                      en_ref, s_ref, fine_elem)

        def body(f, carry):
            g2_ref[0, f] = STEP * (f_ref[0, f] + 4.0 * g1_ref[0, f] + g2_ref[0, f]) / 6.0
            return carry

        lax.fori_loop(0, fields, body, 0)
        rm = r_ref[...]
        for dst, src_ref, lead_index in ((rint_ref, g2_ref, 0), (c1_ref, a2_ref, 0)):
            wide = dot(rm, lanes([src_ref[lead_index, f] for f in range(fields)]))
            for f, part in enumerate(unlanes(wide, columns)):
                dst[f] = part
        for f in range(fields):
            rint_ref[f] = rint_ref[f] - STEP * base_ref[0, f]

    def base_kernel(u_ref, p_ref, n_ref, r_ref, rp_ref, l_ref, x_ref, zc_ref, rx_ref, ra_ref,
                    en_ref, out_ref, c0_ref, bp_ref, bn_ref, s_ref):
        for dst, src_ref, table in ((c0_ref, u_ref, r_ref), (bp_ref, p_ref, rp_ref),
                                    (bn_ref, n_ref, rp_ref)):
            wide = dot(table[...], lanes([src_ref[0, f] for f in range(fields)]))
            for f, part in enumerate(unlanes(wide, columns)):
                dst[0, f] = part
        tendency_into(out_ref, c0_ref, bp_ref, bn_ref, l_ref, x_ref, zc_ref, rx_ref, ra_ref,
                      en_ref, s_ref, coarse_elem)

    def chain_kernel(w_ref, p_ref, n_ref, l_ref, x_ref, zc_ref, rx_ref, ra_ref, en_ref,
                     rint_ref, out_ref, h_ref, t_ref, g_ref, s_ref):
        tendency_into(g_ref, w_ref, p_ref, n_ref, l_ref, x_ref, zc_ref, rx_ref, ra_ref,
                      en_ref, s_ref, coarse_elem)

        def body(f, carry):
            value = w_ref[0, f] + STEP * g_ref[0, f] + rint_ref[0, 0, f]
            out_ref[0, f] = value
            h_ref[0, f] = value[:coarse_rows]
            t_ref[0, f] = value[coarse_span - coarse_rows:]
            return carry

        lax.fori_loop(0, fields, body, 0)

    def plain_kernel(w_ref, p_ref, n_ref, l_ref, x_ref, zc_ref, rx_ref, ra_ref, en_ref,
                     out_ref, s_ref):
        tendency_into(out_ref, w_ref, p_ref, n_ref, l_ref, x_ref, zc_ref, rx_ref, ra_ref,
                      en_ref, s_ref, coarse_elem)

    def first_kernel(w_ref, g_ref, rint_ref, out_ref, h_ref, t_ref):
        for f in range(fields):
            value = w_ref[0, f] + STEP * g_ref[0, f] + rint_ref[0, 0, f]
            out_ref[0, f] = value
            h_ref[0, f] = value[:coarse_rows]
            t_ref[0, f] = value[coarse_span - coarse_rows:]

    def pick(sec_ref, w_refs, f, offset):
        value = w_refs[offset][0, f]
        for n in range(1, sections):
            value = jnp.where(sec_ref[0] == n, w_refs[n + offset][0, f], value)
        return value

    def correct_kernel(*refs):
        a1_ref, a2_ref, c0_ref, c1_ref = refs[:4]
        w_refs = refs[4:5 + sections]
        prev_ref, us_ref, r_ref, pm_ref, lead_ref, sec_ref, out_ref, h_ref, t_ref = refs[
            5 + sections:]
        pm = pm_ref[...]
        w0 = [pick(sec_ref, w_refs, f, 0) for f in range(fields)]
        first_change = [w0[f] - c0_ref[0, f] for f in range(fields)]
        last_change = [pick(sec_ref, w_refs, f, 1) - c1_ref[f] for f in range(fields)]
        middle_fix = unlanes(
            dot(pm, lanes([0.5 * (first_change[f] + last_change[f]) for f in range(fields)])),
            columns,
        )
        last_fix = unlanes(dot(pm, lanes(last_change)), columns)
        handed = lanes([prev_ref[0, f] for f in range(fields)])
        handed_fix = unlanes(
            dot(pm, lanes(w0) - dot(r_ref[...], handed)),
            columns,
        )
        for f in range(fields):
            values = (
                jnp.where(lead_ref[0] != 0, us_ref[f], prev_ref[0, f] + handed_fix[f]),
                a1_ref[0, f] + middle_fix[f],
                a2_ref[0, f] + last_fix[f],
            )
            for b, value in enumerate(values):
                out_ref[b, f] = value
                h_ref[b, f] = value[:rows]
                t_ref[b, f] = value[span - rows:]

    def finish_kernel(*refs):
        a2_ref, c1_ref = refs[:2]
        w_refs = refs[2:3 + sections]
        pm_ref, sec_ref, out_ref, coarse_ref = refs[3 + sections:]
        w1 = [pick(sec_ref, w_refs, f, 1) for f in range(fields)]
        fix = unlanes(
            dot(pm_ref[...], lanes([w1[f] - c1_ref[f] for f in range(fields)])), columns
        )
        for f in range(fields):
            out_ref[0, f] = a2_ref[0, f] + fix[f]
            coarse_ref[0, f] = w1[f]

    fine_cost = tendency_cost(1, fields, span, columns, reaction_count)
    coarse_cost = tendency_cost(1, fields, coarse_span, columns, reaction_count)

    def fine_scratch(states):
        return pltpu.VMEM((states, fields, span, columns), f32)

    def coarse_scratch(states):
        return pltpu.VMEM((states, fields, coarse_span, columns), f32)

    u_flat = u_start.reshape(fields, span, columns)
    nodes = guess[0].reshape(3, fields, span, columns)
    nodes = jnp.concatenate([jnp.where(section == 0, u_flat, nodes[0])[None], nodes[1:]], axis=0)
    coarse_start = jnp.einsum("cy,fzyx->fzcx", restrict_plane,
                              u_start, precision=HIGHEST).reshape(fields, coarse_span, columns)
    start_halo = halo(coarse_start, coarse_rows)

    coarse_one = jax.ShapeDtypeStruct((1, fields, coarse_span, columns), f32)
    plane_one = jax.ShapeDtypeStruct((1, fields, coarse_rows, columns), f32)
    fine_plane = jax.ShapeDtypeStruct((1, fields, rows, columns), f32)
    node_planes = jax.ShapeDtypeStruct((3, fields, rows, columns), f32)

    def coarse_step(w, w_halo, rint_all, n):
        def section_block():
            return pl.BlockSpec((1, 1, fields, coarse_span, columns), lambda i: (n, 0, 0, 0, 0),
                                memory_space=pltpu.VMEM)

        return call(
            chain_kernel,
            (w, w_halo[0], w_halo[1], lop_coarse, xt) + coarse_scalars + (rint_all,),
            (False,) * 5 + scalar_kinds + (False,),
            (coarse_one, plane_one, plane_one),
            [pltpu.VMEM((1, fields, coarse_span, columns), f32), coarse_scratch(1)],
            *coarse_cost,
            blocks={9: section_block()},
        )

    hop_pairs = [(d, d + 1) for d in range(sections - 1)]
    (start_tendency,) = call(
        plain_kernel,
        (coarse_start[None], start_halo[0][None], start_halo[1][None], lop_coarse, xt)
        + coarse_scalars,
        (False,) * 5 + scalar_kinds,
        (coarse_one,),
        [coarse_scratch(1)],
        *coarse_cost,
    )
    where_now = section.astype(jnp.int32).reshape(1)

    fine_end = None
    coarse_end = None
    for iteration in range(ITERS):
        if iteration == 0:
            node_prev, node_next = halo(nodes, rows)
        else:
            node_prev, node_next = swap(node_head, node_tail)
        f_all, a1, a1_head, a1_tail = call(
            nodes_kernel,
            (nodes, node_prev, node_next, lop_fine, xt) + scalars,
            (False,) * 5 + scalar_kinds,
            (jax.ShapeDtypeStruct((3, fields, span, columns), f32), fine_state, fine_plane,
             fine_plane),
            [fine_scratch(3)],
            fine_cost[0] * 3, fine_cost[1] * 3,
        )
        a1_prev, a1_next = swap(a1_head, a1_tail)
        g1, a2, a2_head, a2_tail = call(
            middle_kernel,
            (a1, a1_prev, a1_next, lop_fine, xt) + scalars + (f_all,),
            (False,) * 5 + scalar_kinds + (False,),
            (fine_state, fine_state, fine_plane, fine_plane),
            [fine_scratch(1)],
            *fine_cost,
        )
        a2_prev, a2_next = swap(a2_head, a2_tail)
        base, c0 = call(
            base_kernel,
            (nodes, node_prev, node_next, rmat, restrict_plane, lop_coarse, xt) + coarse_scalars,
            (False,) * 7 + scalar_kinds,
            (coarse_one, coarse_one),
            [pltpu.VMEM((1, fields, coarse_rows, columns), f32),
             pltpu.VMEM((1, fields, coarse_rows, columns), f32), coarse_scratch(1)],
            *coarse_cost,
        )
        rint, c1 = call(
            ending_kernel,
            (a2, a2_prev, a2_next, lop_fine, xt) + scalars + (f_all, g1, rmat, base),
            (False,) * 5 + scalar_kinds + (False,) * 4,
            (coarse_state, coarse_state),
            [pltpu.VMEM((1, fields, span, columns), f32), fine_scratch(1)],
            *fine_cost,
        )
        rint_all = lax.all_gather(rint[None], "tm")
        last = iteration + 1 == ITERS
        if not last:
            a2_handed = lax.ppermute(a2, "tm", hop_pairs)
        w = coarse_start[None]
        w_halo = (start_halo[0][None], start_halo[1][None])
        chain = [w]
        for n in range(sections):
            if n == 0:
                w, head, tail = call(
                    first_kernel,
                    (w, start_tendency, rint_all),
                    (False,) * 3,
                    (coarse_one, plane_one, plane_one),
                    [],
                    4 * fields * coarse_span * columns, 0,
                    blocks={2: pl.BlockSpec((1, 1, fields, coarse_span, columns),
                                            lambda i: (0, 0, 0, 0, 0),
                                            memory_space=pltpu.VMEM)},
                )
            else:
                w, head, tail = coarse_step(w, w_halo, rint_all, n)
            chain.append(w)
            if n + 1 < sections:
                w_halo = swap(head, tail)
        if last:
            fine_end, coarse_end = call(
                finish_kernel,
                (a2, c1) + tuple(chain) + (pmat, where_now),
                (False,) * (3 + sections) + (False, True),
                (fine_state, coarse_one),
                [],
                2 * fields * span * coarse_span * columns * 6, 0,
            )
        else:
            nodes, node_head, node_tail = call(
                correct_kernel,
                (a1, a2, c0, c1) + tuple(chain) + (a2_handed, u_flat, rmat, pmat, lead, where_now),
                (False,) * (5 + sections) + (False,) * 4 + (True, True),
                (jax.ShapeDtypeStruct((3, fields, span, columns), f32), node_planes,
                 node_planes),
                [],
                8 * fields * span * coarse_span * columns * 6, 0,
            )
    fine_end = fine_end.reshape(1, fields, depth, rows, columns)
    coarse_end = coarse_end.reshape(1, fields, depth, coarse_rows, columns)
    return (fine_end, coarse_end)


def solution(mesh):
    return jax.shard_map(
        per_device,
        mesh=mesh,
        in_specs=(
            P(None, "space", None, None),
            P("tm", None, None, "space", None, None),
            P(),
            P(),
            P(),
            P(),
        ),
        out_specs=(P("tm", None, "space", None, None), P("tm", None, "space", None, None)),
        check_vma=False,
    )
```

```python
import jax
import jax.numpy as jnp
import numpy as np
from jax import lax
from jax.experimental import pallas as pl
from jax.experimental.pallas import tpu as pltpu
from jax.sharding import PartitionSpec as P

ITERS = 2


STEP = 0.01
HIGHEST = lax.Precision.HIGHEST
FINE_NODES = np.array(
    [
        -1.0,
        -0.8717401485096066,
        -0.5917001814331423,
        -0.2092992179024789,
        0.2092992179024789,
        0.5917001814331423,
        0.8717401485096066,
        1.0,
    ]
)
COARSE_NODES = np.array([-1.0, -0.4472135954999579, 0.4472135954999579, 1.0])


def lagrange_table(source, target):
    table = np.ones((len(target), len(source)))
    for j in range(len(source)):
        for m in range(len(source)):
            if m != j:
                table[:, j] *= (target - source[m]) / (source[j] - source[m])
    return table


def derivative_table(points):
    total = len(points)
    weights = np.array(
        [
            1.0 / np.prod([points[j] - points[m] for m in range(total) if m != j])
            for j in range(total)
        ]
    )
    table = np.zeros((total, total))
    for i in range(total):
        for j in range(total):
            if i != j:
                table[i, j] = weights[j] / weights[i] / (points[i] - points[j])
        table[i, i] = -np.sum(table[i])
    return table


def element_tables(length, table, lift):
    per_element = table.shape[0]
    block = np.kron(np.eye(length // per_element), table)
    position = np.arange(length) % per_element
    identity = np.eye(length)
    before = np.roll(identity, -1, axis=1)
    after = np.roll(identity, 1, axis=1)
    first_mask = np.where(position == 0, 1.0, 0.0)
    last_mask = np.where(position == per_element - 1, 1.0, 0.0)
    upwind = lift * first_mask[:, None] * (before - identity)
    downwind = lift * last_mask[:, None] * (after - identity)
    return (block, upwind, downwind)


def widen(matrix):
    length = matrix.shape[0]
    wider = np.zeros((length, matrix.shape[1] + 2))
    wider[:, 1:-1] = matrix
    return wider


def padded_tables(length, table, lift):
    block, upwind, downwind = element_tables(length, table, lift)
    block_wide = widen(block)
    upwind_wide = widen(upwind)
    downwind_wide = widen(downwind)
    upwind_wide[0, length] = 0.0
    upwind_wide[0, 0] = lift
    downwind_wide[length - 1, 1] = 0.0
    downwind_wide[length - 1, length + 1] = lift
    return (block_wide, upwind_wide, downwind_wide)


def field_operators(speed, tables):
    block = jnp.asarray(tables[0], jnp.float32)
    upwind = jnp.asarray(tables[1], jnp.float32)
    downwind = jnp.asarray(tables[2], jnp.float32)
    speeds = speed[:, None, None]
    return (
        -speeds * block + jnp.maximum(speeds, 0.0) * upwind + jnp.maximum(-speeds, 0.0) * downwind
    )


def speed_combination(speed, tables):
    block = jnp.asarray(tables[0], jnp.float32)[None]
    upwind = jnp.asarray(tables[1], jnp.float32)[None]
    downwind = jnp.asarray(tables[2], jnp.float32)[None]
    speeds = speed[:, None, None]
    return (
        -speeds * block + jnp.maximum(speeds, 0.0) * upwind + jnp.maximum(-speeds, 0.0) * downwind
    )


def dot(a, b):
    return jnp.dot(a, b, precision=HIGHEST, preferred_element_type=jnp.float32)


def tdot(a, b):
    return jnp.dot(a, b, precision=lax.Precision.HIGH, preferred_element_type=jnp.float32)


def lanes(parts):
    return jnp.concatenate(parts, axis=1)


def unlanes(wide, width):
    return [wide[:, i * width:(i + 1) * width] for i in range(wide.shape[1] // width)]


def tendency_into(out_ref, v_ref, prev_ref, next_ref, k_ref, d_ref, cf_ref, rx_ref,
                  rate_ref, en_ref, s_ref, y_elem):
    states, fields, span, columns = v_ref.shape
    rows = prev_ref.shape[2]
    planes = span // rows
    f32 = jnp.float32
    row = lax.broadcasted_iota(jnp.int32, (span, columns), 0)
    lane = lax.broadcasted_iota(jnp.int32, (span, columns), 1)
    yy = row % rows
    zz = row // rows
    x_first = lane % 8 == 0
    x_last = lane % 8 == 7
    y_first = yy % y_elem == 0
    y_last = yy % y_elem == y_elem - 1
    z_first = zz % 8 == 0
    z_last = zz % 8 == 7

    def scoped(xd_ref, yz_ref):
        for b in range(states):
            xd_ref[b] = tdot(v_ref[b].reshape(fields * span, columns), d_ref[...]).reshape(
                fields, span, columns)
            yz_ref[b] = tdot(k_ref[...], lanes([v_ref[b, f] for f in range(fields)]))
        for b in range(states):
            for f in range(fields):
                v = v_ref[b, f]
                cols = slice(f * columns, (f + 1) * columns)
                t = (cf_ref[0, f] * xd_ref[b, f] + cf_ref[1, f] * yz_ref[b, :span, cols]
                     + cf_ref[2, f] * yz_ref[b, span:, cols])
                before_x = pltpu.roll(v, 1, 1)
                after_x = pltpu.roll(v, columns - 1, 1)
                t = t + jnp.where(x_first, cf_ref[3, f] * (before_x - v), 0.0)
                t = t + jnp.where(x_last, cf_ref[4, f] * (after_x - v), 0.0)
                before_y = jnp.where(yy == 0, pltpu.roll(v, span - rows + 1, 0),
                                     pltpu.roll(v, 1, 0))
                after_y = jnp.where(yy == rows - 1, pltpu.roll(v, rows - 1, 0),
                                    pltpu.roll(v, span - 1, 0))
                t = t + jnp.where(y_first, cf_ref[5, f] * (before_y - v), 0.0)
                t = t + jnp.where(y_last, cf_ref[6, f] * (after_y - v), 0.0)
                if planes > 8:
                    before_z = pltpu.roll(v, rows, 0)
                    after_z = pltpu.roll(v, span - rows, 0)
                    t = t + jnp.where(z_first & (zz > 0), cf_ref[7, f] * before_z, 0.0)
                    t = t + jnp.where(z_last & (zz < planes - 1), cf_ref[8, f] * after_z, 0.0)
                t = t - jnp.where(z_first, cf_ref[7, f] * v, 0.0)
                t = t - jnp.where(z_last, cf_ref[8, f] * v, 0.0)
                out_ref[b, f] = t
                out_ref[b, f, pl.ds(0, rows), :] = (
                    out_ref[b, f, pl.ds(0, rows), :] + cf_ref[7, f] * prev_ref[b, f]
                )
                out_ref[b, f, pl.ds(span - rows, rows), :] = (
                    out_ref[b, f, pl.ds(span - rows, rows), :] + cf_ref[8, f] * next_ref[b, f]
                )
                s_ref[b, f] = jnp.tanh(v)

    pl.run_scoped(scoped, pltpu.VMEM((states, fields, span, columns), f32),
                  pltpu.VMEM((states, 2 * span, fields * columns), f32))
    for b in range(states):
        cooling = 1.0 / (1.5 + 0.5 * s_ref[b, fields - 1])

        def reaction_body(r, carry):
            first = rx_ref[r, 0]
            second = rx_ref[r, 1]
            product = rx_ref[r, 2]
            progress = (
                rate_ref[r] * jnp.exp(-en_ref[r] * cooling) * s_ref[b, first] * s_ref[b, second]
            )
            out_ref[b, product] = out_ref[b, product] + progress
            out_ref[b, first] = out_ref[b, first] - progress
            out_ref[b, second] = out_ref[b, second] - progress
            return carry

        lax.fori_loop(0, rx_ref.shape[0], reaction_body, 0, unroll=3)


def vmem():
    return pl.BlockSpec(memory_space=pltpu.VMEM)


def smem():
    return pl.BlockSpec(memory_space=pltpu.SMEM)


def tendency_cost(states, fields, span, columns, reactions):
    flops = states * fields * (2 * span * span * columns + 2 * span * columns * columns) * 6
    flops += states * span * columns * (8 * reactions + 4 * fields)
    trans = states * span * columns * (fields + 2 * reactions)
    return flops, trans


def call(kernel, ins, in_kinds, outs, scratch, flops, trans, blocks=None):
    nbytes = sum(int(np.prod(x.shape)) * 4 for x in ins) + sum(
        int(np.prod(o.shape)) * 4 for o in outs
    )
    return pl.pallas_call(
        kernel,
        out_shape=outs,
        in_specs=[
            (blocks[i] if blocks is not None and i in blocks else smem() if k else vmem())
            for i, k in enumerate(in_kinds)
        ],
        out_specs=tuple(vmem() for _ in outs),
        scratch_shapes=scratch,
        grid=() if blocks is None else (1,),
        cost_estimate=pl.CostEstimate(
            flops=int(flops), transcendentals=int(trans), bytes_accessed=int(nbytes)
        ),
    )(*ins)


def per_device(u_start, guess, velocity, rates, energies, reactions):
    fields, depth, rows, columns = u_start.shape
    coarse_rows = rows // 2
    span = depth * rows
    coarse_span = depth * coarse_rows
    reaction_count = rates.shape[0]
    fine_table = derivative_table(FINE_NODES)
    coarse_table = derivative_table(COARSE_NODES)
    fine_elem = len(FINE_NODES)
    coarse_elem = len(COARSE_NODES)
    xt = jnp.asarray(np.kron(np.eye(columns // fine_elem), fine_table).T, jnp.float32)
    z_block = np.kron(np.eye(depth // fine_elem), fine_table)

    def plane_operator(y_table, plane_rows):
        y_block = np.kron(np.eye(plane_rows // y_table.shape[0]), y_table)
        return jnp.asarray(
            np.concatenate([np.kron(np.eye(depth), y_block), np.kron(z_block, np.eye(plane_rows))]),
            jnp.float32,
        )

    lop_fine = plane_operator(fine_table, rows)
    lop_coarse = plane_operator(coarse_table, coarse_rows)

    def coefficients(y_lift):
        up = jnp.maximum(velocity, 0.0)
        down = jnp.maximum(-velocity, 0.0)
        return jnp.concatenate([
            -velocity,
            28.0 * up[0:1], 28.0 * down[0:1],
            y_lift * up[1:2], y_lift * down[1:2],
            28.0 * up[2:3], 28.0 * down[2:3],
        ])

    cf_fine = coefficients(28.0)
    cf_coarse = coefficients(6.0)
    restrict_rows = np.kron(np.eye(rows // 8), lagrange_table(FINE_NODES, COARSE_NODES))
    prolong_rows = np.kron(np.eye(rows // 8), lagrange_table(COARSE_NODES, FINE_NODES))
    rmat = jnp.asarray(np.kron(np.eye(depth), restrict_rows), jnp.float32)
    pmat = jnp.asarray(np.kron(np.eye(depth), prolong_rows), jnp.float32)
    restrict_plane = jnp.asarray(restrict_rows, jnp.float32)
    scalars = (cf_fine, reactions.astype(jnp.int32), rates, energies)
    coarse_scalars = (cf_coarse, reactions.astype(jnp.int32), rates, energies)
    scalar_kinds = (True, True, True, True)

    space_n = lax.axis_size("space")
    sections = lax.axis_size("tm")
    section = lax.axis_index("tm")
    lead = (section == 0).astype(jnp.int32).reshape(1)

    def halo(x, plane_rows):
        head = x[..., :plane_rows, :]
        tail = x[..., x.shape[-2] - plane_rows:, :]
        return swap(head, tail)

    def swap(head, tail):
        prev = lax.ppermute(tail, "space", [(i, (i + 1) % space_n) for i in range(space_n)])
        nxt = lax.ppermute(head, "space", [((i + 1) % space_n, i) for i in range(space_n)])
        return prev, nxt

    f32 = jnp.float32
    fine_state = jax.ShapeDtypeStruct((1, fields, span, columns), f32)
    coarse_state = jax.ShapeDtypeStruct((fields, coarse_span, columns), f32)

    def nodes_kernel(u_ref, p_ref, n_ref, l_ref, x_ref, zc_ref, rx_ref, ra_ref, en_ref,
                     f_ref, a1_ref, h_ref, t_ref, s_ref):
        tendency_into(f_ref, u_ref, p_ref, n_ref, l_ref, x_ref, zc_ref, rx_ref, ra_ref, en_ref,
                      s_ref, fine_elem)

        def body(f, carry):
            value = u_ref[0, f] + STEP * (
                5.0 * f_ref[0, f] + 8.0 * f_ref[1, f] - f_ref[2, f]
            ) / 24.0
            a1_ref[0, f] = value
            h_ref[0, f] = value[:rows]
            t_ref[0, f] = value[span - rows:]
            return carry

        lax.fori_loop(0, fields, body, 0)

    def middle_kernel(a1_ref, p_ref, n_ref, l_ref, x_ref, zc_ref, rx_ref, ra_ref, en_ref,
                      f_ref, g1_ref, a2_ref, h_ref, t_ref, s_ref):
        tendency_into(g1_ref, a1_ref, p_ref, n_ref, l_ref, x_ref, zc_ref, rx_ref, ra_ref,
                      en_ref, s_ref, fine_elem)

        def body(f, carry):
            value = (
                a1_ref[0, f]
                + 0.5 * STEP * (g1_ref[0, f] - f_ref[1, f])
                + STEP * (-f_ref[0, f] + 8.0 * f_ref[1, f] + 5.0 * f_ref[2, f]) / 24.0
            )
            a2_ref[0, f] = value
            h_ref[0, f] = value[:rows]
            t_ref[0, f] = value[span - rows:]
            return carry

        lax.fori_loop(0, fields, body, 0)

    def ending_kernel(a2_ref, p_ref, n_ref, l_ref, x_ref, zc_ref, rx_ref, ra_ref, en_ref,
                      f_ref, g1_ref, r_ref, base_ref, rint_ref, c1_ref, g2_ref, s_ref):
        tendency_into(g2_ref, a2_ref, p_ref, n_ref, l_ref, x_ref, zc_ref, rx_ref, ra_ref,
                      en_ref, s_ref, fine_elem)

        def body(f, carry):
            g2_ref[0, f] = STEP * (f_ref[0, f] + 4.0 * g1_ref[0, f] + g2_ref[0, f]) / 6.0
            return carry

        lax.fori_loop(0, fields, body, 0)
        rm = r_ref[...]
        for dst, src_ref, lead_index in ((rint_ref, g2_ref, 0), (c1_ref, a2_ref, 0)):
            wide = dot(rm, lanes([src_ref[lead_index, f] for f in range(fields)]))
            for f, part in enumerate(unlanes(wide, columns)):
                dst[f] = part
        for f in range(fields):
            rint_ref[f] = rint_ref[f] - STEP * base_ref[0, f]

    def base_kernel(u_ref, p_ref, n_ref, r_ref, rp_ref, l_ref, x_ref, zc_ref, rx_ref, ra_ref,
                    en_ref, out_ref, c0_ref, bp_ref, bn_ref, s_ref):
        for dst, src_ref, table in ((c0_ref, u_ref, r_ref), (bp_ref, p_ref, rp_ref),
                                    (bn_ref, n_ref, rp_ref)):
            wide = dot(table[...], lanes([src_ref[0, f] for f in range(fields)]))
            for f, part in enumerate(unlanes(wide, columns)):
                dst[0, f] = part
        tendency_into(out_ref, c0_ref, bp_ref, bn_ref, l_ref, x_ref, zc_ref, rx_ref, ra_ref,
                      en_ref, s_ref, coarse_elem)

    def chain_kernel(w_ref, p_ref, n_ref, l_ref, x_ref, zc_ref, rx_ref, ra_ref, en_ref,
                     rint_ref, out_ref, h_ref, t_ref, g_ref, s_ref):
        tendency_into(g_ref, w_ref, p_ref, n_ref, l_ref, x_ref, zc_ref, rx_ref, ra_ref,
                      en_ref, s_ref, coarse_elem)

        def body(f, carry):
            value = w_ref[0, f] + STEP * g_ref[0, f] + rint_ref[0, 0, f]
            out_ref[0, f] = value
            h_ref[0, f] = value[:coarse_rows]
            t_ref[0, f] = value[coarse_span - coarse_rows:]
            return carry

        lax.fori_loop(0, fields, body, 0)

    def plain_kernel(w_ref, p_ref, n_ref, l_ref, x_ref, zc_ref, rx_ref, ra_ref, en_ref,
                     out_ref, s_ref):
        tendency_into(out_ref, w_ref, p_ref, n_ref, l_ref, x_ref, zc_ref, rx_ref, ra_ref,
                      en_ref, s_ref, coarse_elem)

    def first_kernel(w_ref, g_ref, rint_ref, out_ref, h_ref, t_ref):
        for f in range(fields):
            value = w_ref[0, f] + STEP * g_ref[0, f] + rint_ref[0, 0, f]
            out_ref[0, f] = value
            h_ref[0, f] = value[:coarse_rows]
            t_ref[0, f] = value[coarse_span - coarse_rows:]

    def pick(sec_ref, w_refs, f, offset):
        value = w_refs[offset][0, f]
        for n in range(1, sections):
            value = jnp.where(sec_ref[0] == n, w_refs[n + offset][0, f], value)
        return value

    def correct_kernel(*refs):
        a1_ref, a2_ref, c0_ref, c1_ref = refs[:4]
        w_refs = refs[4:5 + sections]
        prev_ref, us_ref, r_ref, pm_ref, lead_ref, sec_ref, out_ref, h_ref, t_ref = refs[
            5 + sections:]
        pm = pm_ref[...]
        w0 = [pick(sec_ref, w_refs, f, 0) for f in range(fields)]
        first_change = [w0[f] - c0_ref[0, f] for f in range(fields)]
        last_change = [pick(sec_ref, w_refs, f, 1) - c1_ref[f] for f in range(fields)]
        middle_fix = unlanes(
            dot(pm, lanes([0.5 * (first_change[f] + last_change[f]) for f in range(fields)])),
            columns,
        )
        last_fix = unlanes(dot(pm, lanes(last_change)), columns)
        handed = lanes([prev_ref[0, f] for f in range(fields)])
        handed_fix = unlanes(
            dot(pm, lanes(w0) - dot(r_ref[...], handed)),
            columns,
        )
        for f in range(fields):
            values = (
                jnp.where(lead_ref[0] != 0, us_ref[f], prev_ref[0, f] + handed_fix[f]),
                a1_ref[0, f] + middle_fix[f],
                a2_ref[0, f] + last_fix[f],
            )
            for b, value in enumerate(values):
                out_ref[b, f] = value
                h_ref[b, f] = value[:rows]
                t_ref[b, f] = value[span - rows:]

    def finish_kernel(*refs):
        a2_ref, c1_ref = refs[:2]
        w_refs = refs[2:3 + sections]
        pm_ref, sec_ref, out_ref, coarse_ref = refs[3 + sections:]
        w1 = [pick(sec_ref, w_refs, f, 1) for f in range(fields)]
        fix = unlanes(
            dot(pm_ref[...], lanes([w1[f] - c1_ref[f] for f in range(fields)])), columns
        )
        for f in range(fields):
            out_ref[0, f] = a2_ref[0, f] + fix[f]
            coarse_ref[0, f] = w1[f]

    fine_cost = tendency_cost(1, fields, span, columns, reaction_count)
    coarse_cost = tendency_cost(1, fields, coarse_span, columns, reaction_count)

    def fine_scratch(states):
        return pltpu.VMEM((states, fields, span, columns), f32)

    def coarse_scratch(states):
        return pltpu.VMEM((states, fields, coarse_span, columns), f32)

    u_flat = u_start.reshape(fields, span, columns)
    nodes = guess[0].reshape(3, fields, span, columns)
    nodes = jnp.concatenate([jnp.where(section == 0, u_flat, nodes[0])[None], nodes[1:]], axis=0)
    coarse_start = jnp.einsum("cy,fzyx->fzcx", restrict_plane,
                              u_start, precision=HIGHEST).reshape(fields, coarse_span, columns)
    start_halo = halo(coarse_start, coarse_rows)

    coarse_one = jax.ShapeDtypeStruct((1, fields, coarse_span, columns), f32)
    plane_one = jax.ShapeDtypeStruct((1, fields, coarse_rows, columns), f32)
    fine_plane = jax.ShapeDtypeStruct((1, fields, rows, columns), f32)
    node_planes = jax.ShapeDtypeStruct((3, fields, rows, columns), f32)

    def coarse_step(w, w_halo, rint_all, n):
        def section_block():
            return pl.BlockSpec((1, 1, fields, coarse_span, columns), lambda i: (n, 0, 0, 0, 0),
                                memory_space=pltpu.VMEM)

        return call(
            chain_kernel,
            (w, w_halo[0], w_halo[1], lop_coarse, xt) + coarse_scalars + (rint_all,),
            (False,) * 5 + scalar_kinds + (False,),
            (coarse_one, plane_one, plane_one),
            [pltpu.VMEM((1, fields, coarse_span, columns), f32), coarse_scratch(1)],
            *coarse_cost,
            blocks={9: section_block()},
        )

    hop_pairs = [(d, d + 1) for d in range(sections - 1)]
    (start_tendency,) = call(
        plain_kernel,
        (coarse_start[None], start_halo[0][None], start_halo[1][None], lop_coarse, xt)
        + coarse_scalars,
        (False,) * 5 + scalar_kinds,
        (coarse_one,),
        [coarse_scratch(1)],
        *coarse_cost,
    )
    where_now = section.astype(jnp.int32).reshape(1)

    fine_end = None
    coarse_end = None
    for iteration in range(ITERS):
        if iteration == 0:
            node_prev, node_next = halo(nodes, rows)
        else:
            node_prev, node_next = swap(node_head, node_tail)
        f_all, a1, a1_head, a1_tail = call(
            nodes_kernel,
            (nodes, node_prev, node_next, lop_fine, xt) + scalars,
            (False,) * 5 + scalar_kinds,
            (jax.ShapeDtypeStruct((3, fields, span, columns), f32), fine_state, fine_plane,
             fine_plane),
            [fine_scratch(3)],
            fine_cost[0] * 3, fine_cost[1] * 3,
        )
        a1_prev, a1_next = swap(a1_head, a1_tail)
        g1, a2, a2_head, a2_tail = call(
            middle_kernel,
            (a1, a1_prev, a1_next, lop_fine, xt) + scalars + (f_all,),
            (False,) * 5 + scalar_kinds + (False,),
            (fine_state, fine_state, fine_plane, fine_plane),
            [fine_scratch(1)],
            *fine_cost,
        )
        a2_prev, a2_next = swap(a2_head, a2_tail)
        base, c0 = call(
            base_kernel,
            (nodes, node_prev, node_next, rmat, restrict_plane, lop_coarse, xt) + coarse_scalars,
            (False,) * 7 + scalar_kinds,
            (coarse_one, coarse_one),
            [pltpu.VMEM((1, fields, coarse_rows, columns), f32),
             pltpu.VMEM((1, fields, coarse_rows, columns), f32), coarse_scratch(1)],
            *coarse_cost,
        )
        rint, c1 = call(
            ending_kernel,
            (a2, a2_prev, a2_next, lop_fine, xt) + scalars + (f_all, g1, rmat, base),
            (False,) * 5 + scalar_kinds + (False,) * 4,
            (coarse_state, coarse_state),
            [pltpu.VMEM((1, fields, span, columns), f32), fine_scratch(1)],
            *fine_cost,
        )
        rint_all = lax.all_gather(rint[None], "tm")
        last = iteration + 1 == ITERS
        if not last:
            a2_handed = lax.ppermute(a2, "tm", hop_pairs)
        w = coarse_start[None]
        w_halo = (start_halo[0][None], start_halo[1][None])
        chain = [w]
        for n in range(sections):
            if n == 0:
                w, head, tail = call(
                    first_kernel,
                    (w, start_tendency, rint_all),
                    (False,) * 3,
                    (coarse_one, plane_one, plane_one),
                    [],
                    4 * fields * coarse_span * columns, 0,
                    blocks={2: pl.BlockSpec((1, 1, fields, coarse_span, columns),
                                            lambda i: (0, 0, 0, 0, 0),
                                            memory_space=pltpu.VMEM)},
                )
            else:
                w, head, tail = coarse_step(w, w_halo, rint_all, n)
            chain.append(w)
            if n + 1 < sections:
                w_halo = swap(head, tail)
        if last:
            fine_end, coarse_end = call(
                finish_kernel,
                (a2, c1) + tuple(chain) + (pmat, where_now),
                (False,) * (3 + sections) + (False, True),
                (fine_state, coarse_one),
                [],
                2 * fields * span * coarse_span * columns * 6, 0,
            )
        else:
            nodes, node_head, node_tail = call(
                correct_kernel,
                (a1, a2, c0, c1) + tuple(chain) + (a2_handed, u_flat, rmat, pmat, lead, where_now),
                (False,) * (5 + sections) + (False,) * 4 + (True, True),
                (jax.ShapeDtypeStruct((3, fields, span, columns), f32), node_planes,
                 node_planes),
                [],
                8 * fields * span * coarse_span * columns * 6, 0,
            )
    fine_end = fine_end.reshape(1, fields, depth, rows, columns)
    coarse_end = coarse_end.reshape(1, fields, depth, coarse_rows, columns)
    return (fine_end, coarse_end)


def solution(mesh):
    return jax.shard_map(
        per_device,
        mesh=mesh,
        in_specs=(
            P(None, "space", None, None),
            P("tm", None, None, "space", None, None),
            P(),
            P(),
            P(),
            P(),
        ),
        out_specs=(P("tm", None, "space", None, None), P("tm", None, "space", None, None)),
        check_vma=False,
    )
```
